32 devices in a mesh: dp: 8 (over z, y), tensor: 4 (over x, core).
Axes of the slice: x: 2, y: 2, z: 4, core: 2. Of those that a mesh axis runs over, the one named last changes fastest.
Arguments:
- tokens: bfloat16 [8192, 2048], P('dp'), may hold values from -6 to 6
- attn_gain: float32 [2048], replicated, may hold values from 0.25 to 1.75
- w_query: bfloat16 [2048, 2048], P(None, 'tensor'), may hold values from -0.125 to 0.125
- key_matrix: bfloat16 [2048, 1024], P(None, 'tensor'), may hold values from -0.125 to 0.125
- value_matrix: bfloat16 [2048, 1024], P(None, 'tensor'), may hold values from -0.125 to 0.125
- query_gain: float32 [128], replicated, may hold values from 0.25 to 1.75
- key_gain: float32 [128], replicated, may hold values from 0.25 to 1.75
- w_out: bfloat16 [2048, 2048], P('tensor'), may hold values from -0.5 to 0.5
- mlp_gain: float32 [2048], replicated, may hold values from 0.25 to 1.75
- w_gate: bfloat16 [2048, 6144], P(None, 'tensor'), may hold values from -0.125 to 0.125
- w_up: bfloat16 [2048, 6144], P(None, 'tensor'), may hold values from -0.125 to 0.125
- w_down: bfloat16 [6144, 2048], P('tensor'), may hold values from -0.15625 to 0.15625
- cotangent: bfloat16 [8192, 2048], P('dp'), may hold values from -6 to 6
Outputs:
- mixed: bfloat16 [8192, 2048], P('dp')
- input_grad: float32 [8192, 2048], P('dp')
- attn_gain_grad: float32 [2048], replicated
- mlp_gain_grad: float32 [2048], replicated
- query_gain_grad: float32 [128], replicated
- key_gain_grad: float32 [128], replicated
- w_query_grad: float32 [2048, 2048], P('dp', 'tensor')
- w_key_grad: float32 [2048, 1024], P('dp', 'tensor')
- w_value_grad: float32 [2048, 1024], P('dp', 'tensor')
- w_out_grad: float32 [2048, 2048], P('tensor', 'dp')
- w_gate_grad: float32 [2048, 6144], P('dp', 'tensor')
- w_up_grad: float32 [2048, 6144], P('dp', 'tensor')
- w_down_grad: float32 [6144, 2048], P('tensor', 'dp')
The draws below stay inside these ranges and needn't reach their ends.
All inputs are finite; a program needn't handle non-finite values.
Results may differ from the reference program's by a relative error of at most 0.025.
Values may be sent and summed in bfloat16 or wider, within the bound.
No kernel may reach another device: no remote copies, remote signals or barrier semaphores. Data moves between devices by JAX's collectives and lax.ppermute only.
A program may use at most 320 MiB of HBM per device.

```python
import math
import jax
import jax.numpy as jnp
from jax import lax

MODEL_WIDTH = 2048
QUERY_HEADS = 16
KEY_VALUE_HEADS = 8
HEAD_SIZE = 128
HIDDEN_UNITS = 6144
LEN = 128
SEQ_DEV = 8
TOKENS = 8192
N_DP = 8
N_TENSOR = 4


def block_scale(rng, shape, cuts, smallest, top_value):
    level = 1.0
    for axis_at, blocks in cuts:
        heights = jax.random.uniform(jax.random.fold_in(jax.random.fold_in(rng, 6), axis_at), (blocks,), jnp.float32, smallest / len(cuts), top_value / len(cuts))
        level = level * jnp.repeat(jnp.exp(heights), shape[axis_at] // blocks).reshape((-1,) + (1,) * (len(shape) - 1 - axis_at))
    return level


def bell_draw(own_key, extent, deviation, reach, shards=(), held_as=jnp.bfloat16):
    array = deviation * jax.random.normal(own_key, extent, jnp.float32)
    if shards:
        array = array * block_scale(own_key, extent, shards, -0.22, 0.18)
    return jnp.clip(array, -reach, reach).astype(held_as)


def setup_inputs(seed: int = 0) -> dict:
    seeds = jax.random.split(jax.random.key(seed), 14)
    return {
        "tokens": bell_draw(seeds[0], (TOKENS, MODEL_WIDTH), 1.0, 6.0, ((0, 8),)),
        "attn_gain": jnp.clip(1.0 + 0.15 * jax.random.normal(seeds[1], (MODEL_WIDTH,), jnp.float32), 0.25, 1.75),
        "w_query": bell_draw(seeds[2], (MODEL_WIDTH, QUERY_HEADS * HEAD_SIZE), MODEL_WIDTH ** -0.5, 0.125, ((1, 4),)),
        "key_matrix": bell_draw(seeds[3], (MODEL_WIDTH, KEY_VALUE_HEADS * HEAD_SIZE), MODEL_WIDTH ** -0.5, 0.125, ((1, 4),)),
        "value_matrix": bell_draw(seeds[4], (MODEL_WIDTH, KEY_VALUE_HEADS * HEAD_SIZE), MODEL_WIDTH ** -0.5, 0.125, ((1, 4),)),
        "query_gain": jnp.clip(1.0 + 0.15 * jax.random.normal(seeds[5], (HEAD_SIZE,), jnp.float32), 0.25, 1.75),
        "key_gain": jnp.clip(1.0 + 0.15 * jax.random.normal(seeds[6], (HEAD_SIZE,), jnp.float32), 0.25, 1.75),
        "w_out": bell_draw(seeds[7], (QUERY_HEADS * HEAD_SIZE, MODEL_WIDTH), HEAD_SIZE ** -0.5, 0.5, ((0, 4),)),
        "mlp_gain": jnp.clip(1.0 + 0.15 * jax.random.normal(seeds[8], (MODEL_WIDTH,), jnp.float32), 0.25, 1.75),
        "w_gate": bell_draw(seeds[9], (MODEL_WIDTH, HIDDEN_UNITS), MODEL_WIDTH ** -0.5, 0.125, ((1, 4),)),
        "w_up": bell_draw(seeds[10], (MODEL_WIDTH, HIDDEN_UNITS), MODEL_WIDTH ** -0.5, 0.125, ((1, 4),)),
        "w_down": bell_draw(seeds[11], (HIDDEN_UNITS, MODEL_WIDTH), (HIDDEN_UNITS // 4) ** -0.5, 0.15625, ((0, 4),)),
        "cotangent": bell_draw(seeds[12], (TOKENS, MODEL_WIDTH), 1.0, 6.0, ((0, 8),)),
    }


EPS = 1e-06
THETA = 1000000.0

def product(form, left, right):
    return jnp.einsum(form, left.astype(jnp.float32), right.astype(jnp.float32))

def matmul(left, right):
    return jnp.dot(left, right, preferred_element_type=jnp.float32)

def inner_rows(left, right):
    return lax.dot_general(left, right, (((0,), (0,)), ((), ())), preferred_element_type=jnp.float32)

def rms_scale(values, gain):
    return values * lax.rsqrt(lax.optimization_barrier(jnp.mean(values * values, -1, keepdims=True)) + EPS) * gain

def norm_back(values, gain, upstream):
    factor = lax.rsqrt(lax.optimization_barrier(jnp.mean(values * values, -1, keepdims=True)) + EPS)
    scaled = gain * upstream
    return factor * scaled - values * factor ** 3 * lax.optimization_barrier(jnp.mean(scaled * values, -1, keepdims=True))

def gain_term(values, upstream):
    factor = lax.rsqrt(lax.optimization_barrier(jnp.mean(values * values, -1, keepdims=True)) + EPS)
    return lax.optimization_barrier(jnp.sum(upstream * values * factor, 0))

def swiglu(gate, upper):
    return jax.nn.silu(gate) * upper

def rope_tables(length, width):
    position = jnp.arange(length).astype(jnp.float32)
    freqs = jnp.exp(jnp.arange(width // 2).astype(jnp.float32) * (-2.0 * math.log(THETA) / width))
    angles = position[:, None] * freqs[None, :]
    cosine = jnp.cos(angles)
    sine = jnp.sin(angles)
    return (jnp.concatenate([cosine, cosine], -1), jnp.concatenate([sine, sine], -1))

def head_prep(values, gain, cosine, sine):
    normed = values * lax.rsqrt(lax.optimization_barrier(jnp.mean(values * values, -1, keepdims=True)) + EPS) * gain
    half = normed.shape[-1] // 2
    turned = jnp.concatenate([-normed[..., half:], normed[..., :half]], -1)
    return normed * cosine[:, None, :] + turned * sine[:, None, :]

def causal_scores(queries, keys_rot, length):
    scores = product('sqgrd,skgd->sgrqk', queries, keys_rot) * (1.0 / math.sqrt(HEAD_SIZE))
    allowed = jnp.arange(length)[:, None] >= jnp.arange(length)[None, :]
    return jnp.where(allowed, scores, -1e+30)

def attend(q_raw, k_raw, v_raw, query_gain, key_gain, seqs):
    total = q_raw.shape[0]
    length = total // seqs
    heads = q_raw.shape[1] // HEAD_SIZE
    kv_heads = k_raw.shape[1] // HEAD_SIZE
    repeat = heads // kv_heads
    cosine, sine = rope_tables(length, HEAD_SIZE)
    queries = head_prep(q_raw.reshape(seqs, length, heads, HEAD_SIZE), query_gain, cosine, sine)
    queries = queries.astype(jnp.bfloat16).reshape(seqs, length, kv_heads, repeat, HEAD_SIZE)
    keys_rot = head_prep(k_raw.reshape(seqs, length, kv_heads, HEAD_SIZE), key_gain, cosine, sine).astype(jnp.bfloat16)
    values = v_raw.astype(jnp.bfloat16).reshape(seqs, length, kv_heads, HEAD_SIZE)
    scores = causal_scores(queries, keys_rot, length)
    top = lax.optimization_barrier(jnp.max(scores, -1, keepdims=True))
    logsum = top + jnp.log(lax.optimization_barrier(jnp.sum(jnp.exp(scores - top), -1, keepdims=True)))
    weights = jnp.exp(scores - logsum).astype(jnp.bfloat16)
    attended = product('sgrqk,skgd->sqgrd', weights, values).astype(jnp.bfloat16).reshape(total, heads * HEAD_SIZE)
    return (attended, logsum, queries, keys_rot, values)

def attend_back(upstream, q_raw, k_raw, query_gain, key_gain, queries, keys_rot, values, logsum, seqs):
    total = q_raw.shape[0]
    length = total // seqs
    heads = q_raw.shape[1] // HEAD_SIZE
    kv_heads = k_raw.shape[1] // HEAD_SIZE
    repeat = heads // kv_heads
    cosine, sine = rope_tables(length, HEAD_SIZE)
    grad_out = upstream.reshape(seqs, length, kv_heads, repeat, HEAD_SIZE)
    scores = causal_scores(queries, keys_rot, length)
    probs = jnp.exp(scores - logsum)
    value_grad = product('sgrqk,sqgrd->skgd', probs.astype(jnp.bfloat16), grad_out)
    prob_grad = product('sqgrd,skgd->sgrqk', grad_out, values)
    center = lax.optimization_barrier(jnp.sum(probs * prob_grad, -1, keepdims=True))
    score_grad = (probs * (prob_grad - center) * (1.0 / math.sqrt(HEAD_SIZE))).astype(jnp.bfloat16)
    query_rot_grad = product('sgrqk,skgd->sqgrd', score_grad, keys_rot).reshape(seqs, length, heads, HEAD_SIZE)
    key_rot_grad = product('sgrqk,sqgrd->skgd', score_grad, queries)
    query_in = q_raw.reshape(seqs, length, heads, HEAD_SIZE)
    key_in = k_raw.reshape(seqs, length, kv_heads, HEAD_SIZE)
    _, pull_query = jax.vjp(lambda inner, gain: head_prep(inner, gain, cosine, sine), query_in, query_gain)
    query_grad, query_gain_grad = pull_query(query_rot_grad)
    _, pull_key = jax.vjp(lambda inner, gain: head_prep(inner, gain, cosine, sine), key_in, key_gain)
    key_grad, key_gain_grad = pull_key(key_rot_grad)
    return (query_grad.astype(jnp.bfloat16).reshape(total, heads * HEAD_SIZE), key_grad.astype(jnp.bfloat16).reshape(total, kv_heads * HEAD_SIZE), value_grad.astype(jnp.bfloat16).reshape(total, kv_heads * HEAD_SIZE), query_gain_grad, key_gain_grad)

def group_terms(left, weight, groups):
    count = left.shape[0]
    inner = left.shape[1] // groups
    split_left = left.astype(jnp.float32).reshape(count, groups, inner)
    split_weight = weight.astype(jnp.float32).reshape(groups, inner, weight.shape[1])
    return jnp.einsum('tgk,gkn->gtn', split_left, split_weight)

def group_terms_back(upstream, weight, groups):
    count = upstream.shape[0]
    inner = upstream.shape[1] // groups
    split_up = upstream.astype(jnp.float32).reshape(count, groups, inner)
    split_weight = weight.astype(jnp.float32).reshape(weight.shape[0], groups, inner)
    return jnp.einsum('tgn,kgn->gtk', split_up, split_weight)

def round_sum(parts):
    return lax.optimization_barrier(jnp.sum(lax.optimization_barrier(parts.astype(jnp.bfloat16)).astype(jnp.float32), 0))

def reference(tokens, attn_gain, w_query, key_matrix, value_matrix, query_gain, key_gain, w_out, mlp_gain, w_gate, w_up, w_down, cotangent):
    block_rows = SEQ_DEV * LEN
    groups = N_TENSOR

    def block(carry, pair):
        span_in, span_cot = pair
        stream = span_in.astype(jnp.float32)
        normed_in = rms_scale(stream, attn_gain).astype(jnp.bfloat16)
        q_raw = matmul(normed_in, w_query)
        k_raw = matmul(normed_in, key_matrix)
        v_raw = matmul(normed_in, value_matrix)
        attended, logsum, queries, keys_rot, values = attend(q_raw, k_raw, v_raw, query_gain, key_gain, SEQ_DEV)
        resid = stream + round_sum(group_terms(attended, w_out, groups))
        normed_mid = rms_scale(resid, mlp_gain).astype(jnp.bfloat16)
        gate = matmul(normed_mid, w_gate)
        upper = matmul(normed_mid, w_up)
        hidden = swiglu(gate, upper).astype(jnp.bfloat16)
        mixed = (resid + round_sum(group_terms(hidden, w_down, groups))).astype(jnp.bfloat16)
        down_grad = inner_rows(hidden, span_cot)
        hidden_grad = lax.dot_general(span_cot, w_down, (((1,), (1,)), ((), ())), preferred_element_type=jnp.float32)
        _, pull = jax.vjp(swiglu, gate, upper)
        gate_grad, upper_grad = pull(hidden_grad)
        gate_grad = gate_grad.astype(jnp.bfloat16)
        upper_grad = upper_grad.astype(jnp.bfloat16)
        gate_w_grad = inner_rows(normed_mid, gate_grad)
        up_w_grad = inner_rows(normed_mid, upper_grad)
        mid_grad = round_sum(group_terms_back(gate_grad, w_gate, groups) + group_terms_back(upper_grad, w_up, groups))
        resid_grad = span_cot.astype(jnp.float32) + norm_back(resid, mlp_gain, mid_grad)
        mlp_gain_part = gain_term(resid, mid_grad)
        resid_low = resid_grad.astype(jnp.bfloat16)
        out_w_grad = inner_rows(attended, resid_low)
        attended_grad = lax.dot_general(resid_low, w_out, (((1,), (1,)), ((), ())), preferred_element_type=jnp.float32).astype(jnp.bfloat16)
        q_grad, k_grad, v_grad, qg_part, kg_part = attend_back(attended_grad, q_raw, k_raw, query_gain, key_gain, queries, keys_rot, values, logsum, SEQ_DEV)
        query_w_grad = inner_rows(normed_in, q_grad)
        key_w_grad = inner_rows(normed_in, k_grad)
        value_w_grad = inner_rows(normed_in, v_grad)
        in_parts = group_terms_back(q_grad, w_query, groups) + group_terms_back(k_grad, key_matrix, groups) + group_terms_back(v_grad, value_matrix, groups)
        in_grad = round_sum(in_parts)
        input_grad = resid_grad + norm_back(stream, attn_gain, in_grad)
        attn_gain_part = gain_term(stream, in_grad)
        terms = (attn_gain_part, mlp_gain_part, qg_part, kg_part, query_w_grad, key_w_grad, value_w_grad, out_w_grad, gate_w_grad, up_w_grad, down_grad)
        carry = tuple((total + term for total, term in zip(carry, terms)))
        return (carry, (mixed, input_grad))
    begin_index = (jnp.zeros((MODEL_WIDTH,), jnp.float32), jnp.zeros((MODEL_WIDTH,), jnp.float32), jnp.zeros((HEAD_SIZE,), jnp.float32), jnp.zeros((HEAD_SIZE,), jnp.float32), jnp.zeros((MODEL_WIDTH, QUERY_HEADS * HEAD_SIZE), jnp.float32), jnp.zeros((MODEL_WIDTH, KEY_VALUE_HEADS * HEAD_SIZE), jnp.float32), jnp.zeros((MODEL_WIDTH, KEY_VALUE_HEADS * HEAD_SIZE), jnp.float32), jnp.zeros((QUERY_HEADS * HEAD_SIZE, MODEL_WIDTH), jnp.float32), jnp.zeros((MODEL_WIDTH, HIDDEN_UNITS), jnp.float32), jnp.zeros((MODEL_WIDTH, HIDDEN_UNITS), jnp.float32), jnp.zeros((HIDDEN_UNITS, MODEL_WIDTH), jnp.float32))
    totals, (mixed, input_grad) = lax.scan(block, begin_index, (tokens.reshape(N_DP, block_rows, MODEL_WIDTH), cotangent.reshape(N_DP, block_rows, MODEL_WIDTH)))
    return (mixed.reshape(TOKENS, MODEL_WIDTH), input_grad.reshape(TOKENS, MODEL_WIDTH), totals[0], totals[1], totals[2], totals[3], totals[4], totals[5], totals[6], totals[7], totals[8], totals[9], totals[10])
```

```python
import itertools
import math

import jax
import jax.numpy as jnp
import numpy as np
from jax import lax
from jax.sharding import PartitionSpec as P

HEAD_SIZE = 128
LEN = 128


EPS = 1e-06
THETA = 1000000.0


def product(form, left, right):
    return jnp.einsum(form, left, right, preferred_element_type=jnp.float32)


def matmul(left, right):
    return jnp.dot(left, right, preferred_element_type=jnp.float32)


def inner_rows(left, right):
    return lax.dot_general(
        left, right, (((0,), (0,)), ((), ())), preferred_element_type=jnp.float32
    )


def outer_cols(left, right):
    return lax.dot_general(
        left, right, (((1,), (1,)), ((), ())), preferred_element_type=jnp.float32
    )


def rms_scale(values, gain):
    return values * lax.rsqrt(jnp.mean(values * values, -1, keepdims=True) + EPS) * gain


def norm_back(values, gain, upstream):
    factor = lax.rsqrt(jnp.mean(values * values, -1, keepdims=True) + EPS)
    scaled = gain * upstream
    return factor * scaled - values * factor**3 * jnp.mean(scaled * values, -1, keepdims=True)


def gain_term(values, upstream):
    factor = lax.rsqrt(jnp.mean(values * values, -1, keepdims=True) + EPS)
    return jnp.sum(upstream * values * factor, 0)


def swiglu(gate, upper):
    return jax.nn.silu(gate) * upper


def rope_tables(length, width):
    position = jnp.arange(length).astype(jnp.float32)
    freqs = jnp.exp(jnp.arange(width // 2).astype(jnp.float32) * (-2.0 * math.log(THETA) / width))
    angles = position[:, None] * freqs[None, :]
    cosine = jnp.cos(angles)
    sine = jnp.sin(angles)
    return (jnp.concatenate([cosine, cosine], -1), jnp.concatenate([sine, sine], -1))


def head_prep(values, gain, cosine, sine):
    normed = values * lax.rsqrt(jnp.mean(values * values, -1, keepdims=True) + EPS) * gain
    half = normed.shape[-1] // 2
    turned = jnp.concatenate([-normed[..., half:], normed[..., :half]], -1)
    return normed * cosine[:, None, :] + turned * sine[:, None, :]


def causal_scores(queries, keys_rot, length):
    scores = product("sqgrd,skgd->sgrqk", queries, keys_rot) * (1.0 / math.sqrt(HEAD_SIZE))
    allowed = jnp.arange(length)[:, None] >= jnp.arange(length)[None, :]
    return jnp.where(allowed, scores, -1e30)


def attend(q_raw, k_raw, v_raw, query_gain, key_gain, seqs):
    total = q_raw.shape[0]
    length = total // seqs
    heads = q_raw.shape[1] // HEAD_SIZE
    kv_heads = k_raw.shape[1] // HEAD_SIZE
    repeat = heads // kv_heads
    cosine, sine = rope_tables(length, HEAD_SIZE)
    queries = head_prep(q_raw.reshape(seqs, length, heads, HEAD_SIZE), query_gain, cosine, sine)
    queries = queries.astype(jnp.bfloat16).reshape(seqs, length, kv_heads, repeat, HEAD_SIZE)
    keys_rot = head_prep(
        k_raw.reshape(seqs, length, kv_heads, HEAD_SIZE), key_gain, cosine, sine
    ).astype(jnp.bfloat16)
    values = v_raw.astype(jnp.bfloat16).reshape(seqs, length, kv_heads, HEAD_SIZE)
    scores = causal_scores(queries, keys_rot, length)
    top = jnp.max(scores, -1, keepdims=True)
    logsum = top + jnp.log(jnp.sum(jnp.exp(scores - top), -1, keepdims=True))
    weights = jnp.exp(scores - logsum).astype(jnp.bfloat16)
    attended = (
        product("sgrqk,skgd->sqgrd", weights, values)
        .astype(jnp.bfloat16)
        .reshape(total, heads * HEAD_SIZE)
    )
    return (attended, logsum, queries, keys_rot, values)


def attend_back(
    upstream, q_raw, k_raw, query_gain, key_gain, queries, keys_rot, values, logsum, seqs
):
    total = q_raw.shape[0]
    length = total // seqs
    heads = q_raw.shape[1] // HEAD_SIZE
    kv_heads = k_raw.shape[1] // HEAD_SIZE
    repeat = heads // kv_heads
    cosine, sine = rope_tables(length, HEAD_SIZE)
    grad_out = upstream.reshape(seqs, length, kv_heads, repeat, HEAD_SIZE)
    scores = causal_scores(queries, keys_rot, length)
    probs = jnp.exp(scores - logsum)
    value_grad = product("sgrqk,sqgrd->skgd", probs.astype(jnp.bfloat16), grad_out)
    prob_grad = product("sqgrd,skgd->sgrqk", grad_out, values)
    center = jnp.sum(probs * prob_grad, -1, keepdims=True)
    score_grad = (probs * (prob_grad - center) * (1.0 / math.sqrt(HEAD_SIZE))).astype(jnp.bfloat16)
    query_rot_grad = product("sgrqk,skgd->sqgrd", score_grad, keys_rot).reshape(
        seqs, length, heads, HEAD_SIZE
    )
    key_rot_grad = product("sgrqk,sqgrd->skgd", score_grad, queries)
    query_in = q_raw.reshape(seqs, length, heads, HEAD_SIZE)
    key_in = k_raw.reshape(seqs, length, kv_heads, HEAD_SIZE)
    _, pull_query = jax.vjp(
        lambda inner, gain: head_prep(inner, gain, cosine, sine), query_in, query_gain
    )
    query_grad, query_gain_grad = pull_query(query_rot_grad)
    _, pull_key = jax.vjp(
        lambda inner, gain: head_prep(inner, gain, cosine, sine), key_in, key_gain
    )
    key_grad, key_gain_grad = pull_key(key_rot_grad)
    return (
        query_grad.astype(jnp.bfloat16).reshape(total, heads * HEAD_SIZE),
        key_grad.astype(jnp.bfloat16).reshape(total, kv_heads * HEAD_SIZE),
        value_grad.astype(jnp.bfloat16).reshape(total, kv_heads * HEAD_SIZE),
        query_gain_grad,
        key_gain_grad,
    )


def snake_ring(coords):
    coords = [tuple(c) for c in coords]
    dims = [d for d in range(len(coords[0])) if len({c[d] for c in coords}) > 1]
    if not dims:
        return list(range(len(coords)))
    values = [sorted({c[d] for c in coords}) for d in dims]
    where = {tuple(c[d] for d in dims): i for i, c in enumerate(coords)}
    best = None
    for perm in itertools.permutations(range(len(dims))):
        def walk(level):
            if level == len(perm):
                return [()]
            inner = walk(level + 1)
            out = []
            for i, value in enumerate(values[perm[level]]):
                seq = inner if i % 2 == 0 else inner[::-1]
                out += [((perm[level], value),) + t for t in seq]
            return out

        order = []
        for path in walk(0):
            key = dict(path)
            point = tuple(key[k] for k in range(len(dims)))
            if point in where:
                order.append(where[point])
        if len(order) != len(coords):
            continue
        cost = sum(
            sum(abs(a - b) for a, b in zip(coords[order[i]], coords[order[(i + 1) % len(order)]]))
            for i in range(len(order))
        )
        if best is None or cost < best[0]:
            best = (cost, order)
    return best[1] if best else list(range(len(coords)))


class Plan:
    def __init__(self, mesh):
        names = mesh.axis_names
        devices = np.asarray(mesh.devices)
        dp_axis, tp_axis = names.index("dp"), names.index("tensor")
        devices = np.transpose(devices, (dp_axis, tp_axis))
        self.n_dp, self.n_tp = devices.shape
        dp_coords = [tuple(devices[d, 0].coords) for d in range(self.n_dp)]
        self.ring = snake_ring(dp_coords)
        self.pos = [self.ring.index(d) for d in range(self.n_dp)]
        n = self.n_dp
        self.cw = [(self.ring[i], self.ring[(i + 1) % n]) for i in range(n)]
        self.ccw = [(b, a) for a, b in self.cw]
        group = [devices[0, t] for t in range(self.n_tp)]
        self.tp_ok = False
        if self.n_tp == 4:
            chip = [tuple(g.coords) for g in group]
            core = [g.core_on_chip for g in group]
            same = [[u for u in range(4) if u != t and chip[u] == chip[t]] for t in range(4)]
            cross = [
                [u for u in range(4) if chip[u] != chip[t] and core[u] == core[t]] for t in range(4)
            ]
            if all(len(s) == 1 for s in same) and all(len(c) == 1 for c in cross):
                self.core_pairs = [(t, same[t][0]) for t in range(4)]
                self.chip_pairs = [(t, cross[t][0]) for t in range(4)]
                self.half_of = [0 if t < same[t][0] else 1 for t in range(4)]
                self.tp_ok = True

    def tp_sum(self, part):
        if not self.tp_ok:
            return lax.psum(part.astype(jnp.float32), "tensor").astype(jnp.bfloat16)
        rows = part.shape[0]
        h = rows // 2
        t = lax.axis_index("tensor")
        half = jnp.array(self.half_of, jnp.int32)[t]
        keep = lax.dynamic_slice_in_dim(part, half * h, h, 0)
        give = lax.dynamic_slice_in_dim(part, (1 - half) * h, h, 0)
        got = lax.ppermute(give, "tensor", self.core_pairs)
        chip_sum = (keep.astype(jnp.float32) + got.astype(jnp.float32)).astype(jnp.bfloat16)
        other = lax.ppermute(chip_sum, "tensor", self.chip_pairs)
        done = (chip_sum.astype(jnp.float32) + other.astype(jnp.float32)).astype(jnp.bfloat16)
        partner = lax.ppermute(done, "tensor", self.core_pairs)
        first = jnp.where(half == 0, done, partner)
        second = jnp.where(half == 0, partner, done)
        return jnp.concatenate([first, second], 0)

    def dp_rs(self, grads):
        n = self.n_dp
        me = lax.axis_index("dp")
        pos = jnp.array(self.pos, jnp.int32)[me]
        ring = jnp.array(self.ring, jnp.int32)
        blocks = [g.reshape(n, 2, g.shape[0] // n // 2, g.shape[1]) for g in grads]
        acc_a = acc_b = None
        for s in range(n - 1):
            ia = ring[(pos - 1 - s) % n]
            ib = ring[(pos + 1 + s) % n]
            own_a = [lax.dynamic_index_in_dim(b, ia, 0, keepdims=False)[0] for b in blocks]
            own_b = [lax.dynamic_index_in_dim(b, ib, 0, keepdims=False)[1] for b in blocks]
            if acc_a is None:
                send_a, send_b = own_a, own_b
            else:
                send_a = [x + y for x, y in zip(acc_a, own_a)]
                send_b = [x + y for x, y in zip(acc_b, own_b)]
            send_a = [x.astype(jnp.bfloat16) for x in send_a]
            send_b = [x.astype(jnp.bfloat16) for x in send_b]
            acc_a = [x.astype(jnp.float32) for x in lax.ppermute(send_a, "dp", self.cw)]
            acc_b = [x.astype(jnp.float32) for x in lax.ppermute(send_b, "dp", self.ccw)]
        out = []
        for b, xa, xb in zip(blocks, acc_a, acc_b):
            mine = lax.dynamic_index_in_dim(b, me, 0, keepdims=False)
            out.append(jnp.concatenate([xa + mine[0], xb + mine[1]], 0))
        return out

    def all_sum(self, x):
        for axis, size in (("tensor", self.n_tp), ("dp", self.n_dp)):
            if size & (size - 1):
                x = lax.psum(x, axis)
                continue
            bit = 1
            while bit < size:
                x = x + lax.ppermute(x, axis, [(i, i ^ bit) for i in range(size)])
                bit *= 2
        return x


def make_on_device(plan):
    def on_device(
        tokens,
        attn_gain,
        w_query,
        key_matrix,
        value_matrix,
        query_gain,
        key_gain,
        w_out,
        mlp_gain,
        w_gate,
        w_up,
        w_down,
        cotangent,
    ):
        count = tokens.shape[0]
        seqs = count // LEN
        share = count // lax.axis_size("tensor")
        offset = lax.axis_index("tensor") * share
        stream = tokens.astype(jnp.float32)
        stream_rows = lax.dynamic_slice_in_dim(stream, offset, share, 0)
        normed_in = rms_scale(stream, attn_gain).astype(jnp.bfloat16)
        q_raw = matmul(normed_in, w_query)
        k_raw = matmul(normed_in, key_matrix)
        v_raw = matmul(normed_in, value_matrix)
        attended, logsum, queries, keys_rot, values = attend(
            q_raw, k_raw, v_raw, query_gain, key_gain, seqs
        )
        attn_part = matmul(attended, w_out).astype(jnp.bfloat16)
        resid = stream + plan.tp_sum(attn_part).astype(jnp.float32)
        resid_rows = lax.dynamic_slice_in_dim(resid, offset, share, 0)
        normed_mid = rms_scale(resid, mlp_gain).astype(jnp.bfloat16)
        gate = matmul(normed_mid, w_gate)
        upper = matmul(normed_mid, w_up)
        hidden = swiglu(gate, upper).astype(jnp.bfloat16)
        mlp_part = matmul(hidden, w_down).astype(jnp.bfloat16)
        mixed = (resid + plan.tp_sum(mlp_part).astype(jnp.float32)).astype(jnp.bfloat16)
        down_grad_t = inner_rows(cotangent, hidden)
        hidden_grad = outer_cols(cotangent, w_down)
        _, pull = jax.vjp(swiglu, gate, upper)
        gate_grad, upper_grad = pull(hidden_grad)
        gate_grad = gate_grad.astype(jnp.bfloat16)
        upper_grad = upper_grad.astype(jnp.bfloat16)
        gate_w_grad = inner_rows(normed_mid, gate_grad)
        up_w_grad = inner_rows(normed_mid, upper_grad)
        mlp_sums = plan.dp_rs([down_grad_t, gate_w_grad, up_w_grad])
        mid_part = (outer_cols(gate_grad, w_gate) + outer_cols(upper_grad, w_up)).astype(
            jnp.bfloat16
        )
        mid_grad = plan.tp_sum(mid_part).astype(jnp.float32)
        resid_grad = cotangent.astype(jnp.float32) + norm_back(resid, mlp_gain, mid_grad)
        mlp_gain_part = gain_term(resid_rows, lax.dynamic_slice_in_dim(mid_grad, offset, share, 0))
        resid_low = resid_grad.astype(jnp.bfloat16)
        out_w_grad_t = inner_rows(resid_low, attended)
        attended_grad = outer_cols(resid_low, w_out).astype(jnp.bfloat16)
        q_grad, k_grad, v_grad, qg_part, kg_part = attend_back(
            attended_grad, q_raw, k_raw, query_gain, key_gain, queries, keys_rot, values, logsum, seqs
        )
        query_w_grad = inner_rows(normed_in, q_grad)
        key_w_grad = inner_rows(normed_in, k_grad)
        value_w_grad = inner_rows(normed_in, v_grad)
        attn_sums = plan.dp_rs([out_w_grad_t, query_w_grad, key_w_grad, value_w_grad])
        in_part = (
            outer_cols(q_grad, w_query)
            + outer_cols(k_grad, key_matrix)
            + outer_cols(v_grad, value_matrix)
        ).astype(jnp.bfloat16)
        in_grad = plan.tp_sum(in_part).astype(jnp.float32)
        input_grad = resid_grad + norm_back(stream, attn_gain, in_grad)
        attn_gain_part = gain_term(stream_rows, lax.dynamic_slice_in_dim(in_grad, offset, share, 0))
        gains = plan.all_sum(jnp.concatenate([attn_gain_part, mlp_gain_part, qg_part, kg_part]))
        width = attn_gain_part.shape[0]
        head = qg_part.shape[0]
        attn_gain_grad = gains[:width]
        mlp_gain_grad = gains[width : 2 * width]
        query_gain_grad = gains[2 * width : 2 * width + head]
        key_gain_grad = gains[2 * width + head :]
        down_sum, gate_sum, up_sum = mlp_sums
        out_sum, query_sum, key_sum, value_sum = attn_sums
        return (
            mixed,
            input_grad,
            attn_gain_grad,
            mlp_gain_grad,
            query_gain_grad,
            key_gain_grad,
            query_sum,
            key_sum,
            value_sum,
            out_sum.T,
            gate_sum,
            up_sum,
            down_sum.T,
        )

    return on_device


def solution(mesh):
    plan = Plan(mesh)
    placed = (
        P("dp", None),
        P(),
        P(None, "tensor"),
        P(None, "tensor"),
        P(None, "tensor"),
        P(),
        P(),
        P("tensor", None),
        P(),
        P(None, "tensor"),
        P(None, "tensor"),
        P("tensor", None),
        P("dp", None),
    )
    return jax.shard_map(
        make_on_device(plan),
        mesh=mesh,
        in_specs=placed,
        out_specs=(
            P("dp", None),
            P("dp", None),
            P(),
            P(),
            P(),
            P(),
            P("dp", "tensor"),
            P("dp", "tensor"),
            P("dp", "tensor"),
            P("tensor", "dp"),
            P("dp", "tensor"),
            P("dp", "tensor"),
            P("tensor", "dp"),
        ),
        check_vma=False,
    )
```

```python
import itertools
import math

import jax
import jax.numpy as jnp
import numpy as np
from jax import lax
from jax.sharding import PartitionSpec as P

HEAD_SIZE = 128
LEN = 128


EPS = 1e-06
THETA = 1000000.0


def product(form, left, right):
    return jnp.einsum(form, left, right, preferred_element_type=jnp.float32)


def matmul(left, right):
    return jnp.dot(left, right, preferred_element_type=jnp.float32)


def inner_rows(left, right):
    return lax.dot_general(
        left, right, (((0,), (0,)), ((), ())), preferred_element_type=jnp.float32
    )


def outer_cols(left, right):
    return lax.dot_general(
        left, right, (((1,), (1,)), ((), ())), preferred_element_type=jnp.float32
    )


def rms_scale(values, gain):
    return values * lax.rsqrt(jnp.mean(values * values, -1, keepdims=True) + EPS) * gain


def norm_back(values, gain, upstream):
    factor = lax.rsqrt(jnp.mean(values * values, -1, keepdims=True) + EPS)
    scaled = gain * upstream
    return factor * scaled - values * factor**3 * jnp.mean(scaled * values, -1, keepdims=True)


def gain_term(values, upstream):
    factor = lax.rsqrt(jnp.mean(values * values, -1, keepdims=True) + EPS)
    return jnp.sum(upstream * values * factor, 0)


def swiglu(gate, upper):
    return jax.nn.silu(gate) * upper


def rope_tables(length, width):
    position = jnp.arange(length).astype(jnp.float32)
    freqs = jnp.exp(jnp.arange(width // 2).astype(jnp.float32) * (-2.0 * math.log(THETA) / width))
    angles = position[:, None] * freqs[None, :]
    cosine = jnp.cos(angles)
    sine = jnp.sin(angles)
    return (jnp.concatenate([cosine, cosine], -1), jnp.concatenate([sine, sine], -1))


def head_prep(values, gain, cosine, sine):
    normed = values * lax.rsqrt(jnp.mean(values * values, -1, keepdims=True) + EPS) * gain
    half = normed.shape[-1] // 2
    turned = jnp.concatenate([-normed[..., half:], normed[..., :half]], -1)
    return normed * cosine[:, None, :] + turned * sine[:, None, :]


def causal_scores(queries, keys_rot, length):
    scores = product("sqgrd,skgd->sgrqk", queries, keys_rot) * (1.0 / math.sqrt(HEAD_SIZE))
    allowed = jnp.arange(length)[:, None] >= jnp.arange(length)[None, :]
    return jnp.where(allowed, scores, -1e30)


def attend(q_raw, k_raw, v_raw, query_gain, key_gain, seqs):
    total = q_raw.shape[0]
    length = total // seqs
    heads = q_raw.shape[1] // HEAD_SIZE
    kv_heads = k_raw.shape[1] // HEAD_SIZE
    repeat = heads // kv_heads
    cosine, sine = rope_tables(length, HEAD_SIZE)
    queries = head_prep(q_raw.reshape(seqs, length, heads, HEAD_SIZE), query_gain, cosine, sine)
    queries = queries.astype(jnp.bfloat16).reshape(seqs, length, kv_heads, repeat, HEAD_SIZE)
    keys_rot = head_prep(
        k_raw.reshape(seqs, length, kv_heads, HEAD_SIZE), key_gain, cosine, sine
    ).astype(jnp.bfloat16)
    values = v_raw.astype(jnp.bfloat16).reshape(seqs, length, kv_heads, HEAD_SIZE)
    scores = causal_scores(queries, keys_rot, length)
    top = jnp.max(scores, -1, keepdims=True)
    logsum = top + jnp.log(jnp.sum(jnp.exp(scores - top), -1, keepdims=True))
    weights = jnp.exp(scores - logsum).astype(jnp.bfloat16)
    attended = (
        product("sgrqk,skgd->sqgrd", weights, values)
        .astype(jnp.bfloat16)
        .reshape(total, heads * HEAD_SIZE)
    )
    return (attended, logsum, queries, keys_rot, values)


def attend_back(
    upstream, q_raw, k_raw, query_gain, key_gain, queries, keys_rot, values, logsum, seqs
):
    total = q_raw.shape[0]
    length = total // seqs
    heads = q_raw.shape[1] // HEAD_SIZE
    kv_heads = k_raw.shape[1] // HEAD_SIZE
    repeat = heads // kv_heads
    cosine, sine = rope_tables(length, HEAD_SIZE)
    grad_out = upstream.reshape(seqs, length, kv_heads, repeat, HEAD_SIZE)
    scores = causal_scores(queries, keys_rot, length)
    probs = jnp.exp(scores - logsum)
    value_grad = product("sgrqk,sqgrd->skgd", probs.astype(jnp.bfloat16), grad_out)
    prob_grad = product("sqgrd,skgd->sgrqk", grad_out, values)
    center = jnp.sum(probs * prob_grad, -1, keepdims=True)
    score_grad = (probs * (prob_grad - center) * (1.0 / math.sqrt(HEAD_SIZE))).astype(jnp.bfloat16)
    query_rot_grad = product("sgrqk,skgd->sqgrd", score_grad, keys_rot).reshape(
        seqs, length, heads, HEAD_SIZE
    )
    key_rot_grad = product("sgrqk,sqgrd->skgd", score_grad, queries)
    query_in = q_raw.reshape(seqs, length, heads, HEAD_SIZE)
    key_in = k_raw.reshape(seqs, length, kv_heads, HEAD_SIZE)
    _, pull_query = jax.vjp(
        lambda inner, gain: head_prep(inner, gain, cosine, sine), query_in, query_gain
    )
    query_grad, query_gain_grad = pull_query(query_rot_grad)
    _, pull_key = jax.vjp(
        lambda inner, gain: head_prep(inner, gain, cosine, sine), key_in, key_gain
    )
    key_grad, key_gain_grad = pull_key(key_rot_grad)
    return (
        query_grad.astype(jnp.bfloat16).reshape(total, heads * HEAD_SIZE),
        key_grad.astype(jnp.bfloat16).reshape(total, kv_heads * HEAD_SIZE),
        value_grad.astype(jnp.bfloat16).reshape(total, kv_heads * HEAD_SIZE),
        query_gain_grad,
        key_gain_grad,
    )


def snake_ring(coords):
    coords = [tuple(c) for c in coords]
    dims = [d for d in range(len(coords[0])) if len({c[d] for c in coords}) > 1]
    if not dims:
        return list(range(len(coords)))
    values = [sorted({c[d] for c in coords}) for d in dims]
    where = {tuple(c[d] for d in dims): i for i, c in enumerate(coords)}
    best = None
    for perm in itertools.permutations(range(len(dims))):
        def walk(level):
            if level == len(perm):
                return [()]
            inner = walk(level + 1)
            out = []
            for i, value in enumerate(values[perm[level]]):
                seq = inner if i % 2 == 0 else inner[::-1]
                out += [((perm[level], value),) + t for t in seq]
            return out

        order = []
        for path in walk(0):
            key = dict(path)
            point = tuple(key[k] for k in range(len(dims)))
            if point in where:
                order.append(where[point])
        if len(order) != len(coords):
            continue
        cost = sum(
            sum(abs(a - b) for a, b in zip(coords[order[i]], coords[order[(i + 1) % len(order)]]))
            for i in range(len(order))
        )
        if best is None or cost < best[0]:
            best = (cost, order)
    return best[1] if best else list(range(len(coords)))


class Plan:
    def __init__(self, mesh):
        names = mesh.axis_names
        devices = np.asarray(mesh.devices)
        dp_axis, tp_axis = names.index("dp"), names.index("tensor")
        devices = np.transpose(devices, (dp_axis, tp_axis))
        self.n_dp, self.n_tp = devices.shape
        dp_coords = [tuple(devices[d, 0].coords) for d in range(self.n_dp)]
        self.ring = snake_ring(dp_coords)
        self.pos = [self.ring.index(d) for d in range(self.n_dp)]
        n = self.n_dp
        self.cw = [(self.ring[i], self.ring[(i + 1) % n]) for i in range(n)]
        self.ccw = [(b, a) for a, b in self.cw]
        group = [devices[0, t] for t in range(self.n_tp)]
        self.tp_ok = False
        if self.n_tp == 4:
            chip = [tuple(g.coords) for g in group]
            core = [g.core_on_chip for g in group]
            same = [[u for u in range(4) if u != t and chip[u] == chip[t]] for t in range(4)]
            cross = [
                [u for u in range(4) if chip[u] != chip[t] and core[u] == core[t]] for t in range(4)
            ]
            if all(len(s) == 1 for s in same) and all(len(c) == 1 for c in cross):
                self.core_pairs = [(t, same[t][0]) for t in range(4)]
                self.chip_pairs = [(t, cross[t][0]) for t in range(4)]
                self.half_of = [0 if t < same[t][0] else 1 for t in range(4)]
                self.tp_ok = True

    def tp_sum(self, part):
        if not self.tp_ok:
            return lax.psum(part.astype(jnp.float32), "tensor").astype(jnp.bfloat16)
        rows = part.shape[0]
        h = rows // 2
        t = lax.axis_index("tensor")
        half = jnp.array(self.half_of, jnp.int32)[t]
        keep = lax.dynamic_slice_in_dim(part, half * h, h, 0)
        give = lax.dynamic_slice_in_dim(part, (1 - half) * h, h, 0)
        got = lax.ppermute(give, "tensor", self.core_pairs)
        chip_sum = (keep.astype(jnp.float32) + got.astype(jnp.float32)).astype(jnp.bfloat16)
        other = lax.ppermute(chip_sum, "tensor", self.chip_pairs)
        done = (chip_sum.astype(jnp.float32) + other.astype(jnp.float32)).astype(jnp.bfloat16)
        partner = lax.ppermute(done, "tensor", self.core_pairs)
        first = jnp.where(half == 0, done, partner)
        second = jnp.where(half == 0, partner, done)
        return jnp.concatenate([first, second], 0)

    def dp_rs(self, grads):
        ring = Ring(self, grads)
        for _ in range(ring.steps):
            ring.step()
        return ring.result()

    def all_sum(self, x):
        for axis, size in (("tensor", self.n_tp), ("dp", self.n_dp)):
            if size & (size - 1):
                x = lax.psum(x, axis)
                continue
            bit = 1
            while bit < size:
                x = x + lax.ppermute(x, axis, [(i, i ^ bit) for i in range(size)])
                bit *= 2
        return x


class Ring:
    def __init__(self, plan, grads):
        self.plan = plan
        self.n = n = plan.n_dp
        self.me = lax.axis_index("dp")
        self.pos = jnp.array(plan.pos, jnp.int32)[self.me]
        self.order = jnp.array(plan.ring, jnp.int32)
        self.widths = [g.shape[1] for g in grads]
        self.blocks = [g.reshape(n, 2, g.shape[0] // n // 2, g.shape[1]) for g in grads]
        self.steps = n - 1
        self.done = 0
        self.state = None

    def piece(self, index, side):
        parts = [lax.dynamic_index_in_dim(b, index, 0, keepdims=False)[side] for b in self.blocks]
        return parts[0] if len(parts) == 1 else jnp.concatenate(parts, 1)

    def step(self):
        n, s = self.n, self.done
        own_a = self.piece(self.order[(self.pos - 1 - s) % n], 0)
        own_b = self.piece(self.order[(self.pos + 1 + s) % n], 1)
        if self.state is None:
            send_a, send_b = own_a, own_b
        else:
            send_a, send_b = self.state[0] + own_a, self.state[1] + own_b
        got_a = lax.ppermute(send_a.astype(jnp.bfloat16), "dp", self.plan.cw)
        got_b = lax.ppermute(send_b.astype(jnp.bfloat16), "dp", self.plan.ccw)
        self.state = (got_a.astype(jnp.float32), got_b.astype(jnp.float32))
        self.done += 1

    def result(self):
        acc_a, acc_b = self.state
        total = jnp.concatenate([acc_a + self.piece(self.me, 0), acc_b + self.piece(self.me, 1)], 0)
        out, start = [], 0
        for w in self.widths:
            out.append(total[:, start : start + w])
            start += w
        return out


def make_on_device(plan):
    def on_device(
        tokens,
        attn_gain,
        w_query,
        key_matrix,
        value_matrix,
        query_gain,
        key_gain,
        w_out,
        mlp_gain,
        w_gate,
        w_up,
        w_down,
        cotangent,
    ):
        count = tokens.shape[0]
        seqs = count // LEN
        share = count // lax.axis_size("tensor")
        offset = lax.axis_index("tensor") * share
        stream = tokens.astype(jnp.float32)
        stream_rows = lax.dynamic_slice_in_dim(stream, offset, share, 0)
        normed_in = rms_scale(stream, attn_gain).astype(jnp.bfloat16)
        q_raw = matmul(normed_in, w_query)
        k_raw = matmul(normed_in, key_matrix)
        v_raw = matmul(normed_in, value_matrix)
        attended, logsum, queries, keys_rot, values = attend(
            q_raw, k_raw, v_raw, query_gain, key_gain, seqs
        )
        attn_part = matmul(attended, w_out).astype(jnp.bfloat16)
        resid = stream + plan.tp_sum(attn_part).astype(jnp.float32)
        resid_rows = lax.dynamic_slice_in_dim(resid, offset, share, 0)
        normed_mid = rms_scale(resid, mlp_gain).astype(jnp.bfloat16)
        gate = matmul(normed_mid, w_gate)
        upper = matmul(normed_mid, w_up)
        hidden = swiglu(gate, upper).astype(jnp.bfloat16)
        mlp_part = matmul(hidden, w_down).astype(jnp.bfloat16)
        mixed = (resid + plan.tp_sum(mlp_part).astype(jnp.float32)).astype(jnp.bfloat16)
        down_grad_t = inner_rows(cotangent, hidden)
        hidden_grad = outer_cols(cotangent, w_down)
        _, pull = jax.vjp(swiglu, gate, upper)
        gate_grad, upper_grad = pull(hidden_grad)
        gate_grad = gate_grad.astype(jnp.bfloat16)
        upper_grad = upper_grad.astype(jnp.bfloat16)
        gate_w_grad = inner_rows(normed_mid, gate_grad)
        up_w_grad = inner_rows(normed_mid, upper_grad)
        mid_part = (outer_cols(gate_grad, w_gate) + outer_cols(upper_grad, w_up)).astype(
            jnp.bfloat16
        )
        mid_sum = plan.tp_sum(mid_part)
        mid_sum, down_grad_t, gate_w_grad, up_w_grad = lax.optimization_barrier(
            (mid_sum, down_grad_t, gate_w_grad, up_w_grad)
        )
        mid_grad = mid_sum.astype(jnp.float32)
        resid_grad = cotangent.astype(jnp.float32) + norm_back(resid, mlp_gain, mid_grad)
        mlp_gain_part = gain_term(resid_rows, lax.dynamic_slice_in_dim(mid_grad, offset, share, 0))
        resid_low = resid_grad.astype(jnp.bfloat16)
        out_w_grad_t = inner_rows(resid_low, attended)
        attended_grad = outer_cols(resid_low, w_out).astype(jnp.bfloat16)
        big = Ring(plan, [down_grad_t, gate_w_grad, up_w_grad, out_w_grad_t])
        big.step()
        chunks = 4 if seqs % 4 == 0 else 1
        per = seqs // chunks
        rows = per * LEN
        plan_steps = [big.steps * (c + 1) // (chunks + 1) for c in range(chunks)]
        q_parts, k_parts, v_parts, in_parts = [], [], [], []
        qg_part = kg_part = 0.0
        for c in range(chunks):
            span = slice(c * rows, (c + 1) * rows)
            seq_span = slice(c * per, (c + 1) * per)
            qc, kc, vc, qgc, kgc = attend_back(
                attended_grad[span],
                q_raw[span],
                k_raw[span],
                query_gain,
                key_gain,
                queries[seq_span],
                keys_rot[seq_span],
                values[seq_span],
                logsum[seq_span],
                per,
            )
            in_c = (
                outer_cols(qc, w_query) + outer_cols(kc, key_matrix) + outer_cols(vc, value_matrix)
            ).astype(jnp.bfloat16)
            while big.done < plan_steps[c]:
                big.step()
            big.state, qc, kc, vc, in_c = lax.optimization_barrier((big.state, qc, kc, vc, in_c))
            in_parts.append(plan.tp_sum(in_c))
            q_parts.append(qc)
            k_parts.append(kc)
            v_parts.append(vc)
            qg_part = qg_part + qgc
            kg_part = kg_part + kgc
        q_grad = jnp.concatenate(q_parts, 0)
        k_grad = jnp.concatenate(k_parts, 0)
        v_grad = jnp.concatenate(v_parts, 0)
        query_w_grad = inner_rows(normed_in, q_grad)
        key_w_grad = inner_rows(normed_in, k_grad)
        value_w_grad = inner_rows(normed_in, v_grad)
        while big.done < big.steps:
            big.step()
        down_sum, gate_sum, up_sum, out_sum = big.result()
        query_sum, key_sum, value_sum = plan.dp_rs([query_w_grad, key_w_grad, value_w_grad])
        in_grad = jnp.concatenate(in_parts, 0).astype(jnp.float32)
        input_grad = resid_grad + norm_back(stream, attn_gain, in_grad)
        attn_gain_part = gain_term(stream_rows, lax.dynamic_slice_in_dim(in_grad, offset, share, 0))
        gains = plan.all_sum(jnp.concatenate([attn_gain_part, mlp_gain_part, qg_part, kg_part]))
        width = attn_gain_part.shape[0]
        head = qg_part.shape[0]
        attn_gain_grad = gains[:width]
        mlp_gain_grad = gains[width : 2 * width]
        query_gain_grad = gains[2 * width : 2 * width + head]
        key_gain_grad = gains[2 * width + head :]
        return (
            mixed,
            input_grad,
            attn_gain_grad,
            mlp_gain_grad,
            query_gain_grad,
            key_gain_grad,
            query_sum,
            key_sum,
            value_sum,
            out_sum.T,
            gate_sum,
            up_sum,
            down_sum.T,
        )

    return on_device


def solution(mesh):
    plan = Plan(mesh)
    placed = (
        P("dp", None),
        P(),
        P(None, "tensor"),
        P(None, "tensor"),
        P(None, "tensor"),
        P(),
        P(),
        P("tensor", None),
        P(),
        P(None, "tensor"),
        P(None, "tensor"),
        P("tensor", None),
        P("dp", None),
    )
    return jax.shard_map(
        make_on_device(plan),
        mesh=mesh,
        in_specs=placed,
        out_specs=(
            P("dp", None),
            P("dp", None),
            P(),
            P(),
            P(),
            P(),
            P("dp", "tensor"),
            P("dp", "tensor"),
            P("dp", "tensor"),
            P("tensor", "dp"),
            P("dp", "tensor"),
            P("dp", "tensor"),
            P("tensor", "dp"),
        ),
        check_vma=False,
    )
```

```python
import itertools
import math

import jax
import jax.numpy as jnp
import numpy as np
from jax import lax
from jax.sharding import PartitionSpec as P


HEAD_SIZE = 128
LEN = 128


EPS = 1e-06
THETA = 1000000.0


def product(form, left, right):
    return jnp.einsum(form, left, right, preferred_element_type=jnp.float32)


def matmul(left, right):
    return jnp.dot(left, right, preferred_element_type=jnp.float32)


def inner_rows(left, right):
    return lax.dot_general(
        left, right, (((0,), (0,)), ((), ())), preferred_element_type=jnp.float32
    )


def outer_cols(left, right):
    return lax.dot_general(
        left, right, (((1,), (1,)), ((), ())), preferred_element_type=jnp.float32
    )


def rms_scale(values, gain):
    return values * lax.rsqrt(jnp.mean(values * values, -1, keepdims=True) + EPS) * gain


def norm_back(values, gain, upstream):
    factor = lax.rsqrt(jnp.mean(values * values, -1, keepdims=True) + EPS)
    scaled = gain * upstream
    return factor * scaled - values * factor**3 * jnp.mean(scaled * values, -1, keepdims=True)


def gain_term(values, upstream):
    factor = lax.rsqrt(jnp.mean(values * values, -1, keepdims=True) + EPS)
    return jnp.sum(upstream * values * factor, 0)


def swiglu(gate, upper):
    return jax.nn.silu(gate) * upper


def rope_tables(length, width):
    position = jnp.arange(length).astype(jnp.float32)
    freqs = jnp.exp(jnp.arange(width // 2).astype(jnp.float32) * (-2.0 * math.log(THETA) / width))
    angles = position[:, None] * freqs[None, :]
    cosine = jnp.cos(angles)
    sine = jnp.sin(angles)
    return (jnp.concatenate([cosine, cosine], -1), jnp.concatenate([sine, sine], -1))


def head_prep(values, gain, cosine, sine):
    normed = values * lax.rsqrt(jnp.mean(values * values, -1, keepdims=True) + EPS) * gain
    half = normed.shape[-1] // 2
    turned = jnp.concatenate([-normed[..., half:], normed[..., :half]], -1)
    return normed * cosine[:, None, :] + turned * sine[:, None, :]


def causal_scores(queries, keys_rot, length):
    scores = product("sqgrd,skgd->sgrqk", queries, keys_rot) * (1.0 / math.sqrt(HEAD_SIZE))
    allowed = jnp.arange(length)[:, None] >= jnp.arange(length)[None, :]
    return jnp.where(allowed, scores, -1e30)


def attend(q_raw, k_raw, v_raw, query_gain, key_gain, seqs):
    total = q_raw.shape[0]
    length = total // seqs
    heads = q_raw.shape[1] // HEAD_SIZE
    kv_heads = k_raw.shape[1] // HEAD_SIZE
    repeat = heads // kv_heads
    cosine, sine = rope_tables(length, HEAD_SIZE)
    queries = head_prep(q_raw.reshape(seqs, length, heads, HEAD_SIZE), query_gain, cosine, sine)
    queries = queries.astype(jnp.bfloat16).reshape(seqs, length, kv_heads, repeat, HEAD_SIZE)
    keys_rot = head_prep(
        k_raw.reshape(seqs, length, kv_heads, HEAD_SIZE), key_gain, cosine, sine
    ).astype(jnp.bfloat16)
    values = v_raw.astype(jnp.bfloat16).reshape(seqs, length, kv_heads, HEAD_SIZE)
    scores = causal_scores(queries, keys_rot, length)
    top = jnp.max(scores, -1, keepdims=True)
    logsum = top + jnp.log(jnp.sum(jnp.exp(scores - top), -1, keepdims=True))
    weights = jnp.exp(scores - logsum).astype(jnp.bfloat16)
    attended = (
        product("sgrqk,skgd->sqgrd", weights, values)
        .astype(jnp.bfloat16)
        .reshape(total, heads * HEAD_SIZE)
    )
    return (attended, logsum, queries, keys_rot, values)


def attend_back(
    upstream, q_raw, k_raw, query_gain, key_gain, queries, keys_rot, values, logsum, seqs
):
    total = q_raw.shape[0]
    length = total // seqs
    heads = q_raw.shape[1] // HEAD_SIZE
    kv_heads = k_raw.shape[1] // HEAD_SIZE
    repeat = heads // kv_heads
    cosine, sine = rope_tables(length, HEAD_SIZE)
    grad_out = upstream.reshape(seqs, length, kv_heads, repeat, HEAD_SIZE)
    scores = causal_scores(queries, keys_rot, length)
    probs = jnp.exp(scores - logsum)
    value_grad = product("sgrqk,sqgrd->skgd", probs.astype(jnp.bfloat16), grad_out)
    prob_grad = product("sqgrd,skgd->sgrqk", grad_out, values)
    center = jnp.sum(probs * prob_grad, -1, keepdims=True)
    score_grad = (probs * (prob_grad - center) * (1.0 / math.sqrt(HEAD_SIZE))).astype(jnp.bfloat16)
    query_rot_grad = product("sgrqk,skgd->sqgrd", score_grad, keys_rot).reshape(
        seqs, length, heads, HEAD_SIZE
    )
    key_rot_grad = product("sgrqk,sqgrd->skgd", score_grad, queries)
    query_in = q_raw.reshape(seqs, length, heads, HEAD_SIZE)
    key_in = k_raw.reshape(seqs, length, kv_heads, HEAD_SIZE)
    _, pull_query = jax.vjp(
        lambda inner, gain: head_prep(inner, gain, cosine, sine), query_in, query_gain
    )
    query_grad, query_gain_grad = pull_query(query_rot_grad)
    _, pull_key = jax.vjp(
        lambda inner, gain: head_prep(inner, gain, cosine, sine), key_in, key_gain
    )
    key_grad, key_gain_grad = pull_key(key_rot_grad)
    return (
        query_grad.astype(jnp.bfloat16).reshape(total, heads * HEAD_SIZE),
        key_grad.astype(jnp.bfloat16).reshape(total, kv_heads * HEAD_SIZE),
        value_grad.astype(jnp.bfloat16).reshape(total, kv_heads * HEAD_SIZE),
        query_gain_grad,
        key_gain_grad,
    )


def snake_ring(coords):
    coords = [tuple(c) for c in coords]
    dims = [d for d in range(len(coords[0])) if len({c[d] for c in coords}) > 1]
    if not dims:
        return list(range(len(coords)))
    values = [sorted({c[d] for c in coords}) for d in dims]
    where = {tuple(c[d] for d in dims): i for i, c in enumerate(coords)}
    best = None
    for perm in itertools.permutations(range(len(dims))):
        def walk(level):
            if level == len(perm):
                return [()]
            inner = walk(level + 1)
            out = []
            for i, value in enumerate(values[perm[level]]):
                seq = inner if i % 2 == 0 else inner[::-1]
                out += [((perm[level], value),) + t for t in seq]
            return out

        order = []
        for path in walk(0):
            key = dict(path)
            point = tuple(key[k] for k in range(len(dims)))
            if point in where:
                order.append(where[point])
        if len(order) != len(coords):
            continue
        cost = sum(
            sum(abs(a - b) for a, b in zip(coords[order[i]], coords[order[(i + 1) % len(order)]]))
            for i in range(len(order))
        )
        if best is None or cost < best[0]:
            best = (cost, order)
    return best[1] if best else list(range(len(coords)))


class Plan:
    def __init__(self, mesh):
        names = mesh.axis_names
        devices = np.asarray(mesh.devices)
        dp_axis, tp_axis = names.index("dp"), names.index("tensor")
        devices = np.transpose(devices, (dp_axis, tp_axis))
        self.n_dp, self.n_tp = devices.shape
        dp_coords = [tuple(devices[d, 0].coords) for d in range(self.n_dp)]
        self.ring = snake_ring(dp_coords)
        self.pos = [self.ring.index(d) for d in range(self.n_dp)]
        n = self.n_dp
        self.cw = [(self.ring[i], self.ring[(i + 1) % n]) for i in range(n)]
        self.ccw = [(b, a) for a, b in self.cw]
        group = [devices[0, t] for t in range(self.n_tp)]
        self.tp_ok = False
        if self.n_tp == 4:
            chip = [tuple(g.coords) for g in group]
            core = [g.core_on_chip for g in group]
            same = [[u for u in range(4) if u != t and chip[u] == chip[t]] for t in range(4)]
            cross = [
                [u for u in range(4) if chip[u] != chip[t] and core[u] == core[t]] for t in range(4)
            ]
            if all(len(s) == 1 for s in same) and all(len(c) == 1 for c in cross):
                self.core_pairs = [(t, same[t][0]) for t in range(4)]
                self.chip_pairs = [(t, cross[t][0]) for t in range(4)]
                self.half_of = [0 if t < same[t][0] else 1 for t in range(4)]
                self.tp_ok = True

    def tp_sum(self, part):
        if not self.tp_ok:
            return lax.psum(part.astype(jnp.float32), "tensor").astype(jnp.bfloat16)
        rows = part.shape[0]
        h = rows // 2
        t = lax.axis_index("tensor")
        half = jnp.array(self.half_of, jnp.int32)[t]
        keep = lax.dynamic_slice_in_dim(part, half * h, h, 0)
        give = lax.dynamic_slice_in_dim(part, (1 - half) * h, h, 0)
        got = lax.ppermute(give, "tensor", self.core_pairs)
        chip_sum = (keep.astype(jnp.float32) + got.astype(jnp.float32)).astype(jnp.bfloat16)
        other = lax.ppermute(chip_sum, "tensor", self.chip_pairs)
        done = (chip_sum.astype(jnp.float32) + other.astype(jnp.float32)).astype(jnp.bfloat16)
        partner = lax.ppermute(done, "tensor", self.core_pairs)
        first = jnp.where(half == 0, done, partner)
        second = jnp.where(half == 0, partner, done)
        return jnp.concatenate([first, second], 0)

    def dp_rs(self, grads):
        ring = Ring(self, grads)
        for _ in range(ring.steps):
            ring.step()
        return ring.result()

    def all_sum(self, x):
        for axis, size in (("tensor", self.n_tp), ("dp", self.n_dp)):
            if size & (size - 1):
                x = lax.psum(x, axis)
                continue
            bit = 1
            while bit < size:
                x = x + lax.ppermute(x, axis, [(i, i ^ bit) for i in range(size)])
                bit *= 2
        return x


class Ring:
    def __init__(self, plan, grads):
        self.plan = plan
        self.n = n = plan.n_dp
        self.me = lax.axis_index("dp")
        self.pos = jnp.array(plan.pos, jnp.int32)[self.me]
        self.order = jnp.array(plan.ring, jnp.int32)
        self.widths = [g.shape[1] for g in grads]
        self.blocks = [g.reshape(n, 2, g.shape[0] // n // 2, g.shape[1]) for g in grads]
        self.steps = n - 1
        self.done = 0
        self.state = None

    def piece(self, index, side):
        parts = [lax.dynamic_index_in_dim(b, index, 0, keepdims=False)[side] for b in self.blocks]
        return parts[0] if len(parts) == 1 else jnp.concatenate(parts, 1)

    def step(self):
        n, s = self.n, self.done
        own_a = self.piece(self.order[(self.pos - 1 - s) % n], 0)
        own_b = self.piece(self.order[(self.pos + 1 + s) % n], 1)
        if self.state is None:
            send_a, send_b = own_a, own_b
        else:
            send_a, send_b = self.state[0] + own_a, self.state[1] + own_b
        got_a = lax.ppermute(send_a.astype(jnp.bfloat16), "dp", self.plan.cw)
        got_b = lax.ppermute(send_b.astype(jnp.bfloat16), "dp", self.plan.ccw)
        self.state = (got_a.astype(jnp.float32), got_b.astype(jnp.float32))
        self.done += 1

    def result(self):
        acc_a, acc_b = self.state
        total = jnp.concatenate([acc_a + self.piece(self.me, 0), acc_b + self.piece(self.me, 1)], 0)
        out, start = [], 0
        for w in self.widths:
            out.append(total[:, start : start + w])
            start += w
        return out


def make_on_device(plan):
    def body(
        tokens,
        attn_gain,
        w_query,
        key_matrix,
        value_matrix,
        query_gain,
        key_gain,
        w_out,
        mlp_gain,
        w_gate,
        w_up,
        w_down,
        cotangent,
    ):
        count = tokens.shape[0]
        seqs = count // LEN
        share = count // lax.axis_size("tensor")
        offset = lax.axis_index("tensor") * share
        stream = tokens.astype(jnp.float32)
        stream_rows = lax.dynamic_slice_in_dim(stream, offset, share, 0)
        normed_in = rms_scale(stream, attn_gain).astype(jnp.bfloat16)
        q_raw = matmul(normed_in, w_query)
        k_raw = matmul(normed_in, key_matrix)
        v_raw = matmul(normed_in, value_matrix)
        attended, logsum, queries, keys_rot, values = attend(
            q_raw, k_raw, v_raw, query_gain, key_gain, seqs
        )
        attn_part = matmul(attended, w_out).astype(jnp.bfloat16)
        resid = stream + plan.tp_sum(attn_part).astype(jnp.float32)
        resid_rows = lax.dynamic_slice_in_dim(resid, offset, share, 0)
        normed_mid = rms_scale(resid, mlp_gain).astype(jnp.bfloat16)
        gate = matmul(normed_mid, w_gate)
        upper = matmul(normed_mid, w_up)
        hidden = swiglu(gate, upper).astype(jnp.bfloat16)
        mlp_part = matmul(hidden, w_down).astype(jnp.bfloat16)
        mixed = (resid + plan.tp_sum(mlp_part).astype(jnp.float32)).astype(jnp.bfloat16)
        down_grad_t = inner_rows(cotangent, hidden)
        hidden_grad = outer_cols(cotangent, w_down)
        _, pull = jax.vjp(swiglu, gate, upper)
        gate_grad, upper_grad = pull(hidden_grad)
        gate_grad = gate_grad.astype(jnp.bfloat16)
        upper_grad = upper_grad.astype(jnp.bfloat16)
        mid_part = (outer_cols(gate_grad, w_gate) + outer_cols(upper_grad, w_up)).astype(
            jnp.bfloat16
        )
        mid_sum = plan.tp_sum(mid_part)
        gate_w_grad = inner_rows(normed_mid, gate_grad)
        up_w_grad = inner_rows(normed_mid, upper_grad)
        big = Ring(plan, [down_grad_t, gate_w_grad, up_w_grad])
        big.step()
        mid_grad = mid_sum.astype(jnp.float32)
        resid_grad = cotangent.astype(jnp.float32) + norm_back(resid, mlp_gain, mid_grad)
        mlp_gain_part = gain_term(resid_rows, lax.dynamic_slice_in_dim(mid_grad, offset, share, 0))
        resid_low = resid_grad.astype(jnp.bfloat16)
        out_w_grad_t = inner_rows(resid_low, attended)
        attended_grad = outer_cols(resid_low, w_out).astype(jnp.bfloat16)
        small = Ring(plan, [out_w_grad_t])
        for _ in range(big.steps - 1):
            big.step()
            small.step()
        q_grad, k_grad, v_grad, qg_part, kg_part = attend_back(
            attended_grad, q_raw, k_raw, query_gain, key_gain, queries, keys_rot, values, logsum, seqs
        )
        in_part = (
            outer_cols(q_grad, w_query)
            + outer_cols(k_grad, key_matrix)
            + outer_cols(v_grad, value_matrix)
        ).astype(jnp.bfloat16)
        query_w_grad = inner_rows(normed_in, q_grad)
        key_w_grad = inner_rows(normed_in, k_grad)
        value_w_grad = inner_rows(normed_in, v_grad)
        small.step()
        in_grad = plan.tp_sum(in_part).astype(jnp.float32)
        down_sum, gate_sum, up_sum = big.result()
        (out_sum,) = small.result()
        query_sum, key_sum, value_sum = plan.dp_rs([query_w_grad, key_w_grad, value_w_grad])
        input_grad = resid_grad + norm_back(stream, attn_gain, in_grad)
        attn_gain_part = gain_term(stream_rows, lax.dynamic_slice_in_dim(in_grad, offset, share, 0))
        gains = plan.all_sum(jnp.concatenate([attn_gain_part, mlp_gain_part, qg_part, kg_part]))
        width = attn_gain_part.shape[0]
        head = qg_part.shape[0]
        attn_gain_grad = gains[:width]
        mlp_gain_grad = gains[width : 2 * width]
        query_gain_grad = gains[2 * width : 2 * width + head]
        key_gain_grad = gains[2 * width + head :]
        return (
            mixed,
            input_grad,
            attn_gain_grad,
            mlp_gain_grad,
            query_gain_grad,
            key_gain_grad,
            query_sum,
            key_sum,
            value_sum,
            out_sum.T,
            gate_sum,
            up_sum,
            down_sum.T,
        )

    return body


def solution(mesh):
    plan = Plan(mesh)
    placed = (
        P("dp", None),
        P(),
        P(None, "tensor"),
        P(None, "tensor"),
        P(None, "tensor"),
        P(),
        P(),
        P("tensor", None),
        P(),
        P(None, "tensor"),
        P(None, "tensor"),
        P("tensor", None),
        P("dp", None),
    )
    return jax.shard_map(
        make_on_device(plan),
        mesh=mesh,
        in_specs=placed,
        out_specs=(
            P("dp", None),
            P("dp", None),
            P(),
            P(),
            P(),
            P(),
            P("dp", "tensor"),
            P("dp", "tensor"),
            P("dp", "tensor"),
            P("tensor", "dp"),
            P("dp", "tensor"),
            P("dp", "tensor"),
            P("tensor", "dp"),
        ),
        check_vma=False,
    )
```

```python
import itertools
import math

import jax
import jax.numpy as jnp
import numpy as np
from jax import lax
from jax.sharding import PartitionSpec as P

HEAD_SIZE = 128
LEN = 128


EPS = 1e-06
THETA = 1000000.0


def product(form, left, right):
    return jnp.einsum(form, left, right, preferred_element_type=jnp.float32)


def matmul(left, right):
    return jnp.dot(left, right, preferred_element_type=jnp.float32)


def inner_rows(left, right):
    return lax.dot_general(
        left, right, (((0,), (0,)), ((), ())), preferred_element_type=jnp.float32
    )


def outer_cols(left, right):
    return lax.dot_general(
        left, right, (((1,), (1,)), ((), ())), preferred_element_type=jnp.float32
    )


def rms_scale(values, gain):
    return values * lax.rsqrt(jnp.mean(values * values, -1, keepdims=True) + EPS) * gain


def norm_back(values, gain, upstream):
    factor = lax.rsqrt(jnp.mean(values * values, -1, keepdims=True) + EPS)
    scaled = gain * upstream
    return factor * scaled - values * factor**3 * jnp.mean(scaled * values, -1, keepdims=True)


def gain_term(values, upstream):
    factor = lax.rsqrt(jnp.mean(values * values, -1, keepdims=True) + EPS)
    return jnp.sum(upstream * values * factor, 0)


def swiglu(gate, upper):
    return jax.nn.silu(gate) * upper


def rope_tables(length, width):
    position = jnp.arange(length).astype(jnp.float32)
    freqs = jnp.exp(jnp.arange(width // 2).astype(jnp.float32) * (-2.0 * math.log(THETA) / width))
    angles = position[:, None] * freqs[None, :]
    cosine = jnp.cos(angles)
    sine = jnp.sin(angles)
    return (jnp.concatenate([cosine, cosine], -1), jnp.concatenate([sine, sine], -1))


def head_prep(values, gain, cosine, sine):
    normed = values * lax.rsqrt(jnp.mean(values * values, -1, keepdims=True) + EPS) * gain
    half = normed.shape[-1] // 2
    turned = jnp.concatenate([-normed[..., half:], normed[..., :half]], -1)
    return normed * cosine[:, None, :] + turned * sine[:, None, :]


def causal_scores(queries, keys_rot, length):
    scores = product("sqgrd,skgd->sgrqk", queries, keys_rot) * (1.0 / math.sqrt(HEAD_SIZE))
    allowed = jnp.arange(length)[:, None] >= jnp.arange(length)[None, :]
    return jnp.where(allowed, scores, -1e30)


def attend(q_raw, k_raw, v_raw, query_gain, key_gain, seqs):
    total = q_raw.shape[0]
    length = total // seqs
    heads = q_raw.shape[1] // HEAD_SIZE
    kv_heads = k_raw.shape[1] // HEAD_SIZE
    repeat = heads // kv_heads
    cosine, sine = rope_tables(length, HEAD_SIZE)
    queries = head_prep(q_raw.reshape(seqs, length, heads, HEAD_SIZE), query_gain, cosine, sine)
    queries = queries.astype(jnp.bfloat16).reshape(seqs, length, kv_heads, repeat, HEAD_SIZE)
    keys_rot = head_prep(
        k_raw.reshape(seqs, length, kv_heads, HEAD_SIZE), key_gain, cosine, sine
    ).astype(jnp.bfloat16)
    values = v_raw.astype(jnp.bfloat16).reshape(seqs, length, kv_heads, HEAD_SIZE)
    scores = causal_scores(queries, keys_rot, length)
    top = jnp.max(scores, -1, keepdims=True)
    logsum = top + jnp.log(jnp.sum(jnp.exp(scores - top), -1, keepdims=True))
    weights = jnp.exp(scores - logsum).astype(jnp.bfloat16)
    attended = (
        product("sgrqk,skgd->sqgrd", weights, values)
        .astype(jnp.bfloat16)
        .reshape(total, heads * HEAD_SIZE)
    )
    return (attended, logsum, queries, keys_rot, values)


def attend_back(
    upstream, q_raw, k_raw, query_gain, key_gain, queries, keys_rot, values, logsum, seqs, hook
):
    total = q_raw.shape[0]
    length = total // seqs
    heads = q_raw.shape[1] // HEAD_SIZE
    kv_heads = k_raw.shape[1] // HEAD_SIZE
    repeat = heads // kv_heads
    cosine, sine = rope_tables(length, HEAD_SIZE)
    grad_out = upstream.reshape(seqs, length, kv_heads, repeat, HEAD_SIZE)
    scores = causal_scores(queries, keys_rot, length)
    probs = jnp.exp(scores - logsum)
    probs = hook(probs)
    value_grad = product("sgrqk,sqgrd->skgd", probs.astype(jnp.bfloat16), grad_out)
    prob_grad = product("sqgrd,skgd->sgrqk", grad_out, values)
    value_grad, prob_grad = hook((value_grad, prob_grad))
    center = jnp.sum(probs * prob_grad, -1, keepdims=True)
    score_grad = (probs * (prob_grad - center) * (1.0 / math.sqrt(HEAD_SIZE))).astype(jnp.bfloat16)
    score_grad = hook(score_grad)
    query_rot_grad = product("sgrqk,skgd->sqgrd", score_grad, keys_rot).reshape(
        seqs, length, heads, HEAD_SIZE
    )
    key_rot_grad = product("sgrqk,sqgrd->skgd", score_grad, queries)
    query_rot_grad, key_rot_grad = hook((query_rot_grad, key_rot_grad))
    query_in = q_raw.reshape(seqs, length, heads, HEAD_SIZE)
    key_in = k_raw.reshape(seqs, length, kv_heads, HEAD_SIZE)
    _, pull_query = jax.vjp(
        lambda inner, gain: head_prep(inner, gain, cosine, sine), query_in, query_gain
    )
    query_grad, query_gain_grad = pull_query(query_rot_grad)
    _, pull_key = jax.vjp(
        lambda inner, gain: head_prep(inner, gain, cosine, sine), key_in, key_gain
    )
    key_grad, key_gain_grad = pull_key(key_rot_grad)
    query_grad, key_grad = hook((query_grad, key_grad))
    return (
        query_grad.astype(jnp.bfloat16).reshape(total, heads * HEAD_SIZE),
        key_grad.astype(jnp.bfloat16).reshape(total, kv_heads * HEAD_SIZE),
        value_grad.astype(jnp.bfloat16).reshape(total, kv_heads * HEAD_SIZE),
        query_gain_grad,
        key_gain_grad,
    )


def snake_ring(coords):
    coords = [tuple(c) for c in coords]
    dims = [d for d in range(len(coords[0])) if len({c[d] for c in coords}) > 1]
    if not dims:
        return list(range(len(coords)))
    values = [sorted({c[d] for c in coords}) for d in dims]
    where = {tuple(c[d] for d in dims): i for i, c in enumerate(coords)}
    best = None
    for perm in itertools.permutations(range(len(dims))):
        def walk(level):
            if level == len(perm):
                return [()]
            inner = walk(level + 1)
            out = []
            for i, value in enumerate(values[perm[level]]):
                seq = inner if i % 2 == 0 else inner[::-1]
                out += [((perm[level], value),) + t for t in seq]
            return out

        order = []
        for path in walk(0):
            key = dict(path)
            point = tuple(key[k] for k in range(len(dims)))
            if point in where:
                order.append(where[point])
        if len(order) != len(coords):
            continue
        cost = sum(
            sum(abs(a - b) for a, b in zip(coords[order[i]], coords[order[(i + 1) % len(order)]]))
            for i in range(len(order))
        )
        if best is None or cost < best[0]:
            best = (cost, order)
    return best[1] if best else list(range(len(coords)))


class Plan:
    def __init__(self, mesh):
        names = mesh.axis_names
        devices = np.asarray(mesh.devices)
        dp_axis, tp_axis = names.index("dp"), names.index("tensor")
        devices = np.transpose(devices, (dp_axis, tp_axis))
        self.n_dp, self.n_tp = devices.shape
        dp_coords = [tuple(devices[d, 0].coords) for d in range(self.n_dp)]
        self.ring = snake_ring(dp_coords)
        self.pos = [self.ring.index(d) for d in range(self.n_dp)]
        n = self.n_dp
        self.cw = [(self.ring[i], self.ring[(i + 1) % n]) for i in range(n)]
        self.ccw = [(b, a) for a, b in self.cw]
        group = [devices[0, t] for t in range(self.n_tp)]
        self.tp_ok = False
        if self.n_tp == 4:
            chip = [tuple(g.coords) for g in group]
            core = [g.core_on_chip for g in group]
            same = [[u for u in range(4) if u != t and chip[u] == chip[t]] for t in range(4)]
            cross = [
                [u for u in range(4) if chip[u] != chip[t] and core[u] == core[t]] for t in range(4)
            ]
            if all(len(s) == 1 for s in same) and all(len(c) == 1 for c in cross):
                self.core_pairs = [(t, same[t][0]) for t in range(4)]
                self.chip_pairs = [(t, cross[t][0]) for t in range(4)]
                self.half_of = [0 if t < same[t][0] else 1 for t in range(4)]
                self.tp_ok = True

    def tp_sum(self, part):
        if not self.tp_ok:
            return lax.psum(part.astype(jnp.float32), "tensor").astype(jnp.bfloat16)
        rows = part.shape[0]
        h = rows // 2
        t = lax.axis_index("tensor")
        half = jnp.array(self.half_of, jnp.int32)[t]
        keep = lax.dynamic_slice_in_dim(part, half * h, h, 0)
        give = lax.dynamic_slice_in_dim(part, (1 - half) * h, h, 0)
        got = lax.ppermute(give, "tensor", self.core_pairs)
        chip_sum = (keep.astype(jnp.float32) + got.astype(jnp.float32)).astype(jnp.bfloat16)
        other = lax.ppermute(chip_sum, "tensor", self.chip_pairs)
        done = (chip_sum.astype(jnp.float32) + other.astype(jnp.float32)).astype(jnp.bfloat16)
        partner = lax.ppermute(done, "tensor", self.core_pairs)
        first = jnp.where(half == 0, done, partner)
        second = jnp.where(half == 0, partner, done)
        return jnp.concatenate([first, second], 0)

    def dp_rs(self, grads):
        ring = Ring(self, grads)
        for _ in range(ring.steps):
            ring.step()
        return ring.result()

    def all_sum(self, x):
        for axis, size in (("tensor", self.n_tp), ("dp", self.n_dp)):
            if size & (size - 1):
                x = lax.psum(x, axis)
                continue
            bit = 1
            while bit < size:
                x = x + lax.ppermute(x, axis, [(i, i ^ bit) for i in range(size)])
                bit *= 2
        return x


class Ring:
    def __init__(self, plan, grads):
        self.plan = plan
        self.n = n = plan.n_dp
        self.me = lax.axis_index("dp")
        self.pos = jnp.array(plan.pos, jnp.int32)[self.me]
        self.order = jnp.array(plan.ring, jnp.int32)
        self.widths = [g.shape[1] for g in grads]
        self.grads = grads
        self.rows = grads[0].shape[0] // n
        self.steps = n - 1
        self.done = 0
        self.state = None

    def piece(self, index, side):
        half = self.rows // 2
        start = index * self.rows + side * half
        parts = [lax.dynamic_slice_in_dim(g, start, half, 0) for g in self.grads]
        return parts[0] if len(parts) == 1 else jnp.concatenate(parts, 1)

    def step(self):
        n, s = self.n, self.done
        own_a = self.piece(self.order[(self.pos - 1 - s) % n], 0)
        own_b = self.piece(self.order[(self.pos + 1 + s) % n], 1)
        if self.state is None:
            send_a, send_b = own_a, own_b
        else:
            send_a, send_b = self.state[0] + own_a, self.state[1] + own_b
        got_a = lax.ppermute(send_a.astype(jnp.bfloat16), "dp", self.plan.cw)
        got_b = lax.ppermute(send_b.astype(jnp.bfloat16), "dp", self.plan.ccw)
        self.state = (got_a.astype(jnp.float32), got_b.astype(jnp.float32))
        self.done += 1

    def result(self):
        acc_a, acc_b = self.state
        total = jnp.concatenate([acc_a + self.piece(self.me, 0), acc_b + self.piece(self.me, 1)], 0)
        out, start = [], 0
        for w in self.widths:
            out.append(total[:, start : start + w])
            start += w
        return out


def make_on_device(plan):
    def body(
        tokens,
        attn_gain,
        w_query,
        key_matrix,
        value_matrix,
        query_gain,
        key_gain,
        w_out,
        mlp_gain,
        w_gate,
        w_up,
        w_down,
        cotangent,
    ):
        count = tokens.shape[0]
        seqs = count // LEN
        share = count // lax.axis_size("tensor")
        offset = lax.axis_index("tensor") * share
        stream = tokens.astype(jnp.float32)
        stream_rows = lax.dynamic_slice_in_dim(stream, offset, share, 0)
        normed_in = rms_scale(stream, attn_gain).astype(jnp.bfloat16)
        q_raw = matmul(normed_in, w_query)
        k_raw = matmul(normed_in, key_matrix)
        v_raw = matmul(normed_in, value_matrix)
        attended, logsum, queries, keys_rot, values = attend(
            q_raw, k_raw, v_raw, query_gain, key_gain, seqs
        )
        attn_part = matmul(attended, w_out).astype(jnp.bfloat16)
        resid = stream + plan.tp_sum(attn_part).astype(jnp.float32)
        resid_rows = lax.dynamic_slice_in_dim(resid, offset, share, 0)
        normed_mid = rms_scale(resid, mlp_gain).astype(jnp.bfloat16)
        gate = matmul(normed_mid, w_gate)
        upper = matmul(normed_mid, w_up)
        hidden = swiglu(gate, upper).astype(jnp.bfloat16)
        mlp_part = matmul(hidden, w_down).astype(jnp.bfloat16)
        mixed = (resid + plan.tp_sum(mlp_part).astype(jnp.float32)).astype(jnp.bfloat16)
        down_grad_t = inner_rows(cotangent, hidden)
        hidden_grad = outer_cols(cotangent, w_down)
        _, pull = jax.vjp(swiglu, gate, upper)
        gate_grad, upper_grad = pull(hidden_grad)
        gate_grad = gate_grad.astype(jnp.bfloat16)
        upper_grad = upper_grad.astype(jnp.bfloat16)
        mid_part = (outer_cols(gate_grad, w_gate) + outer_cols(upper_grad, w_up)).astype(
            jnp.bfloat16
        )
        mid_sum = plan.tp_sum(mid_part)
        gate_w_grad = inner_rows(normed_mid, gate_grad)
        up_w_grad = inner_rows(normed_mid, upper_grad)
        big = Ring(plan, [down_grad_t, gate_w_grad, up_w_grad])
        big.step()
        mid_grad = mid_sum.astype(jnp.float32)
        resid_grad = cotangent.astype(jnp.float32) + norm_back(resid, mlp_gain, mid_grad)
        mlp_gain_part = gain_term(resid_rows, lax.dynamic_slice_in_dim(mid_grad, offset, share, 0))
        resid_low = resid_grad.astype(jnp.bfloat16)
        out_w_grad_t = inner_rows(resid_low, attended)
        attended_grad = outer_cols(resid_low, w_out).astype(jnp.bfloat16)
        small = Ring(plan, [out_w_grad_t])

        def hook(values):
            if big.done < big.steps:
                big.step()
            if small.done < small.steps:
                small.step()
            big.state, small.state, values = lax.optimization_barrier(
                (big.state, small.state, values)
            )
            return values

        resid_grad, attended_grad = hook((resid_grad, attended_grad))
        q_grad, k_grad, v_grad, qg_part, kg_part = attend_back(
            attended_grad,
            q_raw,
            k_raw,
            query_gain,
            key_gain,
            queries,
            keys_rot,
            values,
            logsum,
            seqs,
            hook,
        )
        in_part = (
            outer_cols(q_grad, w_query)
            + outer_cols(k_grad, key_matrix)
            + outer_cols(v_grad, value_matrix)
        ).astype(jnp.bfloat16)
        query_w_grad = inner_rows(normed_in, q_grad)
        key_w_grad = inner_rows(normed_in, k_grad)
        value_w_grad = inner_rows(normed_in, v_grad)
        while big.done < big.steps:
            big.step()
        while small.done < small.steps:
            small.step()
        in_grad = plan.tp_sum(in_part).astype(jnp.float32)
        down_sum, gate_sum, up_sum = big.result()
        (out_sum,) = small.result()
        query_sum, key_sum, value_sum = plan.dp_rs([query_w_grad, key_w_grad, value_w_grad])
        input_grad = resid_grad + norm_back(stream, attn_gain, in_grad)
        attn_gain_part = gain_term(stream_rows, lax.dynamic_slice_in_dim(in_grad, offset, share, 0))
        gains = plan.all_sum(jnp.concatenate([attn_gain_part, mlp_gain_part, qg_part, kg_part]))
        width = attn_gain_part.shape[0]
        head = qg_part.shape[0]
        attn_gain_grad = gains[:width]
        mlp_gain_grad = gains[width : 2 * width]
        query_gain_grad = gains[2 * width : 2 * width + head]
        key_gain_grad = gains[2 * width + head :]
        return (
            mixed,
            input_grad,
            attn_gain_grad,
            mlp_gain_grad,
            query_gain_grad,
            key_gain_grad,
            query_sum,
            key_sum,
            value_sum,
            out_sum.T,
            gate_sum,
            up_sum,
            down_sum.T,
        )

    return body


def solution(mesh):
    plan = Plan(mesh)
    placed = (
        P("dp", None),
        P(),
        P(None, "tensor"),
        P(None, "tensor"),
        P(None, "tensor"),
        P(),
        P(),
        P("tensor", None),
        P(),
        P(None, "tensor"),
        P(None, "tensor"),
        P("tensor", None),
        P("dp", None),
    )
    return jax.shard_map(
        make_on_device(plan),
        mesh=mesh,
        in_specs=placed,
        out_specs=(
            P("dp", None),
            P("dp", None),
            P(),
            P(),
            P(),
            P(),
            P("dp", "tensor"),
            P("dp", "tensor"),
            P("dp", "tensor"),
            P("tensor", "dp"),
            P("dp", "tensor"),
            P("dp", "tensor"),
            P("tensor", "dp"),
        ),
        check_vma=False,
    )
```

```python
import itertools
import math

import jax
import jax.numpy as jnp
import numpy as np
from jax import lax
from jax.sharding import PartitionSpec as P

HEAD_SIZE = 128
LEN = 128


EPS = 1e-06
THETA = 1000000.0


def product(form, left, right):
    return jnp.einsum(form, left, right, preferred_element_type=jnp.float32)


def matmul(left, right):
    return jnp.dot(left, right, preferred_element_type=jnp.float32)


def inner_rows(left, right):
    return lax.dot_general(
        left, right, (((0,), (0,)), ((), ())), preferred_element_type=jnp.float32
    )


def outer_cols(left, right):
    return lax.dot_general(
        left, right, (((1,), (1,)), ((), ())), preferred_element_type=jnp.float32
    )


def rms_scale(values, gain):
    return values * lax.rsqrt(jnp.mean(values * values, -1, keepdims=True) + EPS) * gain


def norm_back(values, gain, upstream):
    factor = lax.rsqrt(jnp.mean(values * values, -1, keepdims=True) + EPS)
    scaled = gain * upstream
    return factor * scaled - values * factor**3 * jnp.mean(scaled * values, -1, keepdims=True)


def gain_term(values, upstream):
    factor = lax.rsqrt(jnp.mean(values * values, -1, keepdims=True) + EPS)
    return jnp.sum(upstream * values * factor, 0)


def swiglu(gate, upper):
    return jax.nn.silu(gate) * upper


def rope_tables(length, width):
    position = jnp.arange(length).astype(jnp.float32)
    freqs = jnp.exp(jnp.arange(width // 2).astype(jnp.float32) * (-2.0 * math.log(THETA) / width))
    angles = position[:, None] * freqs[None, :]
    cosine = jnp.cos(angles)
    sine = jnp.sin(angles)
    return (jnp.concatenate([cosine, cosine], -1), jnp.concatenate([sine, sine], -1))


def head_prep(values, gain, cosine, sine):
    normed = values * lax.rsqrt(jnp.mean(values * values, -1, keepdims=True) + EPS) * gain
    half = normed.shape[-1] // 2
    turned = jnp.concatenate([-normed[..., half:], normed[..., :half]], -1)
    return normed * cosine[:, None, :] + turned * sine[:, None, :]


def causal_scores(queries, keys_rot, length):
    scores = product("sqgrd,skgd->sgrqk", queries, keys_rot) * (1.0 / math.sqrt(HEAD_SIZE))
    allowed = jnp.arange(length)[:, None] >= jnp.arange(length)[None, :]
    return jnp.where(allowed, scores, -1e30)


def attend(q_raw, k_raw, v_raw, query_gain, key_gain, seqs):
    total = q_raw.shape[0]
    length = total // seqs
    heads = q_raw.shape[1] // HEAD_SIZE
    kv_heads = k_raw.shape[1] // HEAD_SIZE
    repeat = heads // kv_heads
    cosine, sine = rope_tables(length, HEAD_SIZE)
    queries = head_prep(q_raw.reshape(seqs, length, heads, HEAD_SIZE), query_gain, cosine, sine)
    queries = queries.astype(jnp.bfloat16).reshape(seqs, length, kv_heads, repeat, HEAD_SIZE)
    keys_rot = head_prep(
        k_raw.reshape(seqs, length, kv_heads, HEAD_SIZE), key_gain, cosine, sine
    ).astype(jnp.bfloat16)
    values = v_raw.astype(jnp.bfloat16).reshape(seqs, length, kv_heads, HEAD_SIZE)
    scores = causal_scores(queries, keys_rot, length)
    top = jnp.max(scores, -1, keepdims=True)
    logsum = top + jnp.log(jnp.sum(jnp.exp(scores - top), -1, keepdims=True))
    weights = jnp.exp(scores - logsum).astype(jnp.bfloat16)
    attended = (
        product("sgrqk,skgd->sqgrd", weights, values)
        .astype(jnp.bfloat16)
        .reshape(total, heads * HEAD_SIZE)
    )
    return (attended, logsum, queries, keys_rot, values)


def attend_back(
    upstream, q_raw, k_raw, query_gain, key_gain, queries, keys_rot, values, logsum, seqs, hook
):
    total = q_raw.shape[0]
    length = total // seqs
    heads = q_raw.shape[1] // HEAD_SIZE
    kv_heads = k_raw.shape[1] // HEAD_SIZE
    repeat = heads // kv_heads
    cosine, sine = rope_tables(length, HEAD_SIZE)
    grad_out = upstream.reshape(seqs, length, kv_heads, repeat, HEAD_SIZE)
    scores = causal_scores(queries, keys_rot, length)
    probs = jnp.exp(scores - logsum)
    probs = hook(probs)
    value_grad = product("sgrqk,sqgrd->skgd", probs.astype(jnp.bfloat16), grad_out)
    prob_grad = product("sqgrd,skgd->sgrqk", grad_out, values)
    value_grad, prob_grad = hook((value_grad, prob_grad))
    center = jnp.sum(probs * prob_grad, -1, keepdims=True)
    score_grad = (probs * (prob_grad - center) * (1.0 / math.sqrt(HEAD_SIZE))).astype(jnp.bfloat16)
    score_grad = hook(score_grad)
    query_rot_grad = product("sgrqk,skgd->sqgrd", score_grad, keys_rot).reshape(
        seqs, length, heads, HEAD_SIZE
    )
    key_rot_grad = product("sgrqk,sqgrd->skgd", score_grad, queries)
    query_rot_grad, key_rot_grad = hook((query_rot_grad, key_rot_grad))
    query_in = q_raw.reshape(seqs, length, heads, HEAD_SIZE)
    key_in = k_raw.reshape(seqs, length, kv_heads, HEAD_SIZE)
    _, pull_query = jax.vjp(
        lambda inner, gain: head_prep(inner, gain, cosine, sine), query_in, query_gain
    )
    query_grad, query_gain_grad = pull_query(query_rot_grad)
    _, pull_key = jax.vjp(
        lambda inner, gain: head_prep(inner, gain, cosine, sine), key_in, key_gain
    )
    key_grad, key_gain_grad = pull_key(key_rot_grad)
    query_grad, key_grad = hook((query_grad, key_grad))
    return (
        query_grad.astype(jnp.bfloat16).reshape(total, heads * HEAD_SIZE),
        key_grad.astype(jnp.bfloat16).reshape(total, kv_heads * HEAD_SIZE),
        value_grad.astype(jnp.bfloat16).reshape(total, kv_heads * HEAD_SIZE),
        query_gain_grad,
        key_gain_grad,
    )


def snake_ring(coords):
    coords = [tuple(c) for c in coords]
    dims = [d for d in range(len(coords[0])) if len({c[d] for c in coords}) > 1]
    if not dims:
        return list(range(len(coords)))
    values = [sorted({c[d] for c in coords}) for d in dims]
    where = {tuple(c[d] for d in dims): i for i, c in enumerate(coords)}
    best = None
    for perm in itertools.permutations(range(len(dims))):
        def walk(level):
            if level == len(perm):
                return [()]
            inner = walk(level + 1)
            out = []
            for i, value in enumerate(values[perm[level]]):
                seq = inner if i % 2 == 0 else inner[::-1]
                out += [((perm[level], value),) + t for t in seq]
            return out

        order = []
        for path in walk(0):
            key = dict(path)
            point = tuple(key[k] for k in range(len(dims)))
            if point in where:
                order.append(where[point])
        if len(order) != len(coords):
            continue
        cost = sum(
            sum(abs(a - b) for a, b in zip(coords[order[i]], coords[order[(i + 1) % len(order)]]))
            for i in range(len(order))
        )
        if best is None or cost < best[0]:
            best = (cost, order)
    return best[1] if best else list(range(len(coords)))


class Plan:
    def __init__(self, mesh):
        names = mesh.axis_names
        devices = np.asarray(mesh.devices)
        dp_axis, tp_axis = names.index("dp"), names.index("tensor")
        devices = np.transpose(devices, (dp_axis, tp_axis))
        self.n_dp, self.n_tp = devices.shape
        dp_coords = [tuple(devices[d, 0].coords) for d in range(self.n_dp)]
        self.ring = snake_ring(dp_coords)
        self.pos = [self.ring.index(d) for d in range(self.n_dp)]
        n = self.n_dp
        self.cw = [(self.ring[i], self.ring[(i + 1) % n]) for i in range(n)]
        self.ccw = [(b, a) for a, b in self.cw]
        group = [devices[0, t] for t in range(self.n_tp)]
        self.tp_ok = False
        if self.n_tp == 4:
            chip = [tuple(g.coords) for g in group]
            core = [g.core_on_chip for g in group]
            same = [[u for u in range(4) if u != t and chip[u] == chip[t]] for t in range(4)]
            cross = [
                [u for u in range(4) if chip[u] != chip[t] and core[u] == core[t]] for t in range(4)
            ]
            if all(len(s) == 1 for s in same) and all(len(c) == 1 for c in cross):
                self.core_pairs = [(t, same[t][0]) for t in range(4)]
                self.chip_pairs = [(t, cross[t][0]) for t in range(4)]
                self.half_of = [0 if t < same[t][0] else 1 for t in range(4)]
                self.tp_ok = True

    def tp_sum(self, part):
        if not self.tp_ok:
            return lax.psum(part.astype(jnp.float32), "tensor").astype(jnp.bfloat16)
        rows = part.shape[0]
        h = rows // 2
        t = lax.axis_index("tensor")
        half = jnp.array(self.half_of, jnp.int32)[t]
        keep = lax.dynamic_slice_in_dim(part, half * h, h, 0)
        give = lax.dynamic_slice_in_dim(part, (1 - half) * h, h, 0)
        got = lax.ppermute(give, "tensor", self.core_pairs)
        chip_sum = (keep.astype(jnp.float32) + got.astype(jnp.float32)).astype(jnp.bfloat16)
        other = lax.ppermute(chip_sum, "tensor", self.chip_pairs)
        done = (chip_sum.astype(jnp.float32) + other.astype(jnp.float32)).astype(jnp.bfloat16)
        partner = lax.ppermute(done, "tensor", self.core_pairs)
        first = jnp.where(half == 0, done, partner)
        second = jnp.where(half == 0, partner, done)
        return jnp.concatenate([first, second], 0)

    def dp_rs(self, grads):
        ring = Ring(self, grads)
        for _ in range(ring.steps):
            ring.step()
        return ring.result()

    def all_sum(self, x):
        for axis, size in (("tensor", self.n_tp), ("dp", self.n_dp)):
            if size & (size - 1):
                x = lax.psum(x, axis)
                continue
            bit = 1
            while bit < size:
                x = x + lax.ppermute(x, axis, [(i, i ^ bit) for i in range(size)])
                bit *= 2
        return x


class Ring:
    def __init__(self, plan, grads):
        self.plan = plan
        self.n = n = plan.n_dp
        self.me = lax.axis_index("dp")
        self.pos = jnp.array(plan.pos, jnp.int32)[self.me]
        self.order = jnp.array(plan.ring, jnp.int32)
        self.widths = [g.shape[1] for g in grads]
        self.grads = grads
        self.rows = grads[0].shape[0] // n
        self.steps = n - 1
        self.done = 0
        self.state = None

    def piece(self, index, side):
        half = self.rows // 2
        start = index * self.rows + side * half
        parts = [lax.dynamic_slice_in_dim(g, start, half, 0) for g in self.grads]
        return parts[0] if len(parts) == 1 else jnp.concatenate(parts, 1)

    def step(self):
        n, s = self.n, self.done
        own_a = self.piece(self.order[(self.pos - 1 - s) % n], 0)
        own_b = self.piece(self.order[(self.pos + 1 + s) % n], 1)
        if self.state is None:
            send_a, send_b = own_a, own_b
        else:
            send_a, send_b = self.state[0] + own_a, self.state[1] + own_b
        got_a = lax.ppermute(send_a.astype(jnp.bfloat16), "dp", self.plan.cw)
        got_b = lax.ppermute(send_b.astype(jnp.bfloat16), "dp", self.plan.ccw)
        self.state = (got_a.astype(jnp.float32), got_b.astype(jnp.float32))
        self.done += 1

    def result(self):
        acc_a, acc_b = self.state
        total = jnp.concatenate([acc_a + self.piece(self.me, 0), acc_b + self.piece(self.me, 1)], 0)
        out, start = [], 0
        for w in self.widths:
            out.append(total[:, start : start + w])
            start += w
        return out


def make_on_device(plan):
    def body(
        tokens,
        attn_gain,
        w_query,
        key_matrix,
        value_matrix,
        query_gain,
        key_gain,
        w_out,
        mlp_gain,
        w_gate,
        w_up,
        w_down,
        cotangent,
    ):
        count = tokens.shape[0]
        seqs = count // LEN
        share = count // lax.axis_size("tensor")
        offset = lax.axis_index("tensor") * share
        stream = tokens.astype(jnp.float32)
        stream_rows = lax.dynamic_slice_in_dim(stream, offset, share, 0)
        normed_in = rms_scale(stream, attn_gain).astype(jnp.bfloat16)
        q_raw = matmul(normed_in, w_query)
        k_raw = matmul(normed_in, key_matrix)
        v_raw = matmul(normed_in, value_matrix)
        attended, logsum, queries, keys_rot, values = attend(
            q_raw, k_raw, v_raw, query_gain, key_gain, seqs
        )
        attn_part = matmul(attended, w_out).astype(jnp.bfloat16)
        resid = stream + plan.tp_sum(attn_part).astype(jnp.float32)
        resid_rows = lax.dynamic_slice_in_dim(resid, offset, share, 0)
        normed_mid = rms_scale(resid, mlp_gain).astype(jnp.bfloat16)
        gate = matmul(normed_mid, w_gate)
        upper = matmul(normed_mid, w_up)
        hidden = swiglu(gate, upper).astype(jnp.bfloat16)
        down_grad_t = inner_rows(cotangent, hidden)
        down = Ring(plan, [down_grad_t])
        down.step()
        mlp_part = matmul(hidden, w_down).astype(jnp.bfloat16)
        mixed = (resid + plan.tp_sum(mlp_part).astype(jnp.float32)).astype(jnp.bfloat16)

        def down_hook(values):
            if down.done < down.steps:
                down.step()
            down.state, values = lax.optimization_barrier((down.state, values))
            return values

        hidden_grad = down_hook(outer_cols(cotangent, w_down))
        _, pull = jax.vjp(swiglu, gate, upper)
        gate_grad, upper_grad = pull(hidden_grad)
        gate_grad = gate_grad.astype(jnp.bfloat16)
        upper_grad = upper_grad.astype(jnp.bfloat16)
        gate_grad, upper_grad = down_hook((gate_grad, upper_grad))
        mid_part = (outer_cols(gate_grad, w_gate) + outer_cols(upper_grad, w_up)).astype(
            jnp.bfloat16
        )
        mid_part, gate_grad, upper_grad = down_hook((mid_part, gate_grad, upper_grad))
        mid_sum = plan.tp_sum(mid_part)
        gate_w_grad = down_hook(inner_rows(normed_mid, gate_grad))
        up_w_grad = down_hook(inner_rows(normed_mid, upper_grad))
        big = Ring(plan, [gate_w_grad, up_w_grad])
        big.step()
        mid_grad = mid_sum.astype(jnp.float32)
        resid_grad = cotangent.astype(jnp.float32) + norm_back(resid, mlp_gain, mid_grad)
        mlp_gain_part = gain_term(resid_rows, lax.dynamic_slice_in_dim(mid_grad, offset, share, 0))
        resid_low = resid_grad.astype(jnp.bfloat16)
        out_w_grad_t = inner_rows(resid_low, attended)
        attended_grad = outer_cols(resid_low, w_out).astype(jnp.bfloat16)
        small = Ring(plan, [out_w_grad_t])

        def hook(values):
            if big.done < big.steps:
                big.step()
            if small.done < small.steps:
                small.step()
            if down.done < down.steps:
                down.step()
            down.state, big.state, small.state, values = lax.optimization_barrier(
                (down.state, big.state, small.state, values)
            )
            return values

        resid_grad, attended_grad = hook((resid_grad, attended_grad))
        q_grad, k_grad, v_grad, qg_part, kg_part = attend_back(
            attended_grad,
            q_raw,
            k_raw,
            query_gain,
            key_gain,
            queries,
            keys_rot,
            values,
            logsum,
            seqs,
            hook,
        )
        in_part = (
            outer_cols(q_grad, w_query)
            + outer_cols(k_grad, key_matrix)
            + outer_cols(v_grad, value_matrix)
        ).astype(jnp.bfloat16)
        in_part, q_grad, k_grad, v_grad = lax.optimization_barrier(
            (in_part, q_grad, k_grad, v_grad)
        )
        in_sum = plan.tp_sum(in_part)
        query_w_grad = inner_rows(normed_in, q_grad)
        key_w_grad = inner_rows(normed_in, k_grad)
        value_w_grad = inner_rows(normed_in, v_grad)
        while big.done < big.steps:
            big.step()
        while small.done < small.steps:
            small.step()
        while down.done < down.steps:
            down.step()
        in_grad = in_sum.astype(jnp.float32)
        (down_sum,) = down.result()
        gate_sum, up_sum = big.result()
        (out_sum,) = small.result()
        query_sum, key_sum, value_sum = plan.dp_rs([query_w_grad, key_w_grad, value_w_grad])
        input_grad = resid_grad + norm_back(stream, attn_gain, in_grad)
        attn_gain_part = gain_term(stream_rows, lax.dynamic_slice_in_dim(in_grad, offset, share, 0))
        gains = plan.all_sum(jnp.concatenate([attn_gain_part, mlp_gain_part, qg_part, kg_part]))
        width = attn_gain_part.shape[0]
        head = qg_part.shape[0]
        attn_gain_grad = gains[:width]
        mlp_gain_grad = gains[width : 2 * width]
        query_gain_grad = gains[2 * width : 2 * width + head]
        key_gain_grad = gains[2 * width + head :]
        return (
            mixed,
            input_grad,
            attn_gain_grad,
            mlp_gain_grad,
            query_gain_grad,
            key_gain_grad,
            query_sum,
            key_sum,
            value_sum,
            out_sum.T,
            gate_sum,
            up_sum,
            down_sum.T,
        )

    return body


def solution(mesh):
    plan = Plan(mesh)
    placed = (
        P("dp", None),
        P(),
        P(None, "tensor"),
        P(None, "tensor"),
        P(None, "tensor"),
        P(),
        P(),
        P("tensor", None),
        P(),
        P(None, "tensor"),
        P(None, "tensor"),
        P("tensor", None),
        P("dp", None),
    )
    return jax.shard_map(
        make_on_device(plan),
        mesh=mesh,
        in_specs=placed,
        out_specs=(
            P("dp", None),
            P("dp", None),
            P(),
            P(),
            P(),
            P(),
            P("dp", "tensor"),
            P("dp", "tensor"),
            P("dp", "tensor"),
            P("tensor", "dp"),
            P("dp", "tensor"),
            P("dp", "tensor"),
            P("tensor", "dp"),
        ),
        check_vma=False,
    )
```

```python
import itertools
import math

import jax
import jax.numpy as jnp
import numpy as np
from jax import lax
from jax.sharding import PartitionSpec as P

HEAD_SIZE = 128
LEN = 128


EPS = 1e-06
THETA = 1000000.0


def product(form, left, right):
    return jnp.einsum(form, left, right, preferred_element_type=jnp.float32)


def matmul(left, right):
    return jnp.dot(left, right, preferred_element_type=jnp.float32)


def inner_rows(left, right):
    return lax.dot_general(
        left, right, (((0,), (0,)), ((), ())), preferred_element_type=jnp.float32
    )


def outer_cols(left, right):
    return lax.dot_general(
        left, right, (((1,), (1,)), ((), ())), preferred_element_type=jnp.float32
    )


def rms_scale(values, gain):
    return values * lax.rsqrt(jnp.mean(values * values, -1, keepdims=True) + EPS) * gain


def norm_back(values, gain, upstream):
    factor = lax.rsqrt(jnp.mean(values * values, -1, keepdims=True) + EPS)
    scaled = gain * upstream
    return factor * scaled - values * factor**3 * jnp.mean(scaled * values, -1, keepdims=True)


def gain_term(values, upstream):
    factor = lax.rsqrt(jnp.mean(values * values, -1, keepdims=True) + EPS)
    return jnp.sum(upstream * values * factor, 0)


def swiglu(gate, upper):
    return jax.nn.silu(gate) * upper


def rope_tables(length, width):
    position = jnp.arange(length).astype(jnp.float32)
    freqs = jnp.exp(jnp.arange(width // 2).astype(jnp.float32) * (-2.0 * math.log(THETA) / width))
    angles = position[:, None] * freqs[None, :]
    cosine = jnp.cos(angles)
    sine = jnp.sin(angles)
    return (jnp.concatenate([cosine, cosine], -1), jnp.concatenate([sine, sine], -1))


def head_prep(values, gain, cosine, sine):
    normed = values * lax.rsqrt(jnp.mean(values * values, -1, keepdims=True) + EPS) * gain
    half = normed.shape[-1] // 2
    turned = jnp.concatenate([-normed[..., half:], normed[..., :half]], -1)
    return normed * cosine[:, None, :] + turned * sine[:, None, :]


def causal_scores(queries, keys_rot, length):
    scores = product("sqgrd,skgd->sgrqk", queries, keys_rot) * (1.0 / math.sqrt(HEAD_SIZE))
    allowed = jnp.arange(length)[:, None] >= jnp.arange(length)[None, :]
    return jnp.where(allowed, scores, -1e30)


def attend(q_raw, k_raw, v_raw, query_gain, key_gain, seqs):
    total = q_raw.shape[0]
    length = total // seqs
    heads = q_raw.shape[1] // HEAD_SIZE
    kv_heads = k_raw.shape[1] // HEAD_SIZE
    repeat = heads // kv_heads
    cosine, sine = rope_tables(length, HEAD_SIZE)
    queries = head_prep(q_raw.reshape(seqs, length, heads, HEAD_SIZE), query_gain, cosine, sine)
    queries = queries.astype(jnp.bfloat16).reshape(seqs, length, kv_heads, repeat, HEAD_SIZE)
    keys_rot = head_prep(
        k_raw.reshape(seqs, length, kv_heads, HEAD_SIZE), key_gain, cosine, sine
    ).astype(jnp.bfloat16)
    values = v_raw.astype(jnp.bfloat16).reshape(seqs, length, kv_heads, HEAD_SIZE)
    scores = causal_scores(queries, keys_rot, length)
    top = jnp.max(scores, -1, keepdims=True)
    logsum = top + jnp.log(jnp.sum(jnp.exp(scores - top), -1, keepdims=True))
    weights = jnp.exp(scores - logsum).astype(jnp.bfloat16)
    attended = (
        product("sgrqk,skgd->sqgrd", weights, values)
        .astype(jnp.bfloat16)
        .reshape(total, heads * HEAD_SIZE)
    )
    return (attended, logsum, queries, keys_rot, values)


def attend_back(
    upstream, q_raw, k_raw, query_gain, key_gain, queries, keys_rot, values, logsum, seqs, hook
):
    total = q_raw.shape[0]
    length = total // seqs
    heads = q_raw.shape[1] // HEAD_SIZE
    kv_heads = k_raw.shape[1] // HEAD_SIZE
    repeat = heads // kv_heads
    cosine, sine = rope_tables(length, HEAD_SIZE)
    grad_out = upstream.reshape(seqs, length, kv_heads, repeat, HEAD_SIZE)
    scores = causal_scores(queries, keys_rot, length)
    probs = jnp.exp(scores - logsum)
    probs = hook(probs)
    value_grad = product("sgrqk,sqgrd->skgd", probs.astype(jnp.bfloat16), grad_out)
    prob_grad = product("sqgrd,skgd->sgrqk", grad_out, values)
    value_grad, prob_grad = hook((value_grad, prob_grad))
    center = jnp.sum(probs * prob_grad, -1, keepdims=True)
    score_grad = (probs * (prob_grad - center) * (1.0 / math.sqrt(HEAD_SIZE))).astype(jnp.bfloat16)
    score_grad = hook(score_grad)
    query_rot_grad = product("sgrqk,skgd->sqgrd", score_grad, keys_rot).reshape(
        seqs, length, heads, HEAD_SIZE
    )
    key_rot_grad = product("sgrqk,sqgrd->skgd", score_grad, queries)
    query_rot_grad, key_rot_grad = hook((query_rot_grad, key_rot_grad))
    query_in = q_raw.reshape(seqs, length, heads, HEAD_SIZE)
    key_in = k_raw.reshape(seqs, length, kv_heads, HEAD_SIZE)
    _, pull_query = jax.vjp(
        lambda inner, gain: head_prep(inner, gain, cosine, sine), query_in, query_gain
    )
    query_grad, query_gain_grad = pull_query(query_rot_grad)
    _, pull_key = jax.vjp(
        lambda inner, gain: head_prep(inner, gain, cosine, sine), key_in, key_gain
    )
    key_grad, key_gain_grad = pull_key(key_rot_grad)
    query_grad, key_grad = hook((query_grad, key_grad))
    return (
        query_grad.astype(jnp.bfloat16).reshape(total, heads * HEAD_SIZE),
        key_grad.astype(jnp.bfloat16).reshape(total, kv_heads * HEAD_SIZE),
        value_grad.astype(jnp.bfloat16).reshape(total, kv_heads * HEAD_SIZE),
        query_gain_grad,
        key_gain_grad,
    )


def snake_ring(coords):
    coords = [tuple(c) for c in coords]
    dims = [d for d in range(len(coords[0])) if len({c[d] for c in coords}) > 1]
    if not dims:
        return list(range(len(coords)))
    values = [sorted({c[d] for c in coords}) for d in dims]
    where = {tuple(c[d] for d in dims): i for i, c in enumerate(coords)}
    best = None
    for perm in itertools.permutations(range(len(dims))):
        def walk(level):
            if level == len(perm):
                return [()]
            inner = walk(level + 1)
            out = []
            for i, value in enumerate(values[perm[level]]):
                seq = inner if i % 2 == 0 else inner[::-1]
                out += [((perm[level], value),) + t for t in seq]
            return out

        order = []
        for path in walk(0):
            key = dict(path)
            point = tuple(key[k] for k in range(len(dims)))
            if point in where:
                order.append(where[point])
        if len(order) != len(coords):
            continue
        cost = sum(
            sum(abs(a - b) for a, b in zip(coords[order[i]], coords[order[(i + 1) % len(order)]]))
            for i in range(len(order))
        )
        if best is None or cost < best[0]:
            best = (cost, order)
    return best[1] if best else list(range(len(coords)))


class Plan:
    def __init__(self, mesh):
        names = mesh.axis_names
        devices = np.asarray(mesh.devices)
        dp_axis, tp_axis = names.index("dp"), names.index("tensor")
        devices = np.transpose(devices, (dp_axis, tp_axis))
        self.n_dp, self.n_tp = devices.shape
        dp_coords = [tuple(devices[d, 0].coords) for d in range(self.n_dp)]
        self.ring = snake_ring(dp_coords)
        self.pos = [self.ring.index(d) for d in range(self.n_dp)]
        n = self.n_dp
        self.cw = [(self.ring[i], self.ring[(i + 1) % n]) for i in range(n)]
        self.ccw = [(b, a) for a, b in self.cw]
        group = [devices[0, t] for t in range(self.n_tp)]
        self.tp_ok = False
        if self.n_tp == 4:
            chip = [tuple(g.coords) for g in group]
            core = [g.core_on_chip for g in group]
            same = [[u for u in range(4) if u != t and chip[u] == chip[t]] for t in range(4)]
            cross = [
                [u for u in range(4) if chip[u] != chip[t] and core[u] == core[t]] for t in range(4)
            ]
            if all(len(s) == 1 for s in same) and all(len(c) == 1 for c in cross):
                self.core_pairs = [(t, same[t][0]) for t in range(4)]
                self.chip_pairs = [(t, cross[t][0]) for t in range(4)]
                self.half_of = [0 if t < same[t][0] else 1 for t in range(4)]
                self.tp_ok = True

    def tp_sum(self, part):
        if not self.tp_ok:
            return lax.psum(part.astype(jnp.float32), "tensor").astype(jnp.bfloat16)
        rows = part.shape[0]
        h = rows // 2
        t = lax.axis_index("tensor")
        half = jnp.array(self.half_of, jnp.int32)[t]
        keep = lax.dynamic_slice_in_dim(part, half * h, h, 0)
        give = lax.dynamic_slice_in_dim(part, (1 - half) * h, h, 0)
        got = lax.ppermute(give, "tensor", self.core_pairs)
        chip_sum = (keep.astype(jnp.float32) + got.astype(jnp.float32)).astype(jnp.bfloat16)
        other = lax.ppermute(chip_sum, "tensor", self.chip_pairs)
        done = (chip_sum.astype(jnp.float32) + other.astype(jnp.float32)).astype(jnp.bfloat16)
        partner = lax.ppermute(done, "tensor", self.core_pairs)
        first = jnp.where(half == 0, done, partner)
        second = jnp.where(half == 0, partner, done)
        return jnp.concatenate([first, second], 0)

    def dp_rs(self, grads):
        ring = Ring(self, grads)
        for _ in range(ring.steps):
            ring.step()
        return ring.result()

    def all_sum(self, x):
        for axis, size in (("tensor", self.n_tp), ("dp", self.n_dp)):
            if size & (size - 1):
                x = lax.psum(x, axis)
                continue
            bit = 1
            while bit < size:
                x = x + lax.ppermute(x, axis, [(i, i ^ bit) for i in range(size)])
                bit *= 2
        return x


class Ring:
    def __init__(self, plan, grads):
        self.plan = plan
        self.n = n = plan.n_dp
        self.me = lax.axis_index("dp")
        self.pos = jnp.array(plan.pos, jnp.int32)[self.me]
        self.order = jnp.array(plan.ring, jnp.int32)
        self.widths = [g.shape[1] for g in grads]
        self.grads = grads
        self.rows = grads[0].shape[0] // n
        self.steps = n - 1
        self.done = 0
        self.state = None

    def piece(self, index, side):
        half = self.rows // 2
        start = index * self.rows + side * half
        parts = [lax.dynamic_slice_in_dim(g, start, half, 0) for g in self.grads]
        return parts[0] if len(parts) == 1 else jnp.concatenate(parts, 1)

    def step(self):
        n, s = self.n, self.done
        own_a = self.piece(self.order[(self.pos - 1 - s) % n], 0)
        own_b = self.piece(self.order[(self.pos + 1 + s) % n], 1)
        if self.state is None:
            send_a, send_b = own_a, own_b
        else:
            send_a, send_b = self.state[0] + own_a, self.state[1] + own_b
        got_a = lax.ppermute(send_a.astype(jnp.bfloat16), "dp", self.plan.cw)
        got_b = lax.ppermute(send_b.astype(jnp.bfloat16), "dp", self.plan.ccw)
        self.state = (got_a.astype(jnp.float32), got_b.astype(jnp.float32))
        self.done += 1

    def result(self):
        acc_a, acc_b = self.state
        total = jnp.concatenate([acc_a + self.piece(self.me, 0), acc_b + self.piece(self.me, 1)], 0)
        out, start = [], 0
        for w in self.widths:
            out.append(total[:, start : start + w])
            start += w
        return out


def make_on_device(plan):
    def body(
        tokens,
        attn_gain,
        w_query,
        key_matrix,
        value_matrix,
        query_gain,
        key_gain,
        w_out,
        mlp_gain,
        w_gate,
        w_up,
        w_down,
        cotangent,
    ):
        count = tokens.shape[0]
        seqs = count // LEN
        share = count // lax.axis_size("tensor")
        offset = lax.axis_index("tensor") * share
        stream = tokens.astype(jnp.float32)
        stream_rows = lax.dynamic_slice_in_dim(stream, offset, share, 0)
        normed_in = rms_scale(stream, attn_gain).astype(jnp.bfloat16)
        q_raw = matmul(normed_in, w_query)
        k_raw = matmul(normed_in, key_matrix)
        v_raw = matmul(normed_in, value_matrix)
        halves = 2 if seqs % 2 == 0 else 1
        rows = count // halves
        outs = []
        for c in range(halves):
            span = slice(c * rows, (c + 1) * rows)
            att_c, logsum_c, queries_c, keys_c, values_c = attend(
                q_raw[span], k_raw[span], v_raw[span], query_gain, key_gain, seqs // halves
            )
            attn_part = matmul(att_c, w_out).astype(jnp.bfloat16)
            resid_c = stream[span] + plan.tp_sum(attn_part).astype(jnp.float32)
            normed_mid_c = rms_scale(resid_c, mlp_gain).astype(jnp.bfloat16)
            gate_c = matmul(normed_mid_c, w_gate)
            upper_c = matmul(normed_mid_c, w_up)
            hidden_c = swiglu(gate_c, upper_c).astype(jnp.bfloat16)
            mlp_part = matmul(hidden_c, w_down).astype(jnp.bfloat16)
            mlp_sum_c = plan.tp_sum(mlp_part)
            outs.append(
                (att_c, logsum_c, queries_c, keys_c, values_c, resid_c, normed_mid_c, gate_c,
                 upper_c, hidden_c, mlp_sum_c)
            )
        joined = [jnp.concatenate(parts, 0) for parts in zip(*outs)]
        (attended, logsum, queries, keys_rot, values, resid, normed_mid, gate, upper, hidden,
         mlp_sum) = joined
        resid_rows = lax.dynamic_slice_in_dim(resid, offset, share, 0)
        down_grad_t = inner_rows(cotangent, hidden)
        down = Ring(plan, [down_grad_t])
        down.step()

        def down_hook(values):
            if down.done < down.steps:
                down.step()
            down.state, values = lax.optimization_barrier((down.state, values))
            return values

        hidden_grad = down_hook(outer_cols(cotangent, w_down))
        _, pull = jax.vjp(swiglu, gate, upper)
        gate_grad, upper_grad = pull(hidden_grad)
        gate_grad = gate_grad.astype(jnp.bfloat16)
        upper_grad = upper_grad.astype(jnp.bfloat16)
        gate_grad, upper_grad, mlp_sum = down_hook((gate_grad, upper_grad, mlp_sum))
        mixed = (resid + mlp_sum.astype(jnp.float32)).astype(jnp.bfloat16)
        mid_part = (outer_cols(gate_grad, w_gate) + outer_cols(upper_grad, w_up)).astype(
            jnp.bfloat16
        )
        mid_part, gate_grad, upper_grad = down_hook((mid_part, gate_grad, upper_grad))
        mid_sum = plan.tp_sum(mid_part)
        gate_w_grad = down_hook(inner_rows(normed_mid, gate_grad))
        up_w_grad = down_hook(inner_rows(normed_mid, upper_grad))
        big = Ring(plan, [gate_w_grad, up_w_grad])
        big.step()
        mid_grad = mid_sum.astype(jnp.float32)
        resid_grad = cotangent.astype(jnp.float32) + norm_back(resid, mlp_gain, mid_grad)
        mlp_gain_part = gain_term(resid_rows, lax.dynamic_slice_in_dim(mid_grad, offset, share, 0))
        resid_low = resid_grad.astype(jnp.bfloat16)
        out_w_grad_t = inner_rows(resid_low, attended)
        attended_grad = outer_cols(resid_low, w_out).astype(jnp.bfloat16)
        small = Ring(plan, [out_w_grad_t])

        def hook(values):
            if big.done < big.steps:
                big.step()
            if small.done < small.steps:
                small.step()
            if down.done < down.steps:
                down.step()
            down.state, big.state, small.state, values = lax.optimization_barrier(
                (down.state, big.state, small.state, values)
            )
            return values

        resid_grad, attended_grad = hook((resid_grad, attended_grad))
        q_grad, k_grad, v_grad, qg_part, kg_part = attend_back(
            attended_grad,
            q_raw,
            k_raw,
            query_gain,
            key_gain,
            queries,
            keys_rot,
            values,
            logsum,
            seqs,
            hook,
        )
        in_part = (
            outer_cols(q_grad, w_query)
            + outer_cols(k_grad, key_matrix)
            + outer_cols(v_grad, value_matrix)
        ).astype(jnp.bfloat16)
        in_part, q_grad, k_grad, v_grad = lax.optimization_barrier(
            (in_part, q_grad, k_grad, v_grad)
        )
        in_sum = plan.tp_sum(in_part)
        query_w_grad = inner_rows(normed_in, q_grad)
        key_w_grad = inner_rows(normed_in, k_grad)
        value_w_grad = inner_rows(normed_in, v_grad)
        while big.done < big.steps:
            big.step()
        while small.done < small.steps:
            small.step()
        while down.done < down.steps:
            down.step()
        in_grad = in_sum.astype(jnp.float32)
        (down_sum,) = down.result()
        gate_sum, up_sum = big.result()
        (out_sum,) = small.result()
        query_sum, key_sum, value_sum = plan.dp_rs([query_w_grad, key_w_grad, value_w_grad])
        input_grad = resid_grad + norm_back(stream, attn_gain, in_grad)
        attn_gain_part = gain_term(stream_rows, lax.dynamic_slice_in_dim(in_grad, offset, share, 0))
        gains = plan.all_sum(jnp.concatenate([attn_gain_part, mlp_gain_part, qg_part, kg_part]))
        width = attn_gain_part.shape[0]
        head = qg_part.shape[0]
        attn_gain_grad = gains[:width]
        mlp_gain_grad = gains[width : 2 * width]
        query_gain_grad = gains[2 * width : 2 * width + head]
        key_gain_grad = gains[2 * width + head :]
        return (
            mixed,
            input_grad,
            attn_gain_grad,
            mlp_gain_grad,
            query_gain_grad,
            key_gain_grad,
            query_sum,
            key_sum,
            value_sum,
            out_sum.T,
            gate_sum,
            up_sum,
            down_sum.T,
        )

    return body


def solution(mesh):
    plan = Plan(mesh)
    placed = (
        P("dp", None),
        P(),
        P(None, "tensor"),
        P(None, "tensor"),
        P(None, "tensor"),
        P(),
        P(),
        P("tensor", None),
        P(),
        P(None, "tensor"),
        P(None, "tensor"),
        P("tensor", None),
        P("dp", None),
    )
    return jax.shard_map(
        make_on_device(plan),
        mesh=mesh,
        in_specs=placed,
        out_specs=(
            P("dp", None),
            P("dp", None),
            P(),
            P(),
            P(),
            P(),
            P("dp", "tensor"),
            P("dp", "tensor"),
            P("dp", "tensor"),
            P("tensor", "dp"),
            P("dp", "tensor"),
            P("dp", "tensor"),
            P("tensor", "dp"),
        ),
        check_vma=False,
    )
```

```python
import itertools
import math

import jax
import jax.numpy as jnp
import numpy as np
from jax import lax
from jax.sharding import PartitionSpec as P

HEAD_SIZE = 128
LEN = 128


EPS = 1e-06
THETA = 1000000.0


def product(form, left, right):
    return jnp.einsum(form, left, right, preferred_element_type=jnp.float32)


def matmul(left, right):
    return jnp.dot(left, right, preferred_element_type=jnp.float32)


def inner_rows(left, right):
    return lax.dot_general(
        left, right, (((0,), (0,)), ((), ())), preferred_element_type=jnp.float32
    )


def outer_cols(left, right):
    return lax.dot_general(
        left, right, (((1,), (1,)), ((), ())), preferred_element_type=jnp.float32
    )


def rms_scale(values, gain):
    return values * lax.rsqrt(jnp.mean(values * values, -1, keepdims=True) + EPS) * gain


def norm_back(values, gain, upstream):
    factor = lax.rsqrt(jnp.mean(values * values, -1, keepdims=True) + EPS)
    scaled = gain * upstream
    return factor * scaled - values * factor**3 * jnp.mean(scaled * values, -1, keepdims=True)


def gain_term(values, upstream):
    factor = lax.rsqrt(jnp.mean(values * values, -1, keepdims=True) + EPS)
    return jnp.sum(upstream * values * factor, 0)


def swiglu(gate, upper):
    return jax.nn.silu(gate) * upper


def rope_tables(length, width):
    position = jnp.arange(length).astype(jnp.float32)
    freqs = jnp.exp(jnp.arange(width // 2).astype(jnp.float32) * (-2.0 * math.log(THETA) / width))
    angles = position[:, None] * freqs[None, :]
    cosine = jnp.cos(angles)
    sine = jnp.sin(angles)
    return (jnp.concatenate([cosine, cosine], -1), jnp.concatenate([sine, sine], -1))


def head_prep(values, gain, cosine, sine):
    normed = values * lax.rsqrt(jnp.mean(values * values, -1, keepdims=True) + EPS) * gain
    half = normed.shape[-1] // 2
    turned = jnp.concatenate([-normed[..., half:], normed[..., :half]], -1)
    return normed * cosine[:, None, :] + turned * sine[:, None, :]


def causal_scores(queries, keys_rot, length):
    scores = product("sqgrd,skgd->sgrqk", queries, keys_rot) * (1.0 / math.sqrt(HEAD_SIZE))
    allowed = jnp.arange(length)[:, None] >= jnp.arange(length)[None, :]
    return jnp.where(allowed, scores, -1e30)


def attend(q_raw, k_raw, v_raw, query_gain, key_gain, seqs):
    total = q_raw.shape[0]
    length = total // seqs
    heads = q_raw.shape[1] // HEAD_SIZE
    kv_heads = k_raw.shape[1] // HEAD_SIZE
    repeat = heads // kv_heads
    cosine, sine = rope_tables(length, HEAD_SIZE)
    queries = head_prep(q_raw.reshape(seqs, length, heads, HEAD_SIZE), query_gain, cosine, sine)
    queries = queries.astype(jnp.bfloat16).reshape(seqs, length, kv_heads, repeat, HEAD_SIZE)
    keys_rot = head_prep(
        k_raw.reshape(seqs, length, kv_heads, HEAD_SIZE), key_gain, cosine, sine
    ).astype(jnp.bfloat16)
    values = v_raw.astype(jnp.bfloat16).reshape(seqs, length, kv_heads, HEAD_SIZE)
    scores = causal_scores(queries, keys_rot, length)
    top = jnp.max(scores, -1, keepdims=True)
    logsum = top + jnp.log(jnp.sum(jnp.exp(scores - top), -1, keepdims=True))
    weights = jnp.exp(scores - logsum).astype(jnp.bfloat16)
    attended = (
        product("sgrqk,skgd->sqgrd", weights, values)
        .astype(jnp.bfloat16)
        .reshape(total, heads * HEAD_SIZE)
    )
    return (attended, logsum, queries, keys_rot, values)


def attend_back(
    upstream, q_raw, k_raw, query_gain, key_gain, queries, keys_rot, values, logsum, seqs, hook
):
    total = q_raw.shape[0]
    length = total // seqs
    heads = q_raw.shape[1] // HEAD_SIZE
    kv_heads = k_raw.shape[1] // HEAD_SIZE
    repeat = heads // kv_heads
    cosine, sine = rope_tables(length, HEAD_SIZE)
    grad_out = upstream.reshape(seqs, length, kv_heads, repeat, HEAD_SIZE)
    scores = causal_scores(queries, keys_rot, length)
    probs = jnp.exp(scores - logsum)
    probs = hook(probs)
    value_grad = product("sgrqk,sqgrd->skgd", probs.astype(jnp.bfloat16), grad_out)
    prob_grad = product("sqgrd,skgd->sgrqk", grad_out, values)
    value_grad, prob_grad = hook((value_grad, prob_grad))
    center = jnp.sum(probs * prob_grad, -1, keepdims=True)
    score_grad = (probs * (prob_grad - center) * (1.0 / math.sqrt(HEAD_SIZE))).astype(jnp.bfloat16)
    score_grad = hook(score_grad)
    query_rot_grad = product("sgrqk,skgd->sqgrd", score_grad, keys_rot).reshape(
        seqs, length, heads, HEAD_SIZE
    )
    key_rot_grad = product("sgrqk,sqgrd->skgd", score_grad, queries)
    query_rot_grad, key_rot_grad = hook((query_rot_grad, key_rot_grad))
    query_in = q_raw.reshape(seqs, length, heads, HEAD_SIZE)
    key_in = k_raw.reshape(seqs, length, kv_heads, HEAD_SIZE)
    _, pull_query = jax.vjp(
        lambda inner, gain: head_prep(inner, gain, cosine, sine), query_in, query_gain
    )
    query_grad, query_gain_grad = pull_query(query_rot_grad)
    _, pull_key = jax.vjp(
        lambda inner, gain: head_prep(inner, gain, cosine, sine), key_in, key_gain
    )
    key_grad, key_gain_grad = pull_key(key_rot_grad)
    query_grad, key_grad = hook((query_grad, key_grad))
    return (
        query_grad.astype(jnp.bfloat16).reshape(total, heads * HEAD_SIZE),
        key_grad.astype(jnp.bfloat16).reshape(total, kv_heads * HEAD_SIZE),
        value_grad.astype(jnp.bfloat16).reshape(total, kv_heads * HEAD_SIZE),
        query_gain_grad,
        key_gain_grad,
    )


def snake_ring(coords):
    coords = [tuple(c) for c in coords]
    dims = [d for d in range(len(coords[0])) if len({c[d] for c in coords}) > 1]
    if not dims:
        return list(range(len(coords)))
    values = [sorted({c[d] for c in coords}) for d in dims]
    where = {tuple(c[d] for d in dims): i for i, c in enumerate(coords)}
    best = None
    for perm in itertools.permutations(range(len(dims))):
        def walk(level):
            if level == len(perm):
                return [()]
            inner = walk(level + 1)
            out = []
            for i, value in enumerate(values[perm[level]]):
                seq = inner if i % 2 == 0 else inner[::-1]
                out += [((perm[level], value),) + t for t in seq]
            return out

        order = []
        for path in walk(0):
            key = dict(path)
            point = tuple(key[k] for k in range(len(dims)))
            if point in where:
                order.append(where[point])
        if len(order) != len(coords):
            continue
        cost = sum(
            sum(abs(a - b) for a, b in zip(coords[order[i]], coords[order[(i + 1) % len(order)]]))
            for i in range(len(order))
        )
        if best is None or cost < best[0]:
            best = (cost, order)
    return best[1] if best else list(range(len(coords)))


class Plan:
    def __init__(self, mesh):
        names = mesh.axis_names
        devices = np.asarray(mesh.devices)
        dp_axis, tp_axis = names.index("dp"), names.index("tensor")
        devices = np.transpose(devices, (dp_axis, tp_axis))
        self.n_dp, self.n_tp = devices.shape
        dp_coords = [tuple(devices[d, 0].coords) for d in range(self.n_dp)]
        self.ring = snake_ring(dp_coords)
        self.pos = [self.ring.index(d) for d in range(self.n_dp)]
        n = self.n_dp
        self.cw = [(self.ring[i], self.ring[(i + 1) % n]) for i in range(n)]
        self.ccw = [(b, a) for a, b in self.cw]
        group = [devices[0, t] for t in range(self.n_tp)]
        self.tp_ok = False
        if self.n_tp == 4:
            chip = [tuple(g.coords) for g in group]
            core = [g.core_on_chip for g in group]
            same = [[u for u in range(4) if u != t and chip[u] == chip[t]] for t in range(4)]
            cross = [
                [u for u in range(4) if chip[u] != chip[t] and core[u] == core[t]] for t in range(4)
            ]
            if all(len(s) == 1 for s in same) and all(len(c) == 1 for c in cross):
                self.core_pairs = [(t, same[t][0]) for t in range(4)]
                self.chip_pairs = [(t, cross[t][0]) for t in range(4)]
                self.half_of = [0 if t < same[t][0] else 1 for t in range(4)]
                self.tp_ok = True

    def tp_sum(self, part, ties=()):
        if not self.tp_ok:
            return lax.psum(part.astype(jnp.float32), "tensor").astype(jnp.bfloat16)
        ties = list(ties) + [lambda x: x] * (2 - len(ties))
        rows = part.shape[0]
        h = rows // 2
        t = lax.axis_index("tensor")
        half = jnp.array(self.half_of, jnp.int32)[t]
        keep = lax.dynamic_slice_in_dim(part, half * h, h, 0)
        give = lax.dynamic_slice_in_dim(part, (1 - half) * h, h, 0)
        got = ties[0](lax.ppermute(give, "tensor", self.core_pairs))
        chip_sum = (keep.astype(jnp.float32) + got.astype(jnp.float32)).astype(jnp.bfloat16)
        other = ties[1](lax.ppermute(chip_sum, "tensor", self.chip_pairs))
        done = (chip_sum.astype(jnp.float32) + other.astype(jnp.float32)).astype(jnp.bfloat16)
        partner = lax.ppermute(done, "tensor", self.core_pairs)
        first = jnp.where(half == 0, done, partner)
        second = jnp.where(half == 0, partner, done)
        return jnp.concatenate([first, second], 0)

    def dp_rs(self, grads):
        ring = Ring(self, grads)
        for _ in range(ring.steps):
            ring.step()
        return ring.result()

    def all_sum(self, x):
        for axis, size in (("tensor", self.n_tp), ("dp", self.n_dp)):
            if size & (size - 1):
                x = lax.psum(x, axis)
                continue
            bit = 1
            while bit < size:
                x = x + lax.ppermute(x, axis, [(i, i ^ bit) for i in range(size)])
                bit *= 2
        return x


class Ring:
    def __init__(self, plan, grads):
        self.plan = plan
        self.n = n = plan.n_dp
        self.me = lax.axis_index("dp")
        self.pos = jnp.array(plan.pos, jnp.int32)[self.me]
        self.order = jnp.array(plan.ring, jnp.int32)
        self.widths = [g.shape[1] for g in grads]
        self.grads = grads
        self.rows = grads[0].shape[0] // n
        self.steps = n - 1
        self.done = 0
        self.state = None

    def piece(self, index, side):
        half = self.rows // 2
        start = index * self.rows + side * half
        parts = [lax.dynamic_slice_in_dim(g, start, half, 0) for g in self.grads]
        return parts[0] if len(parts) == 1 else jnp.concatenate(parts, 1)

    def step(self):
        n, s = self.n, self.done
        own_a = self.piece(self.order[(self.pos - 1 - s) % n], 0)
        own_b = self.piece(self.order[(self.pos + 1 + s) % n], 1)
        if self.state is None:
            send_a, send_b = own_a, own_b
        else:
            send_a, send_b = self.state[0] + own_a, self.state[1] + own_b
        got_a = lax.ppermute(send_a.astype(jnp.bfloat16), "dp", self.plan.cw)
        got_b = lax.ppermute(send_b.astype(jnp.bfloat16), "dp", self.plan.ccw)
        self.state = (got_a.astype(jnp.float32), got_b.astype(jnp.float32))
        self.done += 1

    def result(self):
        acc_a, acc_b = self.state
        total = jnp.concatenate([acc_a + self.piece(self.me, 0), acc_b + self.piece(self.me, 1)], 0)
        out, start = [], 0
        for w in self.widths:
            out.append(total[:, start : start + w])
            start += w
        return out


def make_on_device(plan):
    def body(
        tokens,
        attn_gain,
        w_query,
        key_matrix,
        value_matrix,
        query_gain,
        key_gain,
        w_out,
        mlp_gain,
        w_gate,
        w_up,
        w_down,
        cotangent,
    ):
        count = tokens.shape[0]
        seqs = count // LEN
        share = count // lax.axis_size("tensor")
        offset = lax.axis_index("tensor") * share
        stream = tokens.astype(jnp.float32)
        stream_rows = lax.dynamic_slice_in_dim(stream, offset, share, 0)
        normed_in = rms_scale(stream, attn_gain).astype(jnp.bfloat16)
        q_raw = matmul(normed_in, w_query)
        k_raw = matmul(normed_in, key_matrix)
        v_raw = matmul(normed_in, value_matrix)
        attended, logsum, queries, keys_rot, values = attend(
            q_raw, k_raw, v_raw, query_gain, key_gain, seqs
        )
        attn_part = matmul(attended, w_out).astype(jnp.bfloat16)
        resid = stream + plan.tp_sum(attn_part).astype(jnp.float32)
        resid_rows = lax.dynamic_slice_in_dim(resid, offset, share, 0)
        normed_mid = rms_scale(resid, mlp_gain).astype(jnp.bfloat16)
        gate = matmul(normed_mid, w_gate)
        upper = matmul(normed_mid, w_up)
        hidden = swiglu(gate, upper).astype(jnp.bfloat16)
        down_grad_t = inner_rows(cotangent, hidden)
        down = Ring(plan, [down_grad_t])
        down.step()
        mlp_part = matmul(hidden, w_down).astype(jnp.bfloat16)
        mlp_sum = plan.tp_sum(mlp_part)

        def down_hook(values):
            if down.done < down.steps:
                down.step()
            down.state, values = lax.optimization_barrier((down.state, values))
            return values

        hidden_grad = down_hook(outer_cols(cotangent, w_down))
        _, pull = jax.vjp(swiglu, gate, upper)
        gate_grad, upper_grad = pull(hidden_grad)
        gate_grad = gate_grad.astype(jnp.bfloat16)
        upper_grad = upper_grad.astype(jnp.bfloat16)
        gate_grad, upper_grad, mlp_sum = down_hook((gate_grad, upper_grad, mlp_sum))
        mixed = (resid + mlp_sum.astype(jnp.float32)).astype(jnp.bfloat16)
        mid_part = (outer_cols(gate_grad, w_gate) + outer_cols(upper_grad, w_up)).astype(
            jnp.bfloat16
        )
        mid_part, gate_grad, upper_grad = down_hook((mid_part, gate_grad, upper_grad))
        held = {}

        def tie_gate(got):
            held["gate"], got = down_hook((inner_rows(normed_mid, gate_grad), got))
            return got

        def tie_up(got):
            held["up"], got = down_hook((inner_rows(normed_mid, upper_grad), got))
            return got

        mid_sum = plan.tp_sum(mid_part, (tie_gate, tie_up))
        gate_w_grad, up_w_grad = held["gate"], held["up"]
        big = Ring(plan, [gate_w_grad, up_w_grad])
        big.step()
        mid_grad = mid_sum.astype(jnp.float32)
        resid_grad = cotangent.astype(jnp.float32) + norm_back(resid, mlp_gain, mid_grad)
        mlp_gain_part = gain_term(resid_rows, lax.dynamic_slice_in_dim(mid_grad, offset, share, 0))
        resid_low = resid_grad.astype(jnp.bfloat16)
        out_w_grad_t = inner_rows(resid_low, attended)
        attended_grad = outer_cols(resid_low, w_out).astype(jnp.bfloat16)
        small = Ring(plan, [out_w_grad_t])

        def hook(values):
            if big.done < big.steps:
                big.step()
            if small.done < small.steps:
                small.step()
            if down.done < down.steps:
                down.step()
            down.state, big.state, small.state, values = lax.optimization_barrier(
                (down.state, big.state, small.state, values)
            )
            return values

        resid_grad, attended_grad = hook((resid_grad, attended_grad))
        q_grad, k_grad, v_grad, qg_part, kg_part = attend_back(
            attended_grad,
            q_raw,
            k_raw,
            query_gain,
            key_gain,
            queries,
            keys_rot,
            values,
            logsum,
            seqs,
            hook,
        )
        in_part = (
            outer_cols(q_grad, w_query)
            + outer_cols(k_grad, key_matrix)
            + outer_cols(v_grad, value_matrix)
        ).astype(jnp.bfloat16)
        in_part, q_grad, k_grad, v_grad = lax.optimization_barrier(
            (in_part, q_grad, k_grad, v_grad)
        )

        def tie_query(got):
            held["query"], got = lax.optimization_barrier((inner_rows(normed_in, q_grad), got))
            return got

        def tie_kv(got):
            held["key"], held["value"], got = lax.optimization_barrier(
                (inner_rows(normed_in, k_grad), inner_rows(normed_in, v_grad), got)
            )
            return got

        in_sum = plan.tp_sum(in_part, (tie_query, tie_kv))
        query_w_grad, key_w_grad, value_w_grad = held["query"], held["key"], held["value"]
        while big.done < big.steps:
            big.step()
        while small.done < small.steps:
            small.step()
        while down.done < down.steps:
            down.step()
        in_grad = in_sum.astype(jnp.float32)
        (down_sum,) = down.result()
        gate_sum, up_sum = big.result()
        (out_sum,) = small.result()
        query_sum, key_sum, value_sum = plan.dp_rs([query_w_grad, key_w_grad, value_w_grad])
        input_grad = resid_grad + norm_back(stream, attn_gain, in_grad)
        attn_gain_part = gain_term(stream_rows, lax.dynamic_slice_in_dim(in_grad, offset, share, 0))
        gains = plan.all_sum(jnp.concatenate([attn_gain_part, mlp_gain_part, qg_part, kg_part]))
        width = attn_gain_part.shape[0]
        head = qg_part.shape[0]
        attn_gain_grad = gains[:width]
        mlp_gain_grad = gains[width : 2 * width]
        query_gain_grad = gains[2 * width : 2 * width + head]
        key_gain_grad = gains[2 * width + head :]
        return (
            mixed,
            input_grad,
            attn_gain_grad,
            mlp_gain_grad,
            query_gain_grad,
            key_gain_grad,
            query_sum,
            key_sum,
            value_sum,
            out_sum.T,
            gate_sum,
            up_sum,
            down_sum.T,
        )

    return body


def solution(mesh):
    plan = Plan(mesh)
    placed = (
        P("dp", None),
        P(),
        P(None, "tensor"),
        P(None, "tensor"),
        P(None, "tensor"),
        P(),
        P(),
        P("tensor", None),
        P(),
        P(None, "tensor"),
        P(None, "tensor"),
        P("tensor", None),
        P("dp", None),
    )
    return jax.shard_map(
        make_on_device(plan),
        mesh=mesh,
        in_specs=placed,
        out_specs=(
            P("dp", None),
            P("dp", None),
            P(),
            P(),
            P(),
            P(),
            P("dp", "tensor"),
            P("dp", "tensor"),
            P("dp", "tensor"),
            P("tensor", "dp"),
            P("dp", "tensor"),
            P("dp", "tensor"),
            P("tensor", "dp"),
        ),
        check_vma=False,
    )
```

```python
import itertools
import math

import jax
import jax.numpy as jnp
import numpy as np
from jax import lax
from jax.sharding import PartitionSpec as P

HEAD_SIZE = 128
LEN = 128


EPS = 1e-06
THETA = 1000000.0


def product(form, left, right):
    return jnp.einsum(form, left, right, preferred_element_type=jnp.float32)


def matmul(left, right):
    return jnp.dot(left, right, preferred_element_type=jnp.float32)


def inner_rows(left, right):
    return lax.dot_general(
        left, right, (((0,), (0,)), ((), ())), preferred_element_type=jnp.float32
    )


def outer_cols(left, right):
    return lax.dot_general(
        left, right, (((1,), (1,)), ((), ())), preferred_element_type=jnp.float32
    )


def rms_scale(values, gain):
    return values * lax.rsqrt(jnp.mean(values * values, -1, keepdims=True) + EPS) * gain


def norm_back(values, gain, upstream):
    factor = lax.rsqrt(jnp.mean(values * values, -1, keepdims=True) + EPS)
    scaled = gain * upstream
    return factor * scaled - values * factor**3 * jnp.mean(scaled * values, -1, keepdims=True)


def gain_term(values, upstream):
    factor = lax.rsqrt(jnp.mean(values * values, -1, keepdims=True) + EPS)
    return jnp.sum(upstream * values * factor, 0)


def swiglu(gate, upper):
    return jax.nn.silu(gate) * upper


def rope_tables(length, width):
    position = jnp.arange(length).astype(jnp.float32)
    freqs = jnp.exp(jnp.arange(width // 2).astype(jnp.float32) * (-2.0 * math.log(THETA) / width))
    angles = position[:, None] * freqs[None, :]
    cosine = jnp.cos(angles)
    sine = jnp.sin(angles)
    return (jnp.concatenate([cosine, cosine], -1), jnp.concatenate([sine, sine], -1))


def head_prep(values, gain, cosine, sine):
    normed = values * lax.rsqrt(jnp.mean(values * values, -1, keepdims=True) + EPS) * gain
    half = normed.shape[-1] // 2
    turned = jnp.concatenate([-normed[..., half:], normed[..., :half]], -1)
    return normed * cosine[:, None, :] + turned * sine[:, None, :]


def causal_scores(queries, keys_rot, length):
    scores = product("sqgrd,skgd->sgrqk", queries, keys_rot) * (1.0 / math.sqrt(HEAD_SIZE))
    allowed = jnp.arange(length)[:, None] >= jnp.arange(length)[None, :]
    return jnp.where(allowed, scores, -1e30)


def attend(q_raw, k_raw, v_raw, query_gain, key_gain, seqs):
    total = q_raw.shape[0]
    length = total // seqs
    heads = q_raw.shape[1] // HEAD_SIZE
    kv_heads = k_raw.shape[1] // HEAD_SIZE
    repeat = heads // kv_heads
    cosine, sine = rope_tables(length, HEAD_SIZE)
    queries = head_prep(q_raw.reshape(seqs, length, heads, HEAD_SIZE), query_gain, cosine, sine)
    queries = queries.astype(jnp.bfloat16).reshape(seqs, length, kv_heads, repeat, HEAD_SIZE)
    keys_rot = head_prep(
        k_raw.reshape(seqs, length, kv_heads, HEAD_SIZE), key_gain, cosine, sine
    ).astype(jnp.bfloat16)
    values = v_raw.astype(jnp.bfloat16).reshape(seqs, length, kv_heads, HEAD_SIZE)
    scores = causal_scores(queries, keys_rot, length)
    top = jnp.max(scores, -1, keepdims=True)
    logsum = top + jnp.log(jnp.sum(jnp.exp(scores - top), -1, keepdims=True))
    weights = jnp.exp(scores - logsum).astype(jnp.bfloat16)
    attended = (
        product("sgrqk,skgd->sqgrd", weights, values)
        .astype(jnp.bfloat16)
        .reshape(total, heads * HEAD_SIZE)
    )
    return (attended, logsum, queries, keys_rot, values)


def attend_back(
    upstream, q_raw, k_raw, query_gain, key_gain, queries, keys_rot, values, logsum, seqs, hook
):
    total = q_raw.shape[0]
    length = total // seqs
    heads = q_raw.shape[1] // HEAD_SIZE
    kv_heads = k_raw.shape[1] // HEAD_SIZE
    repeat = heads // kv_heads
    cosine, sine = rope_tables(length, HEAD_SIZE)
    grad_out = upstream.reshape(seqs, length, kv_heads, repeat, HEAD_SIZE)
    scores = causal_scores(queries, keys_rot, length)
    probs = jnp.exp(scores - logsum)
    probs = hook(probs)
    value_grad = product("sgrqk,sqgrd->skgd", probs.astype(jnp.bfloat16), grad_out)
    prob_grad = product("sqgrd,skgd->sgrqk", grad_out, values)
    value_grad, prob_grad = hook((value_grad, prob_grad))
    center = jnp.sum(probs * prob_grad, -1, keepdims=True)
    score_grad = (probs * (prob_grad - center) * (1.0 / math.sqrt(HEAD_SIZE))).astype(jnp.bfloat16)
    score_grad = hook(score_grad)
    query_rot_grad = product("sgrqk,skgd->sqgrd", score_grad, keys_rot).reshape(
        seqs, length, heads, HEAD_SIZE
    )
    key_rot_grad = product("sgrqk,sqgrd->skgd", score_grad, queries)
    query_rot_grad, key_rot_grad = hook((query_rot_grad, key_rot_grad))
    query_in = q_raw.reshape(seqs, length, heads, HEAD_SIZE)
    key_in = k_raw.reshape(seqs, length, kv_heads, HEAD_SIZE)
    _, pull_query = jax.vjp(
        lambda inner, gain: head_prep(inner, gain, cosine, sine), query_in, query_gain
    )
    query_grad, query_gain_grad = pull_query(query_rot_grad)
    _, pull_key = jax.vjp(
        lambda inner, gain: head_prep(inner, gain, cosine, sine), key_in, key_gain
    )
    key_grad, key_gain_grad = pull_key(key_rot_grad)
    query_grad, key_grad = hook((query_grad, key_grad))
    return (
        query_grad.astype(jnp.bfloat16).reshape(total, heads * HEAD_SIZE),
        key_grad.astype(jnp.bfloat16).reshape(total, kv_heads * HEAD_SIZE),
        value_grad.astype(jnp.bfloat16).reshape(total, kv_heads * HEAD_SIZE),
        query_gain_grad,
        key_gain_grad,
    )


def snake_ring(coords):
    coords = [tuple(c) for c in coords]
    dims = [d for d in range(len(coords[0])) if len({c[d] for c in coords}) > 1]
    if not dims:
        return list(range(len(coords)))
    values = [sorted({c[d] for c in coords}) for d in dims]
    where = {tuple(c[d] for d in dims): i for i, c in enumerate(coords)}
    best = None
    for perm in itertools.permutations(range(len(dims))):
        def walk(level):
            if level == len(perm):
                return [()]
            inner = walk(level + 1)
            out = []
            for i, value in enumerate(values[perm[level]]):
                seq = inner if i % 2 == 0 else inner[::-1]
                out += [((perm[level], value),) + t for t in seq]
            return out

        order = []
        for path in walk(0):
            key = dict(path)
            point = tuple(key[k] for k in range(len(dims)))
            if point in where:
                order.append(where[point])
        if len(order) != len(coords):
            continue
        cost = sum(
            sum(abs(a - b) for a, b in zip(coords[order[i]], coords[order[(i + 1) % len(order)]]))
            for i in range(len(order))
        )
        if best is None or cost < best[0]:
            best = (cost, order)
    return best[1] if best else list(range(len(coords)))


class Plan:
    def __init__(self, mesh):
        names = mesh.axis_names
        devices = np.asarray(mesh.devices)
        dp_axis, tp_axis = names.index("dp"), names.index("tensor")
        devices = np.transpose(devices, (dp_axis, tp_axis))
        self.n_dp, self.n_tp = devices.shape
        dp_coords = [tuple(devices[d, 0].coords) for d in range(self.n_dp)]
        self.ring = snake_ring(dp_coords)
        self.pos = [self.ring.index(d) for d in range(self.n_dp)]
        n = self.n_dp
        self.cw = [(self.ring[i], self.ring[(i + 1) % n]) for i in range(n)]
        self.ccw = [(b, a) for a, b in self.cw]
        group = [devices[0, t] for t in range(self.n_tp)]
        self.tp_ok = False
        if self.n_tp == 4:
            chip = [tuple(g.coords) for g in group]
            core = [g.core_on_chip for g in group]
            same = [[u for u in range(4) if u != t and chip[u] == chip[t]] for t in range(4)]
            cross = [
                [u for u in range(4) if chip[u] != chip[t] and core[u] == core[t]] for t in range(4)
            ]
            if all(len(s) == 1 for s in same) and all(len(c) == 1 for c in cross):
                self.core_pairs = [(t, same[t][0]) for t in range(4)]
                self.chip_pairs = [(t, cross[t][0]) for t in range(4)]
                self.half_of = [0 if t < same[t][0] else 1 for t in range(4)]
                self.tp_ok = True

    def tp_sum(self, part):
        if not self.tp_ok:
            return lax.psum(part.astype(jnp.float32), "tensor").astype(jnp.bfloat16)
        rows = part.shape[0]
        h = rows // 2
        t = lax.axis_index("tensor")
        half = jnp.array(self.half_of, jnp.int32)[t]
        keep = lax.dynamic_slice_in_dim(part, half * h, h, 0)
        give = lax.dynamic_slice_in_dim(part, (1 - half) * h, h, 0)
        got = lax.ppermute(give, "tensor", self.core_pairs)
        chip_sum = (keep.astype(jnp.float32) + got.astype(jnp.float32)).astype(jnp.bfloat16)
        other = lax.ppermute(chip_sum, "tensor", self.chip_pairs)
        done = (chip_sum.astype(jnp.float32) + other.astype(jnp.float32)).astype(jnp.bfloat16)
        partner = lax.ppermute(done, "tensor", self.core_pairs)
        first = jnp.where(half == 0, done, partner)
        second = jnp.where(half == 0, partner, done)
        return jnp.concatenate([first, second], 0)

    def dp_rs(self, lhs, rhs):
        ring = Ring(self, lhs, rhs)
        for _ in range(ring.steps):
            ring.step()
        return ring.result()

    def all_sum(self, x):
        for axis, size in (("tensor", self.n_tp), ("dp", self.n_dp)):
            if size & (size - 1):
                x = lax.psum(x, axis)
                continue
            bit = 1
            while bit < size:
                x = x + lax.ppermute(x, axis, [(i, i ^ bit) for i in range(size)])
                bit *= 2
        return x


class Ring:
    def __init__(self, plan, lhs, rhs):
        self.plan = plan
        self.n = n = plan.n_dp
        self.me = lax.axis_index("dp")
        self.pos = jnp.array(plan.pos, jnp.int32)[self.me]
        self.order = jnp.array(plan.ring, jnp.int32)
        self.lhs = lhs
        self.rhs = rhs
        self.rows = lhs.shape[1] // n
        self.widths = [r.shape[1] for r in rhs]
        total = sum(self.widths)
        cut = total // 2
        self.sides = ([], [])
        start = 0
        for i, w in enumerate(self.widths):
            lo, hi = start, start + w
            if lo < cut:
                self.sides[0].append((i, 0, min(hi, cut) - lo))
            if hi > cut:
                self.sides[1].append((i, max(lo, cut) - lo, w))
            start = hi
        self.steps = n - 1
        self.done = 0
        self.state = None

    def piece(self, index, side):
        block = lax.dynamic_slice_in_dim(self.lhs, index * self.rows, self.rows, 1)
        parts = [
            inner_rows(block, self.rhs[i] if (lo, hi) == (0, self.widths[i]) else self.rhs[i][:, lo:hi])
            for i, lo, hi in self.sides[side]
        ]
        return parts[0] if len(parts) == 1 else jnp.concatenate(parts, 1)

    def step(self):
        n, s = self.n, self.done
        own_a = self.piece(self.order[(self.pos - 1 - s) % n], 0)
        own_b = self.piece(self.order[(self.pos + 1 + s) % n], 1)
        if self.state is None:
            send_a, send_b = own_a, own_b
        else:
            send_a, send_b = self.state[0] + own_a, self.state[1] + own_b
        got_a = lax.ppermute(send_a.astype(jnp.bfloat16), "dp", self.plan.cw)
        got_b = lax.ppermute(send_b.astype(jnp.bfloat16), "dp", self.plan.ccw)
        self.state = (got_a.astype(jnp.float32), got_b.astype(jnp.float32))
        self.done += 1

    def result(self):
        acc_a, acc_b = self.state
        total = jnp.concatenate([acc_a + self.piece(self.me, 0), acc_b + self.piece(self.me, 1)], 1)
        out, start = [], 0
        for w in self.widths:
            out.append(total[:, start : start + w])
            start += w
        return out


def make_on_device(plan):
    def body(
        tokens,
        attn_gain,
        w_query,
        key_matrix,
        value_matrix,
        query_gain,
        key_gain,
        w_out,
        mlp_gain,
        w_gate,
        w_up,
        w_down,
        cotangent,
    ):
        count = tokens.shape[0]
        seqs = count // LEN
        share = count // lax.axis_size("tensor")
        offset = lax.axis_index("tensor") * share
        stream = tokens.astype(jnp.float32)
        stream_rows = lax.dynamic_slice_in_dim(stream, offset, share, 0)
        normed_in = rms_scale(stream, attn_gain).astype(jnp.bfloat16)
        q_raw = matmul(normed_in, w_query)
        k_raw = matmul(normed_in, key_matrix)
        v_raw = matmul(normed_in, value_matrix)
        attended, logsum, queries, keys_rot, values = attend(
            q_raw, k_raw, v_raw, query_gain, key_gain, seqs
        )
        attn_part = matmul(attended, w_out).astype(jnp.bfloat16)
        resid = stream + plan.tp_sum(attn_part).astype(jnp.float32)
        resid_rows = lax.dynamic_slice_in_dim(resid, offset, share, 0)
        normed_mid = rms_scale(resid, mlp_gain).astype(jnp.bfloat16)
        gate = matmul(normed_mid, w_gate)
        upper = matmul(normed_mid, w_up)
        hidden = swiglu(gate, upper).astype(jnp.bfloat16)
        down = Ring(plan, cotangent, [hidden])
        down.step()
        mlp_part = matmul(hidden, w_down).astype(jnp.bfloat16)
        mixed = (resid + plan.tp_sum(mlp_part).astype(jnp.float32)).astype(jnp.bfloat16)

        def down_hook(values):
            if down.done < down.steps:
                down.step()
            down.state, values = lax.optimization_barrier((down.state, values))
            return values

        hidden_grad = down_hook(outer_cols(cotangent, w_down))
        _, pull = jax.vjp(swiglu, gate, upper)
        gate_grad, upper_grad = pull(hidden_grad)
        gate_grad = gate_grad.astype(jnp.bfloat16)
        upper_grad = upper_grad.astype(jnp.bfloat16)
        gate_grad, upper_grad = down_hook((gate_grad, upper_grad))
        mid_part = (outer_cols(gate_grad, w_gate) + outer_cols(upper_grad, w_up)).astype(
            jnp.bfloat16
        )
        mid_part, gate_grad, upper_grad = down_hook((mid_part, gate_grad, upper_grad))
        mid_sum = plan.tp_sum(mid_part)
        big = Ring(plan, normed_mid, [gate_grad, upper_grad])
        big.step()
        mid_grad = mid_sum.astype(jnp.float32)
        resid_grad = cotangent.astype(jnp.float32) + norm_back(resid, mlp_gain, mid_grad)
        mlp_gain_part = gain_term(resid_rows, lax.dynamic_slice_in_dim(mid_grad, offset, share, 0))
        resid_low = resid_grad.astype(jnp.bfloat16)
        attended_grad = outer_cols(resid_low, w_out).astype(jnp.bfloat16)
        small = Ring(plan, resid_low, [attended])

        def hook(values):
            if big.done < big.steps:
                big.step()
            if small.done < small.steps:
                small.step()
            if down.done < down.steps:
                down.step()
            down.state, big.state, small.state, values = lax.optimization_barrier(
                (down.state, big.state, small.state, values)
            )
            return values

        resid_grad, attended_grad = hook((resid_grad, attended_grad))
        q_grad, k_grad, v_grad, qg_part, kg_part = attend_back(
            attended_grad,
            q_raw,
            k_raw,
            query_gain,
            key_gain,
            queries,
            keys_rot,
            values,
            logsum,
            seqs,
            hook,
        )
        in_part = (
            outer_cols(q_grad, w_query)
            + outer_cols(k_grad, key_matrix)
            + outer_cols(v_grad, value_matrix)
        ).astype(jnp.bfloat16)
        in_part, q_grad, k_grad, v_grad = lax.optimization_barrier(
            (in_part, q_grad, k_grad, v_grad)
        )
        in_sum = plan.tp_sum(in_part)
        while big.done < big.steps:
            big.step()
        while small.done < small.steps:
            small.step()
        while down.done < down.steps:
            down.step()
        in_grad = in_sum.astype(jnp.float32)
        (down_sum,) = down.result()
        gate_sum, up_sum = big.result()
        (out_sum,) = small.result()
        query_sum, key_sum, value_sum = plan.dp_rs(normed_in, [q_grad, k_grad, v_grad])
        input_grad = resid_grad + norm_back(stream, attn_gain, in_grad)
        attn_gain_part = gain_term(stream_rows, lax.dynamic_slice_in_dim(in_grad, offset, share, 0))
        gains = plan.all_sum(jnp.concatenate([attn_gain_part, mlp_gain_part, qg_part, kg_part]))
        width = attn_gain_part.shape[0]
        head = qg_part.shape[0]
        attn_gain_grad = gains[:width]
        mlp_gain_grad = gains[width : 2 * width]
        query_gain_grad = gains[2 * width : 2 * width + head]
        key_gain_grad = gains[2 * width + head :]
        return (
            mixed,
            input_grad,
            attn_gain_grad,
            mlp_gain_grad,
            query_gain_grad,
            key_gain_grad,
            query_sum,
            key_sum,
            value_sum,
            out_sum.T,
            gate_sum,
            up_sum,
            down_sum.T,
        )

    return body


def solution(mesh):
    plan = Plan(mesh)
    placed = (
        P("dp", None),
        P(),
        P(None, "tensor"),
        P(None, "tensor"),
        P(None, "tensor"),
        P(),
        P(),
        P("tensor", None),
        P(),
        P(None, "tensor"),
        P(None, "tensor"),
        P("tensor", None),
        P("dp", None),
    )
    return jax.shard_map(
        make_on_device(plan),
        mesh=mesh,
        in_specs=placed,
        out_specs=(
            P("dp", None),
            P("dp", None),
            P(),
            P(),
            P(),
            P(),
            P("dp", "tensor"),
            P("dp", "tensor"),
            P("dp", "tensor"),
            P("tensor", "dp"),
            P("dp", "tensor"),
            P("dp", "tensor"),
            P("tensor", "dp"),
        ),
        check_vma=False,
    )
```

```python
import itertools
import math

import jax
import jax.numpy as jnp
import numpy as np
from jax import lax
from jax.sharding import PartitionSpec as P

HEAD_SIZE = 128
LEN = 128


EPS = 1e-06
THETA = 1000000.0


def product(form, left, right):
    return jnp.einsum(form, left, right, preferred_element_type=jnp.float32)


def matmul(left, right):
    return jnp.dot(left, right, preferred_element_type=jnp.float32)


def inner_rows(left, right):
    return lax.dot_general(
        left, right, (((0,), (0,)), ((), ())), preferred_element_type=jnp.float32
    )


def outer_cols(left, right):
    return lax.dot_general(
        left, right, (((1,), (1,)), ((), ())), preferred_element_type=jnp.float32
    )


def rms_scale(values, gain):
    return values * lax.rsqrt(jnp.mean(values * values, -1, keepdims=True) + EPS) * gain


def norm_back(values, gain, upstream):
    factor = lax.rsqrt(jnp.mean(values * values, -1, keepdims=True) + EPS)
    scaled = gain * upstream
    return factor * scaled - values * factor**3 * jnp.mean(scaled * values, -1, keepdims=True)


def gain_term(values, upstream):
    factor = lax.rsqrt(jnp.mean(values * values, -1, keepdims=True) + EPS)
    return jnp.sum(upstream * values * factor, 0)


def swiglu(gate, upper):
    return jax.nn.silu(gate) * upper


def rope_tables(length, width):
    position = jnp.arange(length).astype(jnp.float32)
    freqs = jnp.exp(jnp.arange(width // 2).astype(jnp.float32) * (-2.0 * math.log(THETA) / width))
    angles = position[:, None] * freqs[None, :]
    cosine = jnp.cos(angles)
    sine = jnp.sin(angles)
    return (jnp.concatenate([cosine, cosine], -1), jnp.concatenate([sine, sine], -1))


def head_prep(values, gain, cosine, sine):
    normed = values * lax.rsqrt(jnp.mean(values * values, -1, keepdims=True) + EPS) * gain
    half = normed.shape[-1] // 2
    turned = jnp.concatenate([-normed[..., half:], normed[..., :half]], -1)
    return normed * cosine[:, None, :] + turned * sine[:, None, :]


def causal_scores(queries, keys_rot, length):
    scores = product("sqgrd,skgd->sgrqk", queries, keys_rot) * (1.0 / math.sqrt(HEAD_SIZE))
    allowed = jnp.arange(length)[:, None] >= jnp.arange(length)[None, :]
    return jnp.where(allowed, scores, -1e30)


def attend(q_raw, k_raw, v_raw, query_gain, key_gain, seqs):
    total = q_raw.shape[0]
    length = total // seqs
    heads = q_raw.shape[1] // HEAD_SIZE
    kv_heads = k_raw.shape[1] // HEAD_SIZE
    repeat = heads // kv_heads
    cosine, sine = rope_tables(length, HEAD_SIZE)
    queries = head_prep(q_raw.reshape(seqs, length, heads, HEAD_SIZE), query_gain, cosine, sine)
    queries = queries.astype(jnp.bfloat16).reshape(seqs, length, kv_heads, repeat, HEAD_SIZE)
    keys_rot = head_prep(
        k_raw.reshape(seqs, length, kv_heads, HEAD_SIZE), key_gain, cosine, sine
    ).astype(jnp.bfloat16)
    values = v_raw.astype(jnp.bfloat16).reshape(seqs, length, kv_heads, HEAD_SIZE)
    scores = causal_scores(queries, keys_rot, length)
    top = jnp.max(scores, -1, keepdims=True)
    logsum = top + jnp.log(jnp.sum(jnp.exp(scores - top), -1, keepdims=True))
    weights = jnp.exp(scores - logsum).astype(jnp.bfloat16)
    attended = (
        product("sgrqk,skgd->sqgrd", weights, values)
        .astype(jnp.bfloat16)
        .reshape(total, heads * HEAD_SIZE)
    )
    return (attended, logsum, queries, keys_rot, values)


def attend_back(
    upstream, q_raw, k_raw, query_gain, key_gain, queries, keys_rot, values, logsum, seqs, hook
):
    total = q_raw.shape[0]
    length = total // seqs
    heads = q_raw.shape[1] // HEAD_SIZE
    kv_heads = k_raw.shape[1] // HEAD_SIZE
    repeat = heads // kv_heads
    cosine, sine = rope_tables(length, HEAD_SIZE)
    grad_out = upstream.reshape(seqs, length, kv_heads, repeat, HEAD_SIZE)
    scores = causal_scores(queries, keys_rot, length)
    probs = jnp.exp(scores - logsum)
    probs = hook(probs)
    value_grad = product("sgrqk,sqgrd->skgd", probs.astype(jnp.bfloat16), grad_out)
    prob_grad = product("sqgrd,skgd->sgrqk", grad_out, values)
    value_grad, prob_grad = hook((value_grad, prob_grad))
    center = jnp.sum(probs * prob_grad, -1, keepdims=True)
    score_grad = (probs * (prob_grad - center) * (1.0 / math.sqrt(HEAD_SIZE))).astype(jnp.bfloat16)
    score_grad = hook(score_grad)
    query_rot_grad = product("sgrqk,skgd->sqgrd", score_grad, keys_rot).reshape(
        seqs, length, heads, HEAD_SIZE
    )
    key_rot_grad = product("sgrqk,sqgrd->skgd", score_grad, queries)
    query_rot_grad, key_rot_grad = hook((query_rot_grad, key_rot_grad))
    query_in = q_raw.reshape(seqs, length, heads, HEAD_SIZE)
    key_in = k_raw.reshape(seqs, length, kv_heads, HEAD_SIZE)
    _, pull_query = jax.vjp(
        lambda inner, gain: head_prep(inner, gain, cosine, sine), query_in, query_gain
    )
    query_grad, query_gain_grad = pull_query(query_rot_grad)
    _, pull_key = jax.vjp(
        lambda inner, gain: head_prep(inner, gain, cosine, sine), key_in, key_gain
    )
    key_grad, key_gain_grad = pull_key(key_rot_grad)
    query_grad, key_grad = hook((query_grad, key_grad))
    return (
        query_grad.astype(jnp.bfloat16).reshape(total, heads * HEAD_SIZE),
        key_grad.astype(jnp.bfloat16).reshape(total, kv_heads * HEAD_SIZE),
        value_grad.astype(jnp.bfloat16).reshape(total, kv_heads * HEAD_SIZE),
        query_gain_grad,
        key_gain_grad,
    )


def snake_ring(coords):
    coords = [tuple(c) for c in coords]
    dims = [d for d in range(len(coords[0])) if len({c[d] for c in coords}) > 1]
    if not dims:
        return list(range(len(coords)))
    values = [sorted({c[d] for c in coords}) for d in dims]
    where = {tuple(c[d] for d in dims): i for i, c in enumerate(coords)}
    best = None
    for perm in itertools.permutations(range(len(dims))):
        def walk(level):
            if level == len(perm):
                return [()]
            inner = walk(level + 1)
            out = []
            for i, value in enumerate(values[perm[level]]):
                seq = inner if i % 2 == 0 else inner[::-1]
                out += [((perm[level], value),) + t for t in seq]
            return out

        order = []
        for path in walk(0):
            key = dict(path)
            point = tuple(key[k] for k in range(len(dims)))
            if point in where:
                order.append(where[point])
        if len(order) != len(coords):
            continue
        cost = sum(
            sum(abs(a - b) for a, b in zip(coords[order[i]], coords[order[(i + 1) % len(order)]]))
            for i in range(len(order))
        )
        if best is None or cost < best[0]:
            best = (cost, order)
    return best[1] if best else list(range(len(coords)))


class Plan:
    def __init__(self, mesh):
        names = mesh.axis_names
        devices = np.asarray(mesh.devices)
        dp_axis, tp_axis = names.index("dp"), names.index("tensor")
        devices = np.transpose(devices, (dp_axis, tp_axis))
        self.n_dp, self.n_tp = devices.shape
        dp_coords = [tuple(devices[d, 0].coords) for d in range(self.n_dp)]
        self.ring = snake_ring(dp_coords)
        self.pos = [self.ring.index(d) for d in range(self.n_dp)]
        n = self.n_dp
        self.cw = [(self.ring[i], self.ring[(i + 1) % n]) for i in range(n)]
        self.ccw = [(b, a) for a, b in self.cw]
        group = [devices[0, t] for t in range(self.n_tp)]
        self.tp_ok = False
        if self.n_tp == 4:
            chip = [tuple(g.coords) for g in group]
            core = [g.core_on_chip for g in group]
            same = [[u for u in range(4) if u != t and chip[u] == chip[t]] for t in range(4)]
            cross = [
                [u for u in range(4) if chip[u] != chip[t] and core[u] == core[t]] for t in range(4)
            ]
            if all(len(s) == 1 for s in same) and all(len(c) == 1 for c in cross):
                self.core_pairs = [(t, same[t][0]) for t in range(4)]
                self.chip_pairs = [(t, cross[t][0]) for t in range(4)]
                self.half_of = [0 if t < same[t][0] else 1 for t in range(4)]
                self.tp_ok = True

    def tp_sum(self, part, ties=()):
        if not self.tp_ok:
            return lax.psum(part.astype(jnp.float32), "tensor").astype(jnp.bfloat16)
        ties = list(ties) + [lambda x: x] * (2 - len(ties))
        rows = part.shape[0]
        h = rows // 2
        t = lax.axis_index("tensor")
        half = jnp.array(self.half_of, jnp.int32)[t]
        keep = lax.dynamic_slice_in_dim(part, half * h, h, 0)
        give = lax.dynamic_slice_in_dim(part, (1 - half) * h, h, 0)
        got = ties[0](lax.ppermute(give, "tensor", self.core_pairs))
        chip_sum = (keep.astype(jnp.float32) + got.astype(jnp.float32)).astype(jnp.bfloat16)
        other = ties[1](lax.ppermute(chip_sum, "tensor", self.chip_pairs))
        done = (chip_sum.astype(jnp.float32) + other.astype(jnp.float32)).astype(jnp.bfloat16)
        partner = lax.ppermute(done, "tensor", self.core_pairs)
        first = jnp.where(half == 0, done, partner)
        second = jnp.where(half == 0, partner, done)
        return jnp.concatenate([first, second], 0)

    def dp_rs(self, grads):
        ring = Ring(self, grads)
        for _ in range(ring.steps):
            ring.step()
        return ring.result()

    def all_sum(self, x):
        for axis, size in (("tensor", self.n_tp), ("dp", self.n_dp)):
            if size & (size - 1):
                x = lax.psum(x, axis)
                continue
            bit = 1
            while bit < size:
                x = x + lax.ppermute(x, axis, [(i, i ^ bit) for i in range(size)])
                bit *= 2
        return x


class Ring:
    def __init__(self, plan, grads):
        self.plan = plan
        self.n = n = plan.n_dp
        self.me = lax.axis_index("dp")
        self.pos = jnp.array(plan.pos, jnp.int32)[self.me]
        self.order = jnp.array(plan.ring, jnp.int32)
        self.widths = [g.shape[1] for g in grads]
        self.grads = grads
        self.rows = grads[0].shape[0] // n
        self.steps = n - 1
        self.done = 0
        self.state = None

    def piece(self, index, side):
        half = self.rows // 2
        start = index * self.rows + side * half
        parts = [lax.dynamic_slice_in_dim(g, start, half, 0) for g in self.grads]
        return parts[0] if len(parts) == 1 else jnp.concatenate(parts, 1)

    def step(self):
        n, s = self.n, self.done
        own_a = self.piece(self.order[(self.pos - 1 - s) % n], 0)
        own_b = self.piece(self.order[(self.pos + 1 + s) % n], 1)
        if self.state is None:
            send_a, send_b = own_a, own_b
        else:
            send_a, send_b = self.state[0] + own_a, self.state[1] + own_b
        got_a = lax.ppermute(send_a.astype(jnp.bfloat16), "dp", self.plan.cw)
        got_b = lax.ppermute(send_b.astype(jnp.bfloat16), "dp", self.plan.ccw)
        self.state = (got_a.astype(jnp.float32), got_b.astype(jnp.float32))
        self.done += 1

    def result(self):
        acc_a, acc_b = self.state
        total = jnp.concatenate([acc_a + self.piece(self.me, 0), acc_b + self.piece(self.me, 1)], 0)
        out, start = [], 0
        for w in self.widths:
            out.append(total[:, start : start + w])
            start += w
        return out


def make_on_device(plan):
    def body(
        tokens,
        attn_gain,
        w_query,
        key_matrix,
        value_matrix,
        query_gain,
        key_gain,
        w_out,
        mlp_gain,
        w_gate,
        w_up,
        w_down,
        cotangent,
    ):
        count = tokens.shape[0]
        seqs = count // LEN
        share = count // lax.axis_size("tensor")
        offset = lax.axis_index("tensor") * share
        stream = tokens.astype(jnp.float32)
        stream_rows = lax.dynamic_slice_in_dim(stream, offset, share, 0)
        normed_in = rms_scale(stream, attn_gain).astype(jnp.bfloat16)
        q_raw = matmul(normed_in, w_query)
        k_raw = matmul(normed_in, key_matrix)
        v_raw = matmul(normed_in, value_matrix)
        attended, logsum, queries, keys_rot, values = attend(
            q_raw, k_raw, v_raw, query_gain, key_gain, seqs
        )
        attn_part = matmul(attended, w_out).astype(jnp.bfloat16)
        held = {}

        def tie_hidden(got):
            held["hidden_grad"], got = lax.optimization_barrier(
                (outer_cols(cotangent, w_down), got)
            )
            return got

        resid = stream + plan.tp_sum(attn_part, (lambda x: x, tie_hidden)).astype(jnp.float32)
        resid_rows = lax.dynamic_slice_in_dim(resid, offset, share, 0)
        normed_mid = rms_scale(resid, mlp_gain).astype(jnp.bfloat16)
        gate = matmul(normed_mid, w_gate)
        upper = matmul(normed_mid, w_up)
        hidden = swiglu(gate, upper).astype(jnp.bfloat16)
        down_grad_t = inner_rows(cotangent, hidden)
        down = Ring(plan, [down_grad_t])
        down.step()
        mlp_part = matmul(hidden, w_down).astype(jnp.bfloat16)
        mixed = (resid + plan.tp_sum(mlp_part).astype(jnp.float32)).astype(jnp.bfloat16)

        def down_hook(values):
            if down.done < down.steps:
                down.step()
            down.state, values = lax.optimization_barrier((down.state, values))
            return values

        hidden_grad = down_hook(held["hidden_grad"])
        _, pull = jax.vjp(swiglu, gate, upper)
        gate_grad, upper_grad = pull(hidden_grad)
        gate_grad = gate_grad.astype(jnp.bfloat16)
        upper_grad = upper_grad.astype(jnp.bfloat16)
        gate_grad, upper_grad = down_hook((gate_grad, upper_grad))
        mid_part = (outer_cols(gate_grad, w_gate) + outer_cols(upper_grad, w_up)).astype(
            jnp.bfloat16
        )
        mid_part, gate_grad, upper_grad = down_hook((mid_part, gate_grad, upper_grad))
        mid_sum = plan.tp_sum(mid_part)
        gate_w_grad = down_hook(inner_rows(normed_mid, gate_grad))
        up_w_grad = down_hook(inner_rows(normed_mid, upper_grad))
        big = Ring(plan, [gate_w_grad, up_w_grad])
        big.step()
        mid_grad = mid_sum.astype(jnp.float32)
        resid_grad = cotangent.astype(jnp.float32) + norm_back(resid, mlp_gain, mid_grad)
        mlp_gain_part = gain_term(resid_rows, lax.dynamic_slice_in_dim(mid_grad, offset, share, 0))
        resid_low = resid_grad.astype(jnp.bfloat16)
        out_w_grad_t = inner_rows(resid_low, attended)
        attended_grad = outer_cols(resid_low, w_out).astype(jnp.bfloat16)
        small = Ring(plan, [out_w_grad_t])

        def hook(values):
            if big.done < big.steps:
                big.step()
            if small.done < small.steps:
                small.step()
            if down.done < down.steps:
                down.step()
            down.state, big.state, small.state, values = lax.optimization_barrier(
                (down.state, big.state, small.state, values)
            )
            return values

        resid_grad, attended_grad = hook((resid_grad, attended_grad))
        q_grad, k_grad, v_grad, qg_part, kg_part = attend_back(
            attended_grad,
            q_raw,
            k_raw,
            query_gain,
            key_gain,
            queries,
            keys_rot,
            values,
            logsum,
            seqs,
            hook,
        )
        in_part = (
            outer_cols(q_grad, w_query)
            + outer_cols(k_grad, key_matrix)
            + outer_cols(v_grad, value_matrix)
        ).astype(jnp.bfloat16)
        in_part, q_grad, k_grad, v_grad = lax.optimization_barrier(
            (in_part, q_grad, k_grad, v_grad)
        )
        in_sum = plan.tp_sum(in_part)
        query_w_grad = inner_rows(normed_in, q_grad)
        key_w_grad = inner_rows(normed_in, k_grad)
        value_w_grad = inner_rows(normed_in, v_grad)
        while big.done < big.steps:
            big.step()
        while small.done < small.steps:
            small.step()
        while down.done < down.steps:
            down.step()
        in_grad = in_sum.astype(jnp.float32)
        (down_sum,) = down.result()
        gate_sum, up_sum = big.result()
        (out_sum,) = small.result()
        query_sum, key_sum, value_sum = plan.dp_rs([query_w_grad, key_w_grad, value_w_grad])
        input_grad = resid_grad + norm_back(stream, attn_gain, in_grad)
        attn_gain_part = gain_term(stream_rows, lax.dynamic_slice_in_dim(in_grad, offset, share, 0))
        gains = plan.all_sum(jnp.concatenate([attn_gain_part, mlp_gain_part, qg_part, kg_part]))
        width = attn_gain_part.shape[0]
        head = qg_part.shape[0]
        attn_gain_grad = gains[:width]
        mlp_gain_grad = gains[width : 2 * width]
        query_gain_grad = gains[2 * width : 2 * width + head]
        key_gain_grad = gains[2 * width + head :]
        return (
            mixed,
            input_grad,
            attn_gain_grad,
            mlp_gain_grad,
            query_gain_grad,
            key_gain_grad,
            query_sum,
            key_sum,
            value_sum,
            out_sum.T,
            gate_sum,
            up_sum,
            down_sum.T,
        )

    return body


def solution(mesh):
    plan = Plan(mesh)
    placed = (
        P("dp", None),
        P(),
        P(None, "tensor"),
        P(None, "tensor"),
        P(None, "tensor"),
        P(),
        P(),
        P("tensor", None),
        P(),
        P(None, "tensor"),
        P(None, "tensor"),
        P("tensor", None),
        P("dp", None),
    )
    return jax.shard_map(
        make_on_device(plan),
        mesh=mesh,
        in_specs=placed,
        out_specs=(
            P("dp", None),
            P("dp", None),
            P(),
            P(),
            P(),
            P(),
            P("dp", "tensor"),
            P("dp", "tensor"),
            P("dp", "tensor"),
            P("tensor", "dp"),
            P("dp", "tensor"),
            P("dp", "tensor"),
            P("tensor", "dp"),
        ),
        check_vma=False,
    )
```

```python
import itertools
import math

import jax
import jax.numpy as jnp
import numpy as np
from jax import lax
from jax.sharding import PartitionSpec as P

HEAD_SIZE = 128
LEN = 128


EPS = 1e-06
THETA = 1000000.0


def product(form, left, right):
    return jnp.einsum(form, left, right, preferred_element_type=jnp.float32)


def matmul(left, right):
    return jnp.dot(left, right, preferred_element_type=jnp.float32)


def inner_rows(left, right):
    return lax.dot_general(
        left, right, (((0,), (0,)), ((), ())), preferred_element_type=jnp.float32
    )


def outer_cols(left, right):
    return lax.dot_general(
        left, right, (((1,), (1,)), ((), ())), preferred_element_type=jnp.float32
    )


def rms_scale(values, gain):
    return values * lax.rsqrt(jnp.mean(values * values, -1, keepdims=True) + EPS) * gain


def norm_back(values, gain, upstream):
    factor = lax.rsqrt(jnp.mean(values * values, -1, keepdims=True) + EPS)
    scaled = gain * upstream
    return factor * scaled - values * factor**3 * jnp.mean(scaled * values, -1, keepdims=True)


def gain_term(values, upstream):
    factor = lax.rsqrt(jnp.mean(values * values, -1, keepdims=True) + EPS)
    return jnp.sum(upstream * values * factor, 0)


def swiglu(gate, upper):
    return jax.nn.silu(gate) * upper


def rope_tables(length, width):
    position = jnp.arange(length).astype(jnp.float32)
    freqs = jnp.exp(jnp.arange(width // 2).astype(jnp.float32) * (-2.0 * math.log(THETA) / width))
    angles = position[:, None] * freqs[None, :]
    cosine = jnp.cos(angles)
    sine = jnp.sin(angles)
    return (jnp.concatenate([cosine, cosine], -1), jnp.concatenate([sine, sine], -1))


def head_prep(values, gain, cosine, sine):
    normed = values * lax.rsqrt(jnp.mean(values * values, -1, keepdims=True) + EPS) * gain
    half = normed.shape[-1] // 2
    turned = jnp.concatenate([-normed[..., half:], normed[..., :half]], -1)
    return normed * cosine[:, None, :] + turned * sine[:, None, :]


def causal_scores(queries, keys_rot, length):
    scores = product("sqgrd,skgd->sgrqk", queries, keys_rot) * (1.0 / math.sqrt(HEAD_SIZE))
    allowed = jnp.arange(length)[:, None] >= jnp.arange(length)[None, :]
    return jnp.where(allowed, scores, -1e30)


def attend(q_raw, k_raw, v_raw, query_gain, key_gain, seqs):
    total = q_raw.shape[0]
    length = total // seqs
    heads = q_raw.shape[1] // HEAD_SIZE
    kv_heads = k_raw.shape[1] // HEAD_SIZE
    repeat = heads // kv_heads
    cosine, sine = rope_tables(length, HEAD_SIZE)
    queries = head_prep(q_raw.reshape(seqs, length, heads, HEAD_SIZE), query_gain, cosine, sine)
    queries = queries.astype(jnp.bfloat16).reshape(seqs, length, kv_heads, repeat, HEAD_SIZE)
    keys_rot = head_prep(
        k_raw.reshape(seqs, length, kv_heads, HEAD_SIZE), key_gain, cosine, sine
    ).astype(jnp.bfloat16)
    values = v_raw.astype(jnp.bfloat16).reshape(seqs, length, kv_heads, HEAD_SIZE)
    scores = causal_scores(queries, keys_rot, length)
    top = jnp.max(scores, -1, keepdims=True)
    logsum = top + jnp.log(jnp.sum(jnp.exp(scores - top), -1, keepdims=True))
    weights = jnp.exp(scores - logsum).astype(jnp.bfloat16)
    attended = (
        product("sgrqk,skgd->sqgrd", weights, values)
        .astype(jnp.bfloat16)
        .reshape(total, heads * HEAD_SIZE)
    )
    return (attended, logsum, queries, keys_rot, values)


def attend_back(
    upstream, q_raw, k_raw, query_gain, key_gain, queries, keys_rot, values, logsum, seqs, hook
):
    total = q_raw.shape[0]
    length = total // seqs
    heads = q_raw.shape[1] // HEAD_SIZE
    kv_heads = k_raw.shape[1] // HEAD_SIZE
    repeat = heads // kv_heads
    cosine, sine = rope_tables(length, HEAD_SIZE)
    grad_out = upstream.reshape(seqs, length, kv_heads, repeat, HEAD_SIZE)
    scores = causal_scores(queries, keys_rot, length)
    probs = jnp.exp(scores - logsum)
    probs = hook(probs)
    value_grad = product("sgrqk,sqgrd->skgd", probs.astype(jnp.bfloat16), grad_out)
    prob_grad = product("sqgrd,skgd->sgrqk", grad_out, values)
    value_grad, prob_grad = hook((value_grad, prob_grad))
    center = jnp.sum(probs * prob_grad, -1, keepdims=True)
    score_grad = (probs * (prob_grad - center) * (1.0 / math.sqrt(HEAD_SIZE))).astype(jnp.bfloat16)
    score_grad = hook(score_grad)
    query_rot_grad = product("sgrqk,skgd->sqgrd", score_grad, keys_rot).reshape(
        seqs, length, heads, HEAD_SIZE
    )
    key_rot_grad = product("sgrqk,sqgrd->skgd", score_grad, queries)
    query_rot_grad, key_rot_grad = hook((query_rot_grad, key_rot_grad))
    query_in = q_raw.reshape(seqs, length, heads, HEAD_SIZE)
    key_in = k_raw.reshape(seqs, length, kv_heads, HEAD_SIZE)
    _, pull_query = jax.vjp(
        lambda inner, gain: head_prep(inner, gain, cosine, sine), query_in, query_gain
    )
    query_grad, query_gain_grad = pull_query(query_rot_grad)
    _, pull_key = jax.vjp(
        lambda inner, gain: head_prep(inner, gain, cosine, sine), key_in, key_gain
    )
    key_grad, key_gain_grad = pull_key(key_rot_grad)
    query_grad, key_grad = hook((query_grad, key_grad))
    return (
        query_grad.astype(jnp.bfloat16).reshape(total, heads * HEAD_SIZE),
        key_grad.astype(jnp.bfloat16).reshape(total, kv_heads * HEAD_SIZE),
        value_grad.astype(jnp.bfloat16).reshape(total, kv_heads * HEAD_SIZE),
        query_gain_grad,
        key_gain_grad,
    )


def snake_ring(coords):
    coords = [tuple(c) for c in coords]
    dims = [d for d in range(len(coords[0])) if len({c[d] for c in coords}) > 1]
    if not dims:
        return list(range(len(coords)))
    values = [sorted({c[d] for c in coords}) for d in dims]
    where = {tuple(c[d] for d in dims): i for i, c in enumerate(coords)}
    best = None
    for perm in itertools.permutations(range(len(dims))):
        def walk(level):
            if level == len(perm):
                return [()]
            inner = walk(level + 1)
            out = []
            for i, value in enumerate(values[perm[level]]):
                seq = inner if i % 2 == 0 else inner[::-1]
                out += [((perm[level], value),) + t for t in seq]
            return out

        order = []
        for path in walk(0):
            key = dict(path)
            point = tuple(key[k] for k in range(len(dims)))
            if point in where:
                order.append(where[point])
        if len(order) != len(coords):
            continue
        cost = sum(
            sum(abs(a - b) for a, b in zip(coords[order[i]], coords[order[(i + 1) % len(order)]]))
            for i in range(len(order))
        )
        if best is None or cost < best[0]:
            best = (cost, order)
    return best[1] if best else list(range(len(coords)))


class Plan:
    def __init__(self, mesh):
        names = mesh.axis_names
        devices = np.asarray(mesh.devices)
        dp_axis, tp_axis = names.index("dp"), names.index("tensor")
        devices = np.transpose(devices, (dp_axis, tp_axis))
        self.n_dp, self.n_tp = devices.shape
        dp_coords = [tuple(devices[d, 0].coords) for d in range(self.n_dp)]
        self.ring = snake_ring(dp_coords)
        self.pos = [self.ring.index(d) for d in range(self.n_dp)]
        n = self.n_dp
        self.cw = [(self.ring[i], self.ring[(i + 1) % n]) for i in range(n)]
        self.ccw = [(b, a) for a, b in self.cw]
        group = [devices[0, t] for t in range(self.n_tp)]
        self.tp_ok = False
        if self.n_tp == 4:
            chip = [tuple(g.coords) for g in group]
            core = [g.core_on_chip for g in group]
            same = [[u for u in range(4) if u != t and chip[u] == chip[t]] for t in range(4)]
            cross = [
                [u for u in range(4) if chip[u] != chip[t] and core[u] == core[t]] for t in range(4)
            ]
            if all(len(s) == 1 for s in same) and all(len(c) == 1 for c in cross):
                self.core_pairs = [(t, same[t][0]) for t in range(4)]
                self.chip_pairs = [(t, cross[t][0]) for t in range(4)]
                self.half_of = [0 if t < same[t][0] else 1 for t in range(4)]
                self.tp_ok = True

    def tp_begin(self, part):
        if not self.tp_ok:
            total = lax.psum(part.astype(jnp.float32), "tensor").astype(jnp.bfloat16)
            return {"got": total, "other": total}
        rows = part.shape[0]
        h = rows // 2
        t = lax.axis_index("tensor")
        half = jnp.array(self.half_of, jnp.int32)[t]
        keep = lax.dynamic_slice_in_dim(part, half * h, h, 0)
        give = lax.dynamic_slice_in_dim(part, (1 - half) * h, h, 0)
        got = lax.ppermute(give, "tensor", self.core_pairs)
        return {"half": half, "keep": keep, "got": got}

    def tp_mid(self, st):
        if not self.tp_ok:
            return
        st["chip_sum"] = (st["keep"].astype(jnp.float32) + st["got"].astype(jnp.float32)).astype(
            jnp.bfloat16
        )
        st["other"] = lax.ppermute(st["chip_sum"], "tensor", self.chip_pairs)

    def tp_end(self, st):
        if not self.tp_ok:
            return st["other"]
        half = st["half"]
        done = (st["chip_sum"].astype(jnp.float32) + st["other"].astype(jnp.float32)).astype(
            jnp.bfloat16
        )
        partner = lax.ppermute(done, "tensor", self.core_pairs)
        first = jnp.where(half == 0, done, partner)
        second = jnp.where(half == 0, partner, done)
        return jnp.concatenate([first, second], 0)

    def tp_sum(self, part, ties=()):
        ties = list(ties) + [lambda x: x] * (2 - len(ties))
        st = self.tp_begin(part)
        st["got"] = ties[0](st["got"])
        self.tp_mid(st)
        st["other"] = ties[1](st["other"])
        return self.tp_end(st)

    def dp_rs(self, grads):
        ring = Ring(self, grads)
        for _ in range(ring.steps):
            ring.step()
        return ring.result()

    def all_sum(self, x):
        for axis, size in (("tensor", self.n_tp), ("dp", self.n_dp)):
            if size & (size - 1):
                x = lax.psum(x, axis)
                continue
            bit = 1
            while bit < size:
                x = x + lax.ppermute(x, axis, [(i, i ^ bit) for i in range(size)])
                bit *= 2
        return x


class Ring:
    def __init__(self, plan, grads):
        self.plan = plan
        self.n = n = plan.n_dp
        self.me = lax.axis_index("dp")
        self.pos = jnp.array(plan.pos, jnp.int32)[self.me]
        self.order = jnp.array(plan.ring, jnp.int32)
        self.widths = [g.shape[1] for g in grads]
        self.grads = grads
        self.rows = grads[0].shape[0] // n
        self.steps = n - 1
        self.done = 0
        self.state = None

    def piece(self, index, side):
        half = self.rows // 2
        start = index * self.rows + side * half
        parts = [lax.dynamic_slice_in_dim(g, start, half, 0) for g in self.grads]
        return parts[0] if len(parts) == 1 else jnp.concatenate(parts, 1)

    def step(self):
        n, s = self.n, self.done
        own_a = self.piece(self.order[(self.pos - 1 - s) % n], 0)
        own_b = self.piece(self.order[(self.pos + 1 + s) % n], 1)
        if self.state is None:
            send_a, send_b = own_a, own_b
        else:
            send_a, send_b = self.state[0] + own_a, self.state[1] + own_b
        got_a = lax.ppermute(send_a.astype(jnp.bfloat16), "dp", self.plan.cw)
        got_b = lax.ppermute(send_b.astype(jnp.bfloat16), "dp", self.plan.ccw)
        self.state = (got_a.astype(jnp.float32), got_b.astype(jnp.float32))
        self.done += 1

    def result(self):
        acc_a, acc_b = self.state
        total = jnp.concatenate([acc_a + self.piece(self.me, 0), acc_b + self.piece(self.me, 1)], 0)
        out, start = [], 0
        for w in self.widths:
            out.append(total[:, start : start + w])
            start += w
        return out


def make_on_device(plan):
    def body(
        tokens,
        attn_gain,
        w_query,
        key_matrix,
        value_matrix,
        query_gain,
        key_gain,
        w_out,
        mlp_gain,
        w_gate,
        w_up,
        w_down,
        cotangent,
    ):
        count = tokens.shape[0]
        seqs = count // LEN
        share = count // lax.axis_size("tensor")
        offset = lax.axis_index("tensor") * share
        stream = tokens.astype(jnp.float32)
        stream_rows = lax.dynamic_slice_in_dim(stream, offset, share, 0)
        normed_in = rms_scale(stream, attn_gain).astype(jnp.bfloat16)
        q_raw = matmul(normed_in, w_query)
        k_raw = matmul(normed_in, key_matrix)
        v_raw = matmul(normed_in, value_matrix)
        attended, logsum, queries, keys_rot, values = attend(
            q_raw, k_raw, v_raw, query_gain, key_gain, seqs
        )
        attn_part = matmul(attended, w_out).astype(jnp.bfloat16)
        held = {}

        def tie_hidden(got):
            held["hidden_grad"], got = lax.optimization_barrier(
                (outer_cols(cotangent, w_down), got)
            )
            return got

        resid = stream + plan.tp_sum(attn_part, (lambda x: x, tie_hidden)).astype(jnp.float32)
        resid_rows = lax.dynamic_slice_in_dim(resid, offset, share, 0)
        normed_mid = rms_scale(resid, mlp_gain).astype(jnp.bfloat16)
        gate = matmul(normed_mid, w_gate)
        upper = matmul(normed_mid, w_up)
        hidden = swiglu(gate, upper).astype(jnp.bfloat16)
        down_grad_t = inner_rows(cotangent, hidden)
        down = Ring(plan, [down_grad_t])
        down.step()
        mlp_part = matmul(hidden, w_down).astype(jnp.bfloat16)
        mlp_st = plan.tp_begin(mlp_part)

        def down_hook(values):
            if down.done < down.steps:
                down.step()
            down.state, values = lax.optimization_barrier((down.state, values))
            return values

        hidden_grad, mlp_st["got"] = down_hook((held["hidden_grad"], mlp_st["got"]))
        plan.tp_mid(mlp_st)
        _, pull = jax.vjp(swiglu, gate, upper)
        gate_grad, upper_grad = pull(hidden_grad)
        gate_grad = gate_grad.astype(jnp.bfloat16)
        upper_grad = upper_grad.astype(jnp.bfloat16)
        gate_grad, upper_grad = down_hook((gate_grad, upper_grad))
        mid_part = (outer_cols(gate_grad, w_gate) + outer_cols(upper_grad, w_up)).astype(
            jnp.bfloat16
        )
        mid_part, gate_grad, upper_grad, mlp_st["other"] = down_hook(
            (mid_part, gate_grad, upper_grad, mlp_st["other"])
        )
        mixed = (resid + plan.tp_end(mlp_st).astype(jnp.float32)).astype(jnp.bfloat16)
        mid_sum = plan.tp_sum(mid_part)
        gate_w_grad = down_hook(inner_rows(normed_mid, gate_grad))
        up_w_grad = down_hook(inner_rows(normed_mid, upper_grad))
        big = Ring(plan, [gate_w_grad, up_w_grad])
        big.step()
        mid_grad = mid_sum.astype(jnp.float32)
        resid_grad = cotangent.astype(jnp.float32) + norm_back(resid, mlp_gain, mid_grad)
        mlp_gain_part = gain_term(resid_rows, lax.dynamic_slice_in_dim(mid_grad, offset, share, 0))
        resid_low = resid_grad.astype(jnp.bfloat16)
        out_w_grad_t = inner_rows(resid_low, attended)
        attended_grad = outer_cols(resid_low, w_out).astype(jnp.bfloat16)
        small = Ring(plan, [out_w_grad_t])

        def hook(values):
            if big.done < big.steps:
                big.step()
            if small.done < small.steps:
                small.step()
            if down.done < down.steps:
                down.step()
            down.state, big.state, small.state, values = lax.optimization_barrier(
                (down.state, big.state, small.state, values)
            )
            return values

        resid_grad, attended_grad = hook((resid_grad, attended_grad))
        q_grad, k_grad, v_grad, qg_part, kg_part = attend_back(
            attended_grad,
            q_raw,
            k_raw,
            query_gain,
            key_gain,
            queries,
            keys_rot,
            values,
            logsum,
            seqs,
            hook,
        )
        in_part = (
            outer_cols(q_grad, w_query)
            + outer_cols(k_grad, key_matrix)
            + outer_cols(v_grad, value_matrix)
        ).astype(jnp.bfloat16)
        in_part, q_grad, k_grad, v_grad = lax.optimization_barrier(
            (in_part, q_grad, k_grad, v_grad)
        )
        in_sum = plan.tp_sum(in_part)
        query_w_grad = inner_rows(normed_in, q_grad)
        key_w_grad = inner_rows(normed_in, k_grad)
        value_w_grad = inner_rows(normed_in, v_grad)
        while big.done < big.steps:
            big.step()
        while small.done < small.steps:
            small.step()
        while down.done < down.steps:
            down.step()
        in_grad = in_sum.astype(jnp.float32)
        (down_sum,) = down.result()
        gate_sum, up_sum = big.result()
        (out_sum,) = small.result()
        query_sum, key_sum, value_sum = plan.dp_rs([query_w_grad, key_w_grad, value_w_grad])
        input_grad = resid_grad + norm_back(stream, attn_gain, in_grad)
        attn_gain_part = gain_term(stream_rows, lax.dynamic_slice_in_dim(in_grad, offset, share, 0))
        gains = plan.all_sum(jnp.concatenate([attn_gain_part, mlp_gain_part, qg_part, kg_part]))
        width = attn_gain_part.shape[0]
        head = qg_part.shape[0]
        attn_gain_grad = gains[:width]
        mlp_gain_grad = gains[width : 2 * width]
        query_gain_grad = gains[2 * width : 2 * width + head]
        key_gain_grad = gains[2 * width + head :]
        return (
            mixed,
            input_grad,
            attn_gain_grad,
            mlp_gain_grad,
            query_gain_grad,
            key_gain_grad,
            query_sum,
            key_sum,
            value_sum,
            out_sum.T,
            gate_sum,
            up_sum,
            down_sum.T,
        )

    return body


def solution(mesh):
    plan = Plan(mesh)
    placed = (
        P("dp", None),
        P(),
        P(None, "tensor"),
        P(None, "tensor"),
        P(None, "tensor"),
        P(),
        P(),
        P("tensor", None),
        P(),
        P(None, "tensor"),
        P(None, "tensor"),
        P("tensor", None),
        P("dp", None),
    )
    return jax.shard_map(
        make_on_device(plan),
        mesh=mesh,
        in_specs=placed,
        out_specs=(
            P("dp", None),
            P("dp", None),
            P(),
            P(),
            P(),
            P(),
            P("dp", "tensor"),
            P("dp", "tensor"),
            P("dp", "tensor"),
            P("tensor", "dp"),
            P("dp", "tensor"),
            P("dp", "tensor"),
            P("tensor", "dp"),
        ),
        check_vma=False,
    )
```

```python
import itertools
import math

import jax
import jax.numpy as jnp
import numpy as np
from jax import lax
from jax.sharding import PartitionSpec as P

HEAD_SIZE = 128
LEN = 128


EPS = 1e-06
THETA = 1000000.0


def product(form, left, right):
    return jnp.einsum(form, left, right, preferred_element_type=jnp.float32)


def matmul(left, right):
    return jnp.dot(left, right, preferred_element_type=jnp.float32)


def inner_rows(left, right):
    return lax.dot_general(
        left, right, (((0,), (0,)), ((), ())), preferred_element_type=jnp.float32
    )


def outer_cols(left, right):
    return lax.dot_general(
        left, right, (((1,), (1,)), ((), ())), preferred_element_type=jnp.float32
    )


def rms_scale(values, gain):
    return values * lax.rsqrt(jnp.mean(values * values, -1, keepdims=True) + EPS) * gain


def norm_back(values, gain, upstream):
    factor = lax.rsqrt(jnp.mean(values * values, -1, keepdims=True) + EPS)
    scaled = gain * upstream
    return factor * scaled - values * factor**3 * jnp.mean(scaled * values, -1, keepdims=True)


def gain_term(values, upstream):
    factor = lax.rsqrt(jnp.mean(values * values, -1, keepdims=True) + EPS)
    return jnp.sum(upstream * values * factor, 0)


def swiglu(gate, upper):
    return jax.nn.silu(gate) * upper


def rope_tables(length, width):
    position = jnp.arange(length).astype(jnp.float32)
    freqs = jnp.exp(jnp.arange(width // 2).astype(jnp.float32) * (-2.0 * math.log(THETA) / width))
    angles = position[:, None] * freqs[None, :]
    cosine = jnp.cos(angles)
    sine = jnp.sin(angles)
    return (jnp.concatenate([cosine, cosine], -1), jnp.concatenate([sine, sine], -1))


def head_prep(values, gain, cosine, sine):
    normed = values * lax.rsqrt(jnp.mean(values * values, -1, keepdims=True) + EPS) * gain
    half = normed.shape[-1] // 2
    turned = jnp.concatenate([-normed[..., half:], normed[..., :half]], -1)
    return normed * cosine[:, None, :] + turned * sine[:, None, :]


def causal_scores(queries, keys_rot, length):
    scores = product("sqgrd,skgd->sgrqk", queries, keys_rot) * (1.0 / math.sqrt(HEAD_SIZE))
    allowed = jnp.arange(length)[:, None] >= jnp.arange(length)[None, :]
    return jnp.where(allowed, scores, -1e30)


def attend(q_raw, k_raw, v_raw, query_gain, key_gain, seqs):
    total = q_raw.shape[0]
    length = total // seqs
    heads = q_raw.shape[1] // HEAD_SIZE
    kv_heads = k_raw.shape[1] // HEAD_SIZE
    repeat = heads // kv_heads
    cosine, sine = rope_tables(length, HEAD_SIZE)
    queries = head_prep(q_raw.reshape(seqs, length, heads, HEAD_SIZE), query_gain, cosine, sine)
    queries = queries.astype(jnp.bfloat16).reshape(seqs, length, kv_heads, repeat, HEAD_SIZE)
    keys_rot = head_prep(
        k_raw.reshape(seqs, length, kv_heads, HEAD_SIZE), key_gain, cosine, sine
    ).astype(jnp.bfloat16)
    values = v_raw.astype(jnp.bfloat16).reshape(seqs, length, kv_heads, HEAD_SIZE)
    scores = causal_scores(queries, keys_rot, length)
    top = jnp.max(scores, -1, keepdims=True)
    logsum = top + jnp.log(jnp.sum(jnp.exp(scores - top), -1, keepdims=True))
    weights = jnp.exp(scores - logsum).astype(jnp.bfloat16)
    attended = (
        product("sgrqk,skgd->sqgrd", weights, values)
        .astype(jnp.bfloat16)
        .reshape(total, heads * HEAD_SIZE)
    )
    return (attended, logsum, queries, keys_rot, values)


def attend_back(
    upstream, q_raw, k_raw, query_gain, key_gain, queries, keys_rot, values, logsum, seqs, hook
):
    total = q_raw.shape[0]
    length = total // seqs
    heads = q_raw.shape[1] // HEAD_SIZE
    kv_heads = k_raw.shape[1] // HEAD_SIZE
    repeat = heads // kv_heads
    cosine, sine = rope_tables(length, HEAD_SIZE)
    grad_out = upstream.reshape(seqs, length, kv_heads, repeat, HEAD_SIZE)
    scores = causal_scores(queries, keys_rot, length)
    probs = jnp.exp(scores - logsum)
    probs = hook(probs)
    value_grad = product("sgrqk,sqgrd->skgd", probs.astype(jnp.bfloat16), grad_out)
    prob_grad = product("sqgrd,skgd->sgrqk", grad_out, values)
    value_grad, prob_grad = hook((value_grad, prob_grad))
    center = jnp.sum(probs * prob_grad, -1, keepdims=True)
    score_grad = (probs * (prob_grad - center) * (1.0 / math.sqrt(HEAD_SIZE))).astype(jnp.bfloat16)
    score_grad = hook(score_grad)
    query_rot_grad = product("sgrqk,skgd->sqgrd", score_grad, keys_rot).reshape(
        seqs, length, heads, HEAD_SIZE
    )
    key_rot_grad = product("sgrqk,sqgrd->skgd", score_grad, queries)
    query_rot_grad, key_rot_grad = hook((query_rot_grad, key_rot_grad))
    query_in = q_raw.reshape(seqs, length, heads, HEAD_SIZE)
    key_in = k_raw.reshape(seqs, length, kv_heads, HEAD_SIZE)
    _, pull_query = jax.vjp(
        lambda inner, gain: head_prep(inner, gain, cosine, sine), query_in, query_gain
    )
    query_grad, query_gain_grad = pull_query(query_rot_grad)
    _, pull_key = jax.vjp(
        lambda inner, gain: head_prep(inner, gain, cosine, sine), key_in, key_gain
    )
    key_grad, key_gain_grad = pull_key(key_rot_grad)
    query_grad, key_grad = hook((query_grad, key_grad))
    return (
        query_grad.astype(jnp.bfloat16).reshape(total, heads * HEAD_SIZE),
        key_grad.astype(jnp.bfloat16).reshape(total, kv_heads * HEAD_SIZE),
        value_grad.astype(jnp.bfloat16).reshape(total, kv_heads * HEAD_SIZE),
        query_gain_grad,
        key_gain_grad,
    )


def snake_ring(coords):
    coords = [tuple(c) for c in coords]
    dims = [d for d in range(len(coords[0])) if len({c[d] for c in coords}) > 1]
    if not dims:
        return list(range(len(coords)))
    values = [sorted({c[d] for c in coords}) for d in dims]
    where = {tuple(c[d] for d in dims): i for i, c in enumerate(coords)}
    best = None
    for perm in itertools.permutations(range(len(dims))):
        def walk(level):
            if level == len(perm):
                return [()]
            inner = walk(level + 1)
            out = []
            for i, value in enumerate(values[perm[level]]):
                seq = inner if i % 2 == 0 else inner[::-1]
                out += [((perm[level], value),) + t for t in seq]
            return out

        order = []
        for path in walk(0):
            key = dict(path)
            point = tuple(key[k] for k in range(len(dims)))
            if point in where:
                order.append(where[point])
        if len(order) != len(coords):
            continue
        cost = sum(
            sum(abs(a - b) for a, b in zip(coords[order[i]], coords[order[(i + 1) % len(order)]]))
            for i in range(len(order))
        )
        if best is None or cost < best[0]:
            best = (cost, order)
    return best[1] if best else list(range(len(coords)))


class Plan:
    def __init__(self, mesh):
        names = mesh.axis_names
        devices = np.asarray(mesh.devices)
        dp_axis, tp_axis = names.index("dp"), names.index("tensor")
        devices = np.transpose(devices, (dp_axis, tp_axis))
        self.n_dp, self.n_tp = devices.shape
        dp_coords = [tuple(devices[d, 0].coords) for d in range(self.n_dp)]
        self.ring = snake_ring(dp_coords)
        self.pos = [self.ring.index(d) for d in range(self.n_dp)]
        n = self.n_dp
        self.cw = [(self.ring[i], self.ring[(i + 1) % n]) for i in range(n)]
        self.ccw = [(b, a) for a, b in self.cw]
        group = [devices[0, t] for t in range(self.n_tp)]
        self.tp_ok = False
        if self.n_tp == 4:
            chip = [tuple(g.coords) for g in group]
            core = [g.core_on_chip for g in group]
            same = [[u for u in range(4) if u != t and chip[u] == chip[t]] for t in range(4)]
            cross = [
                [u for u in range(4) if chip[u] != chip[t] and core[u] == core[t]] for t in range(4)
            ]
            if all(len(s) == 1 for s in same) and all(len(c) == 1 for c in cross):
                self.core_pairs = [(t, same[t][0]) for t in range(4)]
                self.chip_pairs = [(t, cross[t][0]) for t in range(4)]
                self.half_of = [0 if t < same[t][0] else 1 for t in range(4)]
                self.tp_ok = True

    def tp_begin(self, part):
        if not self.tp_ok:
            total = lax.psum(part.astype(jnp.float32), "tensor").astype(jnp.bfloat16)
            return {"got": total, "other": total}
        rows = part.shape[0]
        h = rows // 2
        t = lax.axis_index("tensor")
        half = jnp.array(self.half_of, jnp.int32)[t]
        keep = lax.dynamic_slice_in_dim(part, half * h, h, 0)
        give = lax.dynamic_slice_in_dim(part, (1 - half) * h, h, 0)
        got = lax.ppermute(give, "tensor", self.core_pairs)
        return {"half": half, "keep": keep, "got": got}

    def tp_mid(self, st):
        if not self.tp_ok:
            return
        st["chip_sum"] = (st["keep"].astype(jnp.float32) + st["got"].astype(jnp.float32)).astype(
            jnp.bfloat16
        )
        st["other"] = lax.ppermute(st["chip_sum"], "tensor", self.chip_pairs)

    def tp_end(self, st):
        if not self.tp_ok:
            return st["other"]
        half = st["half"]
        done = (st["chip_sum"].astype(jnp.float32) + st["other"].astype(jnp.float32)).astype(
            jnp.bfloat16
        )
        partner = lax.ppermute(done, "tensor", self.core_pairs)
        first = jnp.where(half == 0, done, partner)
        second = jnp.where(half == 0, partner, done)
        return jnp.concatenate([first, second], 0)

    def tp_sum(self, part, ties=()):
        ties = list(ties) + [lambda x: x] * (2 - len(ties))
        st = self.tp_begin(part)
        st["got"] = ties[0](st["got"])
        self.tp_mid(st)
        st["other"] = ties[1](st["other"])
        return self.tp_end(st)

    def dp_rs(self, grads):
        ring = Ring(self, grads)
        for _ in range(ring.steps):
            ring.step()
        return ring.result()

    def all_sum(self, x):
        for axis, size in (("tensor", self.n_tp), ("dp", self.n_dp)):
            if size & (size - 1):
                x = lax.psum(x, axis)
                continue
            bit = 1
            while bit < size:
                x = x + lax.ppermute(x, axis, [(i, i ^ bit) for i in range(size)])
                bit *= 2
        return x


class Ring:
    def __init__(self, plan, grads):
        self.plan = plan
        self.n = n = plan.n_dp
        self.me = lax.axis_index("dp")
        self.pos = jnp.array(plan.pos, jnp.int32)[self.me]
        self.order = jnp.array(plan.ring, jnp.int32)
        self.widths = [g.shape[1] for g in grads]
        self.grads = grads
        self.rows = grads[0].shape[0] // n
        self.steps = n - 1
        self.done = 0
        self.state = None

    def piece(self, index, side):
        half = self.rows // 2
        start = index * self.rows + side * half
        parts = [lax.dynamic_slice_in_dim(g, start, half, 0) for g in self.grads]
        return parts[0] if len(parts) == 1 else jnp.concatenate(parts, 1)

    def step(self):
        n, s = self.n, self.done
        own_a = self.piece(self.order[(self.pos - 1 - s) % n], 0)
        own_b = self.piece(self.order[(self.pos + 1 + s) % n], 1)
        if self.state is None:
            send_a, send_b = own_a, own_b
        else:
            send_a, send_b = self.state[0] + own_a, self.state[1] + own_b
        got_a = lax.ppermute(send_a.astype(jnp.bfloat16), "dp", self.plan.cw)
        got_b = lax.ppermute(send_b.astype(jnp.bfloat16), "dp", self.plan.ccw)
        self.state = (got_a.astype(jnp.float32), got_b.astype(jnp.float32))
        self.done += 1

    def result(self):
        acc_a, acc_b = self.state
        total = jnp.concatenate([acc_a + self.piece(self.me, 0), acc_b + self.piece(self.me, 1)], 0)
        out, start = [], 0
        for w in self.widths:
            out.append(total[:, start : start + w])
            start += w
        return out


def make_on_device(plan):
    def body(
        tokens,
        attn_gain,
        w_query,
        key_matrix,
        value_matrix,
        query_gain,
        key_gain,
        w_out,
        mlp_gain,
        w_gate,
        w_up,
        w_down,
        cotangent,
    ):
        count = tokens.shape[0]
        seqs = count // LEN
        share = count // lax.axis_size("tensor")
        offset = lax.axis_index("tensor") * share
        stream = tokens.astype(jnp.float32)
        normed_in = rms_scale(stream, attn_gain).astype(jnp.bfloat16)
        q_raw = matmul(normed_in, w_query)
        k_raw = matmul(normed_in, key_matrix)
        v_raw = matmul(normed_in, value_matrix)
        attended, logsum, queries, keys_rot, values = attend(
            q_raw, k_raw, v_raw, query_gain, key_gain, seqs
        )
        attn_part = matmul(attended, w_out).astype(jnp.bfloat16)
        held = {}

        def tie_hidden(got):
            held["hidden_grad"], got = lax.optimization_barrier(
                (outer_cols(cotangent, w_down), got)
            )
            return got

        resid = stream + plan.tp_sum(attn_part, (lambda x: x, tie_hidden)).astype(jnp.float32)
        resid_rows = lax.dynamic_slice_in_dim(resid, offset, share, 0)
        normed_mid = rms_scale(resid, mlp_gain).astype(jnp.bfloat16)
        gate = matmul(normed_mid, w_gate)
        upper = matmul(normed_mid, w_up)
        hidden = swiglu(gate, upper).astype(jnp.bfloat16)
        down_grad_t = inner_rows(cotangent, hidden)
        down = Ring(plan, [down_grad_t])
        down.step()
        mlp_part = matmul(hidden, w_down).astype(jnp.bfloat16)
        mlp_st = plan.tp_begin(mlp_part)

        def down_hook(values):
            if down.done < down.steps:
                down.step()
            down.state, values = lax.optimization_barrier((down.state, values))
            return values

        hidden_grad, mlp_st["got"] = down_hook((held["hidden_grad"], mlp_st["got"]))
        plan.tp_mid(mlp_st)
        _, pull = jax.vjp(swiglu, gate, upper)
        gate_grad, upper_grad = pull(hidden_grad)
        gate_grad = gate_grad.astype(jnp.bfloat16)
        upper_grad = upper_grad.astype(jnp.bfloat16)
        gate_grad, upper_grad = down_hook((gate_grad, upper_grad))
        mid_part = (outer_cols(gate_grad, w_gate) + outer_cols(upper_grad, w_up)).astype(
            jnp.bfloat16
        )
        mid_part, gate_grad, upper_grad, mlp_st["other"] = down_hook(
            (mid_part, gate_grad, upper_grad, mlp_st["other"])
        )
        mixed = (resid + plan.tp_end(mlp_st).astype(jnp.float32)).astype(jnp.bfloat16)
        mid_sum = plan.tp_sum(mid_part)
        gate_w_grad = down_hook(inner_rows(normed_mid, gate_grad))
        up_w_grad = down_hook(inner_rows(normed_mid, upper_grad))
        big = Ring(plan, [gate_w_grad, up_w_grad])
        big.step()
        mid_grad = mid_sum.astype(jnp.float32)
        resid_grad = cotangent.astype(jnp.float32) + norm_back(resid, mlp_gain, mid_grad)
        mlp_gain_part = gain_term(resid_rows, lax.dynamic_slice_in_dim(mid_grad, offset, share, 0))
        resid_low = resid_grad.astype(jnp.bfloat16)
        out_w_grad_t = inner_rows(resid_low, attended)
        attended_grad = outer_cols(resid_low, w_out).astype(jnp.bfloat16)
        small = Ring(plan, [out_w_grad_t])

        def hook(values):
            if big.done < big.steps:
                big.step()
            if small.done < small.steps:
                small.step()
            if down.done < down.steps:
                down.step()
            down.state, big.state, small.state, values = lax.optimization_barrier(
                (down.state, big.state, small.state, values)
            )
            return values

        resid_grad, attended_grad = hook((resid_grad, attended_grad))
        q_grad, k_grad, v_grad, qg_part, kg_part = attend_back(
            attended_grad,
            q_raw,
            k_raw,
            query_gain,
            key_gain,
            queries,
            keys_rot,
            values,
            logsum,
            seqs,
            hook,
        )
        in_part = (
            outer_cols(q_grad, w_query)
            + outer_cols(k_grad, key_matrix)
            + outer_cols(v_grad, value_matrix)
        ).astype(jnp.bfloat16)
        in_part, q_grad, k_grad, v_grad = lax.optimization_barrier(
            (in_part, q_grad, k_grad, v_grad)
        )
        attn_gain_part = gain_term(stream, in_part.astype(jnp.float32))
        gains = plan.all_sum(
            jnp.concatenate([attn_gain_part, mlp_gain_part, qg_part, kg_part])
        )
        in_sum = plan.tp_sum(in_part)
        query_w_grad = inner_rows(normed_in, q_grad)
        key_w_grad = inner_rows(normed_in, k_grad)
        value_w_grad = inner_rows(normed_in, v_grad)
        while big.done < big.steps:
            big.step()
        while small.done < small.steps:
            small.step()
        while down.done < down.steps:
            down.step()
        in_grad = in_sum.astype(jnp.float32)
        (down_sum,) = down.result()
        gate_sum, up_sum = big.result()
        (out_sum,) = small.result()
        query_sum, key_sum, value_sum = plan.dp_rs([query_w_grad, key_w_grad, value_w_grad])
        input_grad = resid_grad + norm_back(stream, attn_gain, in_grad)
        width = attn_gain_part.shape[0]
        head = qg_part.shape[0]
        attn_gain_grad = gains[:width]
        mlp_gain_grad = gains[width : 2 * width]
        query_gain_grad = gains[2 * width : 2 * width + head]
        key_gain_grad = gains[2 * width + head :]
        return (
            mixed,
            input_grad,
            attn_gain_grad,
            mlp_gain_grad,
            query_gain_grad,
            key_gain_grad,
            query_sum,
            key_sum,
            value_sum,
            out_sum.T,
            gate_sum,
            up_sum,
            down_sum.T,
        )

    return body


def solution(mesh):
    plan = Plan(mesh)
    placed = (
        P("dp", None),
        P(),
        P(None, "tensor"),
        P(None, "tensor"),
        P(None, "tensor"),
        P(),
        P(),
        P("tensor", None),
        P(),
        P(None, "tensor"),
        P(None, "tensor"),
        P("tensor", None),
        P("dp", None),
    )
    return jax.shard_map(
        make_on_device(plan),
        mesh=mesh,
        in_specs=placed,
        out_specs=(
            P("dp", None),
            P("dp", None),
            P(),
            P(),
            P(),
            P(),
            P("dp", "tensor"),
            P("dp", "tensor"),
            P("dp", "tensor"),
            P("tensor", "dp"),
            P("dp", "tensor"),
            P("dp", "tensor"),
            P("tensor", "dp"),
        ),
        check_vma=False,
    )
```
